32 devices in a mesh: groups: 2 (over y), gx: 4 (over z), gz: 2 (over x), vert: 2 (over core).
Axes of the slice: x: 2, y: 2, z: 4, core: 2. Of those that a mesh axis runs over, the one named last changes fastest.
Arguments:
- flow_field: bfloat16 [4, 4, 5, 4, 256, 256], P('groups', 'vert', None, 'gx', None, 'gz'), parts along dimension 0, may hold values from -6 to 6
- test_streams: int32 [4], P('groups'), parts along dimension 0, may hold values from 0 to 999999
- snapshot_ids: int32 [4, 4], P('groups', 'vert'), parts along dimension 0, may hold values from 0 to 65535
Outputs:
- sketch_x: float32 [8, 128], P(('groups', 'gx')), parts along dimension 0
- sketch_y: float32 [512, 128], P(('groups', 'gx', 'gz', 'vert')), parts along dimension 0
- sketch_z: float32 [512, 128], P(('groups', 'gz'), ('gx', 'vert')), parts along dimension 0
- core_sketch: float32 [4608, 2, 48], P(('groups', 'gx')), parts along dimension 0
The draws below stay inside these ranges and needn't reach their ends.
There are 2 independent parts, one for each index of `groups`. The reference program is written for one: setup_inputs(seed, part) draws one part's arguments, and reference() takes and returns one part's arrays. A program takes and returns all parts, laid end to end along the dimension named above; each array names one. Nothing has to cross between parts.
All inputs are finite; a program needn't handle non-finite values.
Results may differ from the reference program's by a relative error of at most 0.007.
Values sent between devices are 32-bit elements; how exact they have to be, the bound alone decides.
No kernel may reach another device: no remote copies, remote signals or barrier semaphores. Data moves between devices by JAX's collectives and lax.ppermute only.
A program may use at most 64 MiB of HBM per device.

```python
import math
import jax
import jax.numpy as jnp
from jax import lax

K = 128
S = 48
E = 2
V = 5
BATCHES = 2
SNAP_MB = 4
SNAP_RANGE = 65536
NY = 256
NX = 4
NZ = 256


def plant(values, stream_key, smallest, top_value):
    spot = [jax.random.randint(jax.random.fold_in(stream_key, axis), (), 0, length) for axis, length in enumerate(values.shape)]
    main_axis = values.shape.index(max(values.shape))
    beside = spot[:main_axis] + [(spot[main_axis] + 1) % values.shape[main_axis]] + spot[main_axis + 1:]
    return values.at[tuple(spot)].set(smallest).at[tuple(beside)].set(top_value)


def steps_of(key, dims, split, smallest, largest):
    factor_of = 1.0
    for dim, shards_of in split:
        draws = jax.random.uniform(jax.random.fold_in(jax.random.fold_in(key, 6), dim), (shards_of,), jnp.float32, smallest / len(split), largest / len(split))
        factor_of = factor_of * jnp.repeat(jnp.exp(draws), dims[dim] // shards_of).reshape((-1,) + (1,) * (len(dims) - 1 - dim))
    return factor_of


def noise(rng, extent, scale, bound, shards=(), kind=jnp.bfloat16):
    loudness = steps_of(rng, extent, shards, -0.22, 0.18) if shards else 1.0
    drawn = jax.random.normal(rng, extent, jnp.float32) * scale * loudness
    return jnp.minimum(jnp.maximum(drawn, -bound), bound).astype(kind)


def setup_inputs(seed: int = 0, part: int = 0) -> dict:
    arg_keys = jax.random.split(jax.random.key(seed), 4)
    part_splits = jax.random.split(jax.random.fold_in(arg_keys[3], part), 4)
    flow_field = noise(part_splits[0], (BATCHES, SNAP_MB, V, NX, NY, NZ), 1.0, 6.0, ((1, 2), (3, 4), (5, 2)))
    test_streams = jax.random.randint(part_splits[1], (2,), 0, 1000000).astype(jnp.int32)
    snapshot_ids = plant(jax.random.randint(part_splits[2], (BATCHES, SNAP_MB), 0, SNAP_RANGE), jax.random.fold_in(part_splits[2], 1), 0, SNAP_RANGE - 1).astype(jnp.int32)
    return {"flow_field": flow_field, "test_streams": test_streams, "snapshot_ids": snapshot_ids}


def hash_index(index, stream, salt):
    mixed = index * -1640531535 + stream * -2048144777 + salt
    mixed = jnp.bitwise_xor(mixed, lax.shift_right_logical(mixed, jnp.int32(16)))
    mixed = mixed * 739982445
    mixed = jnp.bitwise_xor(mixed, lax.shift_right_logical(mixed, jnp.int32(13)))
    mixed = mixed * 695872825
    return jnp.bitwise_xor(mixed, lax.shift_right_logical(mixed, jnp.int32(16)))

def unit_value(index, stream, salt):
    upper = lax.shift_right_logical(hash_index(index, stream, salt), jnp.int32(9))
    return ((2 * upper + 1).astype(jnp.float32) * 2.0 ** (-24) - 1.0).astype(jnp.bfloat16)

def test_table(row_ids, col_ids, stride, stream, salt):
    return unit_value(row_ids[:, None] * stride + col_ids[None, :], stream, salt)

def reference(flow_field, test_streams, snapshot_ids):
    highest = lax.Precision.HIGHEST
    factor_stream = test_streams[0]
    core_stream = test_streams[1]
    total_q = BATCHES * SNAP_MB * V
    rank_ids = jnp.arange(K, dtype=jnp.int32)
    sketch_ids = jnp.arange(S, dtype=jnp.int32)
    x_ids = jnp.arange(NX, dtype=jnp.int32)
    y_ids = jnp.arange(NY, dtype=jnp.int32)
    z_ids = jnp.arange(NZ, dtype=jnp.int32)
    ax_tab = test_table(x_ids, rank_ids, K, factor_stream, 1).astype(jnp.float32)
    ay_tab = test_table(y_ids, rank_ids, K, factor_stream, 2).astype(jnp.float32)
    az_low = test_table(z_ids, rank_ids, K, factor_stream, 3)
    phx_tab = test_table(sketch_ids, x_ids, NX, core_stream, 5).astype(jnp.float32)
    phy_tab = test_table(sketch_ids, y_ids, NY, core_stream, 6).astype(jnp.float32)
    phz_low = test_table(sketch_ids, z_ids, NZ, core_stream, 7)
    q_ids = (snapshot_ids[:, :, None] * V + jnp.arange(V, dtype=jnp.int32)[None, None, :]).reshape(-1)
    aq_tab = test_table(q_ids, rank_ids, K, factor_stream, 4).astype(jnp.float32)
    phq_tab = test_table(q_ids, jnp.arange(E, dtype=jnp.int32), E, core_stream, 8).astype(jnp.float32)
    slices = flow_field.reshape(total_q, NX, NY, NZ)

    def one_slice(carry, inputs):
        acc_x, acc_y, acc_z, acc_core = carry
        slab, aq_row, phq_row = inputs
        rows_z = slab.reshape(NX * NY, NZ)
        along_z = jnp.dot(rows_z, az_low, preferred_element_type=jnp.float32).reshape(NX, NY, K)
        along_y = jnp.einsum('xyz,yk->xzk', slab.astype(jnp.float32), ay_tab, precision=highest)
        weights = aq_row[None, :] * ax_tab
        acc_x = acc_x + lax.optimization_barrier(jnp.sum(along_z * ay_tab[None, :, :], axis=1)) * aq_row[None, :]
        acc_y = acc_y + lax.optimization_barrier(jnp.sum(along_z * weights[:, None, :], axis=0))
        acc_z = acc_z + lax.optimization_barrier(jnp.sum(along_y * weights[:, None, :], axis=0))
        first = jnp.dot(rows_z, phz_low.T, preferred_element_type=jnp.float32).reshape(NX, NY, S)
        second = jnp.einsum('xyc,by->bcx', first, phy_tab, precision=highest)
        acc_core = acc_core + second[:, :, None, :] * phq_row[None, None, :, None]
        return ((acc_x, acc_y, acc_z, acc_core), None)
    start_state = (jnp.zeros((NX, K), jnp.float32), jnp.zeros((NY, K), jnp.float32), jnp.zeros((NZ, K), jnp.float32), jnp.zeros((S, S, E, NX), jnp.float32))
    final_state, unused = lax.scan(one_slice, start_state, (slices, aq_tab, phq_tab))
    sum_x, sum_y, sum_z, partial_core = final_state
    core = jnp.einsum('bcex,ax->bcea', partial_core, phx_tab, precision=highest).reshape(S * S, E, S)
    scale_x = 3.0 ** 1.5 / math.sqrt(NY * NZ * total_q)
    scale_y = 3.0 ** 1.5 / math.sqrt(NX * NZ * total_q)
    scale_z = 3.0 ** 1.5 / math.sqrt(NX * NY * total_q)
    scale_core = 9.0 / math.sqrt(NX * NY * NZ * total_q)
    return (sum_x * scale_x, sum_y * scale_y, sum_z * scale_z, core * scale_core)
```

```python
import math

import jax
import jax.numpy as jnp
from jax import lax
from jax.sharding import PartitionSpec as P

K = 128
S = 48
E = 2


def hash_index(index, stream, salt):
    mixed = index * -1640531535 + stream * -2048144777 + salt
    mixed = jnp.bitwise_xor(mixed, lax.shift_right_logical(mixed, jnp.int32(16)))
    mixed = mixed * 739982445
    mixed = jnp.bitwise_xor(mixed, lax.shift_right_logical(mixed, jnp.int32(13)))
    mixed = mixed * 695872825
    return jnp.bitwise_xor(mixed, lax.shift_right_logical(mixed, jnp.int32(16)))


def unit_value(index, stream, salt):
    upper = lax.shift_right_logical(hash_index(index, stream, salt), jnp.int32(9))
    return ((2 * upper + 1).astype(jnp.float32) * 2.0 ** (-24) - 1.0).astype(jnp.bfloat16)


def test_table(row_ids, col_ids, stride, stream, salt):
    return unit_value(row_ids[:, None] * stride + col_ids[None, :], stream, salt)


def bit_of(axis, d):
    return (lax.axis_index(axis) // d) % 2


def halve(arr, dim, bit):
    shape = arr.shape
    split = arr.reshape(shape[:dim] + (shape[dim] // 2, 2) + shape[dim + 1 :])
    keep = lax.dynamic_index_in_dim(split, bit, dim + 1, keepdims=False)
    send = lax.dynamic_index_in_dim(split, 1 - bit, dim + 1, keepdims=False)
    return keep, send


def exchange(axis, d, pieces):
    n = lax.axis_size(axis)
    flat = jnp.concatenate([p.reshape(-1) for p in pieces])
    got = lax.ppermute(flat, axis, [(i, i ^ d) for i in range(n)])
    out, at = [], 0
    for p in pieces:
        out.append(got[at : at + p.size].reshape(p.shape))
        at += p.size
    return out


def bits(n):
    d, out = 1, []
    while d < n:
        out.append(d)
        d *= 2
    return out


def shards(flow_field, test_streams, snapshot_ids):
    highest = lax.Precision.HIGHEST
    f32 = jnp.float32
    batches, local_snaps, variables, cells_x, cells_y, cells_z = flow_field.shape
    n_gx = lax.axis_size("gx")
    n_gz = lax.axis_size("gz")
    n_vert = lax.axis_size("vert")
    total_x = cells_x * n_gx
    total_z = cells_z * n_gz
    total_q = variables * batches * local_snaps * n_vert
    factor_stream = test_streams[0]
    core_stream = test_streams[1]
    gx_me = lax.axis_index("gx")
    rank_ids = jnp.arange(K, dtype=jnp.int32)
    sketch_ids = jnp.arange(S, dtype=jnp.int32)
    x_ids = gx_me * cells_x + jnp.arange(cells_x, dtype=jnp.int32)
    y_ids = jnp.arange(cells_y, dtype=jnp.int32)
    z_ids = lax.axis_index("gz") * cells_z + jnp.arange(cells_z, dtype=jnp.int32)
    q_ids = (
        snapshot_ids[:, :, None] * variables + jnp.arange(variables, dtype=jnp.int32)[None, None, :]
    ).reshape(-1)
    ax = test_table(x_ids, rank_ids, K, factor_stream, 1).astype(f32)
    ay = test_table(y_ids, rank_ids, K, factor_stream, 2)
    az = test_table(z_ids, rank_ids, K, factor_stream, 3)
    aq = test_table(q_ids, rank_ids, K, factor_stream, 4).astype(f32)
    phy = test_table(sketch_ids, y_ids, cells_y, core_stream, 6).astype(f32)
    phz = test_table(sketch_ids, z_ids, total_z, core_stream, 7)
    phq = test_table(q_ids, jnp.arange(E, dtype=jnp.int32), E, core_stream, 8).astype(f32)

    n_q = batches * local_snaps * variables
    field = flow_field.reshape(n_q, cells_x, cells_y, cells_z)
    rows_z = field.reshape(-1, cells_z)

    along_z = jnp.dot(rows_z, az, preferred_element_type=f32).reshape(n_q, cells_x, cells_y, K)
    by_q = jnp.sum(along_z * aq[:, None, None, :], axis=0)
    part_y = jnp.sum(by_q * ax[:, None, :], axis=0)
    part_x = jnp.sum(by_q * ay.astype(f32)[None, :, :], axis=1)
    along_y = jnp.einsum("qxyz,yk->qxzk", field, ay, preferred_element_type=f32)
    weights = aq[:, None, :] * ax[None, :, :]
    part_z = jnp.sum(along_y * weights[:, :, None, :], axis=(0, 1))
    first = jnp.dot(rows_z, phz.T, preferred_element_type=f32).reshape(n_q, cells_x, cells_y, S)
    by_e = jnp.einsum("qxyn,qe->xeyn", first, phq, precision=highest)
    part_core = jnp.einsum("my,xeyn->mnex", phy, by_e, precision=highest).reshape(S * S, E, cells_x)

    rows_each = cells_y // (n_gx * n_gz * n_vert)
    cols_each = K // (n_gx * n_vert)
    core_rows = S * S // n_gx
    sy = part_y.reshape(n_gx, n_gz, n_vert, rows_each, K)
    sz = part_z.reshape(cells_z, n_gx, n_vert, cols_each)
    sx = part_x
    core = part_core.reshape(1, n_gx, core_rows, E, cells_x)

    for d in bits(n_vert):
        b = bit_of("vert", d)
        sy_keep, sy_send = halve(sy, 2, b)
        sz_keep, sz_send = halve(sz, 2, b)
        g_sy, g_sz, g_sx, g_core = exchange("vert", d, [sy_send, sz_send, sx, core])
        sy, sz, sx, core = sy_keep + g_sy, sz_keep + g_sz, sx + g_sx, core + g_core
    for d in bits(n_gz):
        b = bit_of("gz", d)
        sy_keep, sy_send = halve(sy, 1, b)
        g_sy, g_sx, g_core = exchange("gz", d, [sy_send, sx, core])
        sy, sx, core = sy_keep + g_sy, sx + g_sx, core + g_core
    for d in bits(n_gx):
        b = bit_of("gx", d)
        sy_keep, sy_send = halve(sy, 0, b)
        sz_keep, sz_send = halve(sz, 1, b)
        core_keep, core_send = halve(core, 1, b)
        g_sy, g_sz, g_core = exchange("gx", d, [sy_send, sz_send, core_send])
        sy, sz = sy_keep + g_sy, sz_keep + g_sz
        core = jnp.concatenate([core_keep, g_core], axis=0)

    src = jnp.bitwise_xor(gx_me, jnp.arange(n_gx, dtype=jnp.int32))
    x_src = (src[:, None] * cells_x + jnp.arange(cells_x, dtype=jnp.int32)[None, :]).reshape(-1)
    phx = test_table(sketch_ids, x_src, total_x, core_stream, 5).astype(f32)
    held = core.reshape(n_gx, core_rows, E, cells_x).transpose(1, 2, 0, 3).reshape(core_rows, E, n_gx * cells_x)
    core_out = jnp.einsum("rej,aj->rea", held, phx, precision=highest)

    scale_x = 3.0**1.5 / math.sqrt(cells_y * total_z * total_q)
    scale_y = 3.0**1.5 / math.sqrt(total_x * total_z * total_q)
    scale_z = 3.0**1.5 / math.sqrt(total_x * cells_y * total_q)
    scale_core = 9.0 / math.sqrt(total_x * cells_y * total_z * total_q)
    return (
        sx * scale_x,
        sy.reshape(rows_each, K) * scale_y,
        sz.reshape(cells_z, cols_each) * scale_z,
        core_out * scale_core,
    )


def solution(mesh):
    in_specs = (P("groups", "vert", None, "gx", None, "gz"), P("groups"), P("groups", "vert"))
    out_specs = (
        P(("groups", "gx"), None),
        P(("groups", "gx", "gz", "vert"), None),
        P(("groups", "gz"), ("gx", "vert")),
        P(("groups", "gx"), None, None),
    )
    return jax.shard_map(shards, mesh=mesh, in_specs=in_specs, out_specs=out_specs, check_vma=False)
```

```python
import math

import jax
import jax.numpy as jnp
from jax import lax
from jax.sharding import PartitionSpec as P

K = 128
S = 48
E = 2


def hash_index(index, stream, salt):
    mixed = index * -1640531535 + stream * -2048144777 + salt
    mixed = jnp.bitwise_xor(mixed, lax.shift_right_logical(mixed, jnp.int32(16)))
    mixed = mixed * 739982445
    mixed = jnp.bitwise_xor(mixed, lax.shift_right_logical(mixed, jnp.int32(13)))
    mixed = mixed * 695872825
    return jnp.bitwise_xor(mixed, lax.shift_right_logical(mixed, jnp.int32(16)))


def unit_value(index, stream, salt):
    upper = lax.shift_right_logical(hash_index(index, stream, salt), jnp.int32(9))
    return ((2 * upper + 1).astype(jnp.float32) * 2.0 ** (-24) - 1.0).astype(jnp.bfloat16)


def test_table(row_ids, col_ids, stride, stream, salt):
    return unit_value(row_ids[:, None] * stride + col_ids[None, :], stream, salt)


def digit_steps(n):
    d, out = 1, []
    while d < n:
        r = 4 if n // d >= 4 else 2
        out.append((d, r))
        d *= r
    return out


def split_digit(arr, dim, r, digit):
    shape = arr.shape
    split = arr.reshape(shape[:dim] + (shape[dim] // r, r) + shape[dim + 1 :])

    def at(s):
        return lax.dynamic_index_in_dim(split, jnp.bitwise_xor(digit, s), dim + 1, keepdims=False)

    return at


def send_to(axes, n, shift, pieces):
    dense = all(p.size % 128 == 0 for p in pieces)
    if dense:
        flat = jnp.concatenate([p.reshape(-1, 128) for p in pieces], axis=0)
    else:
        flat = jnp.concatenate([p.reshape(-1) for p in pieces])
    got = lax.ppermute(flat, axes, [(i, i ^ shift) for i in range(n)])
    out, at = [], 0
    for p in pieces:
        rows = p.size // 128 if dense else p.size
        out.append(got[at : at + rows].reshape(p.shape))
        at += rows
    return out


def linear_index(axes):
    idx = 0
    for a in axes:
        idx = idx * lax.axis_size(a) + lax.axis_index(a)
    return idx


def shards(flow_field, test_streams, snapshot_ids):
    highest = lax.Precision.HIGHEST
    f32 = jnp.float32
    bf16 = jnp.bfloat16
    batches, local_snaps, variables, cells_x, cells_y, cells_z = flow_field.shape
    n_gx = lax.axis_size("gx")
    n_gz = lax.axis_size("gz")
    n_vert = lax.axis_size("vert")
    total_x = cells_x * n_gx
    total_z = cells_z * n_gz
    total_q = variables * batches * local_snaps * n_vert
    factor_stream = test_streams[0]
    core_stream = test_streams[1]
    gx_me = lax.axis_index("gx")
    rank_ids = jnp.arange(K, dtype=jnp.int32)
    sketch_ids = jnp.arange(S, dtype=jnp.int32)
    x_ids = gx_me * cells_x + jnp.arange(cells_x, dtype=jnp.int32)
    y_ids = jnp.arange(cells_y, dtype=jnp.int32)
    z_ids = lax.axis_index("gz") * cells_z + jnp.arange(cells_z, dtype=jnp.int32)
    q_ids = (
        snapshot_ids[:, :, None] * variables + jnp.arange(variables, dtype=jnp.int32)[None, None, :]
    ).reshape(-1)
    ax = test_table(x_ids, rank_ids, K, factor_stream, 1).astype(f32)
    ay = test_table(y_ids, rank_ids, K, factor_stream, 2)
    az = test_table(z_ids, rank_ids, K, factor_stream, 3)
    aq = test_table(q_ids, rank_ids, K, factor_stream, 4).astype(f32)
    phy = test_table(sketch_ids, y_ids, cells_y, core_stream, 6).astype(f32)
    phz = test_table(sketch_ids, z_ids, total_z, core_stream, 7)
    phq = test_table(q_ids, jnp.arange(E, dtype=jnp.int32), E, core_stream, 8).astype(f32)

    n_q = batches * local_snaps * variables
    field = flow_field.reshape(n_q, cells_x, cells_y, cells_z)
    rows_z = field.reshape(-1, cells_z)

    qz = aq[:, None, :] * az.astype(f32)[None, :, :]
    qz_hi = qz.astype(bf16)
    qz_lo = (qz - qz_hi.astype(f32)).astype(bf16)
    both = jnp.einsum(
        "qxyz,qzk->xyk", field, jnp.concatenate([qz_hi, qz_lo], axis=-1), preferred_element_type=f32
    )
    by_q = both[..., :K] + both[..., K:]
    part_y = jnp.sum(by_q * ax[:, None, :], axis=0)
    part_x = jnp.sum(by_q * ay.astype(f32)[None, :, :], axis=1)
    along_y = jnp.einsum("qxyz,yk->qxzk", field, ay, preferred_element_type=f32)
    weights = aq[:, None, :] * ax[None, :, :]
    part_z = jnp.sum(along_y * weights[:, :, None, :], axis=(0, 1))
    first = jnp.dot(rows_z, phz.T, preferred_element_type=f32).reshape(n_q, cells_x, cells_y, S)
    by_e = jnp.einsum("qxyn,qe->xeyn", first, phq, precision=highest)
    part_core = jnp.einsum("my,xeyn->xemn", phy, by_e, precision=highest)

    rows_each = cells_y // (n_gx * n_gz * n_vert)
    cols_each = K // (n_gx * n_vert)
    core_rows = S * S // n_gx
    n_gzv = n_gz * n_vert
    sy = part_y.reshape(n_gx, n_gzv, rows_each, K)
    sz = part_z.T.reshape(n_gx, n_vert, cols_each, cells_z)
    sx = part_x
    core = (
        part_core.reshape(cells_x, E, n_gx, core_rows)
        .transpose(2, 0, 1, 3)
        .reshape(1, n_gx, cells_x * E * core_rows)
    )

    v_me = lax.axis_index("vert")
    for d, r in digit_steps(n_vert):
        digit = (v_me // d) % r
        at = split_digit(sz, 1, r, digit)
        total = at(0)
        for s in range(1, r):
            (got,) = send_to("vert", n_vert, s * d, [at(s)])
            total = total + got
        sz = total
    gzv_me = linear_index(("gz", "vert"))
    for d, r in digit_steps(n_gzv):
        digit = (gzv_me // d) % r
        at = split_digit(sy, 1, r, digit)
        sy_total, sx_total, core_total = at(0), sx, core
        for s in range(1, r):
            g_sy, g_sx, g_core = send_to(("gz", "vert"), n_gzv, s * d, [at(s), sx, core])
            sy_total, sx_total, core_total = sy_total + g_sy, sx_total + g_sx, core_total + g_core
        sy, sx, core = sy_total, sx_total, core_total
    for d, r in digit_steps(n_gx):
        digit = (gx_me // d) % r
        at_y = split_digit(sy, 0, r, digit)
        at_z = split_digit(sz, 0, r, digit)
        at_c = split_digit(core, 1, r, digit)
        sy_total, sz_total, core_parts = at_y(0), at_z(0), [at_c(0)]
        for s in range(1, r):
            g_sy, g_sz, g_core = send_to("gx", n_gx, s * d, [at_y(s), at_z(s), at_c(s)])
            sy_total, sz_total = sy_total + g_sy, sz_total + g_sz
            core_parts.append(g_core)
        sy, sz = sy_total, sz_total
        core = jnp.concatenate(core_parts, axis=0)

    src = jnp.bitwise_xor(gx_me, jnp.arange(n_gx, dtype=jnp.int32))
    x_src = (src[:, None] * cells_x + jnp.arange(cells_x, dtype=jnp.int32)[None, :]).reshape(-1)
    phx = test_table(sketch_ids, x_src, total_x, core_stream, 5).astype(f32).reshape(S, n_gx, cells_x)
    held = core.reshape(n_gx, cells_x, E, core_rows)
    core_out = jnp.einsum("jxer,ajx->rea", held, phx, precision=highest)

    scale_x = 3.0**1.5 / math.sqrt(cells_y * total_z * total_q)
    scale_y = 3.0**1.5 / math.sqrt(total_x * total_z * total_q)
    scale_z = 3.0**1.5 / math.sqrt(total_x * cells_y * total_q)
    scale_core = 9.0 / math.sqrt(total_x * cells_y * total_z * total_q)
    return (
        sx * scale_x,
        sy.reshape(rows_each, K) * scale_y,
        sz.reshape(cols_each, cells_z).T * scale_z,
        core_out * scale_core,
    )


def solution(mesh):
    in_specs = (P("groups", "vert", None, "gx", None, "gz"), P("groups"), P("groups", "vert"))
    out_specs = (
        P(("groups", "gx"), None),
        P(("groups", "gx", "gz", "vert"), None),
        P(("groups", "gz"), ("gx", "vert")),
        P(("groups", "gx"), None, None),
    )
    return jax.shard_map(shards, mesh=mesh, in_specs=in_specs, out_specs=out_specs, check_vma=False)
```

```python
import math

import jax
import jax.numpy as jnp
from jax import lax
from jax.sharding import PartitionSpec as P

K = 128
S = 48
E = 2


def hash_index(index, stream, salt):
    mixed = index * -1640531535 + stream * -2048144777 + salt
    mixed = jnp.bitwise_xor(mixed, lax.shift_right_logical(mixed, jnp.int32(16)))
    mixed = mixed * 739982445
    mixed = jnp.bitwise_xor(mixed, lax.shift_right_logical(mixed, jnp.int32(13)))
    mixed = mixed * 695872825
    return jnp.bitwise_xor(mixed, lax.shift_right_logical(mixed, jnp.int32(16)))


def unit_value(index, stream, salt):
    upper = lax.shift_right_logical(hash_index(index, stream, salt), jnp.int32(9))
    return ((2 * upper + 1).astype(jnp.float32) * 2.0 ** (-24) - 1.0).astype(jnp.bfloat16)


def test_table(row_ids, col_ids, stride, stream, salt):
    return unit_value(row_ids[:, None] * stride + col_ids[None, :], stream, salt)


def digit_steps(n):
    d, out = 1, []
    while d < n:
        r = 4 if n // d >= 4 else 2
        out.append((d, r))
        d *= r
    return out


def split_digit(arr, dim, r, digit):
    shape = arr.shape
    split = arr.reshape(shape[:dim] + (shape[dim] // r, r) + shape[dim + 1 :])

    def at(s):
        return lax.dynamic_index_in_dim(split, jnp.bitwise_xor(digit, s), dim + 1, keepdims=False)

    return at


def send_to(axes, n, shift, pieces):
    dense = all(p.size % 128 == 0 for p in pieces)
    if dense:
        flat = jnp.concatenate([p.reshape(-1, 128) for p in pieces], axis=0)
    else:
        flat = jnp.concatenate([p.reshape(-1) for p in pieces])
    got = lax.ppermute(flat, axes, [(i, i ^ shift) for i in range(n)])
    out, at = [], 0
    for p in pieces:
        rows = p.size // 128 if dense else p.size
        out.append(got[at : at + rows].reshape(p.shape))
        at += rows
    return out


def linear_index(axes):
    idx = 0
    for a in axes:
        idx = idx * lax.axis_size(a) + lax.axis_index(a)
    return idx


def shards(flow_field, test_streams, snapshot_ids):
    highest = lax.Precision.HIGHEST
    f32 = jnp.float32
    bf16 = jnp.bfloat16
    batches, local_snaps, variables, cells_x, cells_y, cells_z = flow_field.shape
    n_gx = lax.axis_size("gx")
    n_gz = lax.axis_size("gz")
    n_vert = lax.axis_size("vert")
    total_x = cells_x * n_gx
    total_z = cells_z * n_gz
    total_q = variables * batches * local_snaps * n_vert
    factor_stream = test_streams[0]
    core_stream = test_streams[1]
    gx_me = lax.axis_index("gx")
    rank_ids = jnp.arange(K, dtype=jnp.int32)
    sketch_ids = jnp.arange(S, dtype=jnp.int32)
    x_ids = gx_me * cells_x + jnp.arange(cells_x, dtype=jnp.int32)
    y_ids = jnp.arange(cells_y, dtype=jnp.int32)
    z_ids = lax.axis_index("gz") * cells_z + jnp.arange(cells_z, dtype=jnp.int32)
    q_ids = (
        snapshot_ids[:, :, None] * variables + jnp.arange(variables, dtype=jnp.int32)[None, None, :]
    ).reshape(-1)
    ax = test_table(x_ids, rank_ids, K, factor_stream, 1).astype(f32)
    ay = test_table(y_ids, rank_ids, K, factor_stream, 2)
    az = test_table(z_ids, rank_ids, K, factor_stream, 3)
    aq = test_table(q_ids, rank_ids, K, factor_stream, 4).astype(f32)
    phy = test_table(sketch_ids, y_ids, cells_y, core_stream, 6).astype(f32)
    phz = test_table(sketch_ids, z_ids, total_z, core_stream, 7)
    phq = test_table(q_ids, jnp.arange(E, dtype=jnp.int32), E, core_stream, 8).astype(f32)

    n_q = batches * local_snaps * variables
    field = flow_field.reshape(n_q, cells_x, cells_y, cells_z)
    rows_z = field.reshape(-1, cells_z)

    qz = aq[:, None, :] * az.astype(f32)[None, :, :]
    qz_hi = qz.astype(bf16)
    qz_lo = (qz - qz_hi.astype(f32)).astype(bf16)
    both = jnp.einsum(
        "qxyz,qzk->xyk", field, jnp.concatenate([qz_hi, qz_lo], axis=-1), preferred_element_type=f32
    )
    by_q = both[..., :K] + both[..., K:]
    part_y = jnp.sum(by_q * ax[:, None, :], axis=0)
    part_x = jnp.sum(by_q * ay.astype(f32)[None, :, :], axis=1)
    along_y = jnp.einsum("qxyz,yk->qxzk", field, ay, preferred_element_type=f32)
    weights = aq[:, None, :] * ax[None, :, :]
    part_z = jnp.sum(along_y * weights[:, :, None, :], axis=(0, 1))
    first = jnp.dot(rows_z, phz.T, preferred_element_type=f32).reshape(n_q, cells_x, cells_y, S)
    by_e = jnp.einsum("qxyn,qe->xeyn", first, phq, precision=highest)
    part_core = jnp.einsum("my,xeyn->xemn", phy, by_e, precision=highest)

    rows_each = cells_y // (n_gx * n_gz * n_vert)
    cols_each = K // (n_gx * n_vert)
    core_rows = S * S // n_gx
    n_gzv = n_gz * n_vert
    sy = part_y.reshape(n_gx, n_gzv, rows_each, K)
    sz = part_z.T.reshape(n_gx, n_vert, cols_each, cells_z)
    sx = part_x
    core = (
        part_core.reshape(cells_x, E, n_gx, core_rows)
        .transpose(2, 0, 1, 3)
        .reshape(1, n_gx, cells_x * E * core_rows)
    )

    n_run = n_gx * n_gzv
    if n_run <= 16:
        me = linear_index(("gx", "gz", "vert"))
        v_me = lax.axis_index("vert")
        gz_me = lax.axis_index("gz")
        sy_blocks = sy.reshape(n_run, rows_each, K)
        sz_blocks = sz.reshape(n_gx * n_vert, cols_each, cells_z)
        core_blocks = core.reshape(n_gx, -1)
        own = lambda arr, i: lax.dynamic_index_in_dim(arr, i, 0, keepdims=False)
        sy_total = own(sy_blocks, me)
        sz_total = own(sz_blocks, gx_me * n_vert + v_me)
        sx_total = sx
        held = [own(core_blocks, gx_me)] + [None] * (n_gx - 1)
        for s in range(1, n_run):
            s_gx, s_gz, s_v = s // n_gzv, (s // n_vert) % n_gz, s % n_vert
            to_gx = jnp.bitwise_xor(gx_me, s_gx)
            pieces = [own(sy_blocks, jnp.bitwise_xor(me, s)), own(core_blocks, to_gx)]
            if s_gz == 0:
                pieces.append(own(sz_blocks, to_gx * n_vert + jnp.bitwise_xor(v_me, s_v)))
            if s_gx == 0:
                pieces.append(sx)
            got = send_to(("gx", "gz", "vert"), n_run, s, pieces)
            sy_total = sy_total + got[0]
            held[s_gx] = got[1] if held[s_gx] is None else held[s_gx] + got[1]
            if s_gz == 0:
                sz_total = sz_total + got[2]
            if s_gx == 0:
                sx_total = sx_total + got[-1]
        sy, sz, sx = sy_total, sz_total, sx_total
        core = jnp.stack(held)
    else:
        v_me = lax.axis_index("vert")
        for d, r in digit_steps(n_vert):
            digit = (v_me // d) % r
            at = split_digit(sz, 1, r, digit)
            total = at(0)
            for s in range(1, r):
                (got,) = send_to("vert", n_vert, s * d, [at(s)])
                total = total + got
            sz = total
        gzv_me = linear_index(("gz", "vert"))
        for d, r in digit_steps(n_gzv):
            digit = (gzv_me // d) % r
            at = split_digit(sy, 1, r, digit)
            sy_total, sx_total, core_total = at(0), sx, core
            for s in range(1, r):
                g_sy, g_sx, g_core = send_to(("gz", "vert"), n_gzv, s * d, [at(s), sx, core])
                sy_total, sx_total, core_total = sy_total + g_sy, sx_total + g_sx, core_total + g_core
            sy, sx, core = sy_total, sx_total, core_total
        for d, r in digit_steps(n_gx):
            digit = (gx_me // d) % r
            at_y = split_digit(sy, 0, r, digit)
            at_z = split_digit(sz, 0, r, digit)
            at_c = split_digit(core, 1, r, digit)
            sy_total, sz_total, core_parts = at_y(0), at_z(0), [at_c(0)]
            for s in range(1, r):
                g_sy, g_sz, g_core = send_to("gx", n_gx, s * d, [at_y(s), at_z(s), at_c(s)])
                sy_total, sz_total = sy_total + g_sy, sz_total + g_sz
                core_parts.append(g_core)
            sy, sz = sy_total, sz_total
            core = jnp.concatenate(core_parts, axis=0)

    src = jnp.bitwise_xor(gx_me, jnp.arange(n_gx, dtype=jnp.int32))
    x_src = (src[:, None] * cells_x + jnp.arange(cells_x, dtype=jnp.int32)[None, :]).reshape(-1)
    phx = test_table(sketch_ids, x_src, total_x, core_stream, 5).astype(f32).reshape(S, n_gx, cells_x)
    held = core.reshape(n_gx, cells_x, E, core_rows)
    core_out = jnp.einsum("jxer,ajx->rea", held, phx, precision=highest)

    scale_x = 3.0**1.5 / math.sqrt(cells_y * total_z * total_q)
    scale_y = 3.0**1.5 / math.sqrt(total_x * total_z * total_q)
    scale_z = 3.0**1.5 / math.sqrt(total_x * cells_y * total_q)
    scale_core = 9.0 / math.sqrt(total_x * cells_y * total_z * total_q)
    return (
        sx * scale_x,
        sy.reshape(rows_each, K) * scale_y,
        sz.reshape(cols_each, cells_z).T * scale_z,
        core_out * scale_core,
    )


def solution(mesh):
    in_specs = (P("groups", "vert", None, "gx", None, "gz"), P("groups"), P("groups", "vert"))
    out_specs = (
        P(("groups", "gx"), None),
        P(("groups", "gx", "gz", "vert"), None),
        P(("groups", "gz"), ("gx", "vert")),
        P(("groups", "gx"), None, None),
    )
    return jax.shard_map(shards, mesh=mesh, in_specs=in_specs, out_specs=out_specs, check_vma=False)
```

```python
import math

import jax
import jax.numpy as jnp
from jax import lax
from jax.sharding import PartitionSpec as P

K = 128
S = 48
E = 2


def hash_index(index, stream, salt):
    mixed = index * -1640531535 + stream * -2048144777 + salt
    mixed = jnp.bitwise_xor(mixed, lax.shift_right_logical(mixed, jnp.int32(16)))
    mixed = mixed * 739982445
    mixed = jnp.bitwise_xor(mixed, lax.shift_right_logical(mixed, jnp.int32(13)))
    mixed = mixed * 695872825
    return jnp.bitwise_xor(mixed, lax.shift_right_logical(mixed, jnp.int32(16)))


def unit_value(index, stream, salt):
    upper = lax.shift_right_logical(hash_index(index, stream, salt), jnp.int32(9))
    return ((2 * upper + 1).astype(jnp.float32) * 2.0 ** (-24) - 1.0).astype(jnp.bfloat16)


def test_table(row_ids, col_ids, stride, stream, salt):
    return unit_value(row_ids[:, None] * stride + col_ids[None, :], stream, salt)


def digit_steps(n):
    d, out = 1, []
    while d < n:
        r = 4 if n // d >= 4 else 2
        out.append((d, r))
        d *= r
    return out


def split_digit(arr, dim, r, digit):
    shape = arr.shape
    split = arr.reshape(shape[:dim] + (shape[dim] // r, r) + shape[dim + 1 :])

    def at(s):
        return lax.dynamic_index_in_dim(split, jnp.bitwise_xor(digit, s), dim + 1, keepdims=False)

    return at


def send_to(axes, n, shift, pieces):
    dense = all(p.size % 128 == 0 for p in pieces)
    if dense:
        flat = jnp.concatenate([p.reshape(-1, 128) for p in pieces], axis=0)
    else:
        flat = jnp.concatenate([p.reshape(-1) for p in pieces])
    got = lax.ppermute(flat, axes, [(i, i ^ shift) for i in range(n)])
    out, at = [], 0
    for p in pieces:
        rows = p.size // 128 if dense else p.size
        out.append(got[at : at + rows].reshape(p.shape))
        at += rows
    return out


def linear_index(axes):
    idx = 0
    for a in axes:
        idx = idx * lax.axis_size(a) + lax.axis_index(a)
    return idx


def shards(flow_field, test_streams, snapshot_ids):
    highest = lax.Precision.HIGHEST
    f32 = jnp.float32
    bf16 = jnp.bfloat16
    batches, local_snaps, variables, cells_x, cells_y, cells_z = flow_field.shape
    n_gx = lax.axis_size("gx")
    n_gz = lax.axis_size("gz")
    n_vert = lax.axis_size("vert")
    total_x = cells_x * n_gx
    total_z = cells_z * n_gz
    total_q = variables * batches * local_snaps * n_vert
    factor_stream = test_streams[0]
    core_stream = test_streams[1]
    gx_me = lax.axis_index("gx")
    rank_ids = jnp.arange(K, dtype=jnp.int32)
    sketch_ids = jnp.arange(S, dtype=jnp.int32)
    x_ids = gx_me * cells_x + jnp.arange(cells_x, dtype=jnp.int32)
    y_ids = jnp.arange(cells_y, dtype=jnp.int32)
    z_ids = lax.axis_index("gz") * cells_z + jnp.arange(cells_z, dtype=jnp.int32)
    q_ids = (
        snapshot_ids[:, :, None] * variables + jnp.arange(variables, dtype=jnp.int32)[None, None, :]
    ).reshape(-1)
    ax = test_table(x_ids, rank_ids, K, factor_stream, 1).astype(f32)
    ay = test_table(y_ids, rank_ids, K, factor_stream, 2)
    az = test_table(z_ids, rank_ids, K, factor_stream, 3)
    aq = test_table(q_ids, rank_ids, K, factor_stream, 4).astype(f32)
    phy = test_table(sketch_ids, y_ids, cells_y, core_stream, 6).astype(f32)
    phz = test_table(sketch_ids, z_ids, total_z, core_stream, 7)
    phq = test_table(q_ids, jnp.arange(E, dtype=jnp.int32), E, core_stream, 8).astype(f32)

    n_q = batches * local_snaps * variables
    field = flow_field.reshape(n_q, cells_x, cells_y, cells_z)
    rows_z = field.reshape(-1, cells_z)

    qz = aq[:, None, :] * az.astype(f32)[None, :, :]
    qz_hi = qz.astype(bf16)
    qz_lo = (qz - qz_hi.astype(f32)).astype(bf16)
    both = jnp.einsum(
        "qxyz,qzk->xyk", field, jnp.concatenate([qz_hi, qz_lo], axis=-1), preferred_element_type=f32
    )
    by_q = both[..., :K] + both[..., K:]
    part_y = jnp.sum(by_q * ax[:, None, :], axis=0)
    part_x = jnp.sum(by_q * ay.astype(f32)[None, :, :], axis=1)
    along_y = jnp.einsum("qxyz,yk->qxzk", field, ay, preferred_element_type=f32)
    weights = aq[:, None, :] * ax[None, :, :]
    part_z = jnp.sum(along_y * weights[:, :, None, :], axis=(0, 1))
    first = jnp.dot(rows_z, phz.T, preferred_element_type=f32).reshape(n_q, cells_x, cells_y, S)
    by_e = jnp.einsum("qxyn,qe->xeyn", first, phq, precision=highest)
    part_core = jnp.einsum("my,xeyn->xemn", phy, by_e, precision=highest)

    rows_each = cells_y // (n_gx * n_gz * n_vert)
    cols_each = K // (n_gx * n_vert)
    core_rows = S * S // n_gx
    n_gzv = n_gz * n_vert
    sy = part_y.reshape(n_gx, n_gzv, rows_each, K)
    sz = part_z.T.reshape(n_gx, n_vert, cols_each, cells_z)
    sx = part_x
    core = (
        part_core.reshape(cells_x, E, n_gx, core_rows)
        .transpose(2, 0, 1, 3)
        .reshape(1, n_gx, cells_x * E * core_rows)
    )

    v_me = lax.axis_index("vert")
    merge_sz = n_vert == 2
    for d, r in ([] if merge_sz else digit_steps(n_vert)):
        digit = (v_me // d) % r
        at = split_digit(sz, 1, r, digit)
        total = at(0)
        for s in range(1, r):
            (got,) = send_to("vert", n_vert, s * d, [at(s)])
            total = total + got
        sz = total
    gzv_me = linear_index(("gz", "vert"))
    for d, r in digit_steps(n_gzv):
        digit = (gzv_me // d) % r
        at = split_digit(sy, 1, r, digit)
        sy_total, sx_total, core_total = at(0), sx, core
        with_sz = merge_sz and d == 1
        if with_sz:
            at_z = split_digit(sz, 1, 2, v_me)
            sz_total = at_z(0)
        for s in range(1, r):
            pieces = [at(s), sx, core] + ([at_z(1)] if with_sz and s == 1 else [])
            got = send_to(("gz", "vert"), n_gzv, s * d, pieces)
            sy_total, sx_total, core_total = sy_total + got[0], sx_total + got[1], core_total + got[2]
            if with_sz and s == 1:
                sz_total = sz_total + got[3]
        sy, sx, core = sy_total, sx_total, core_total
        if with_sz:
            sz = sz_total
    for d, r in digit_steps(n_gx):
        digit = (gx_me // d) % r
        at_y = split_digit(sy, 0, r, digit)
        at_z = split_digit(sz, 0, r, digit)
        at_c = split_digit(core, 1, r, digit)
        sy_total, sz_total, core_parts = at_y(0), at_z(0), [at_c(0)]
        for s in range(1, r):
            g_sy, g_sz, g_core = send_to("gx", n_gx, s * d, [at_y(s), at_z(s), at_c(s)])
            sy_total, sz_total = sy_total + g_sy, sz_total + g_sz
            core_parts.append(g_core)
        sy, sz = sy_total, sz_total
        core = jnp.concatenate(core_parts, axis=0)

    src = jnp.bitwise_xor(gx_me, jnp.arange(n_gx, dtype=jnp.int32))
    x_src = (src[:, None] * cells_x + jnp.arange(cells_x, dtype=jnp.int32)[None, :]).reshape(-1)
    phx = test_table(sketch_ids, x_src, total_x, core_stream, 5).astype(f32).reshape(S, n_gx, cells_x)
    held = core.reshape(n_gx, cells_x, E, core_rows)
    core_out = jnp.einsum("jxer,ajx->rea", held, phx, precision=highest)

    scale_x = 3.0**1.5 / math.sqrt(cells_y * total_z * total_q)
    scale_y = 3.0**1.5 / math.sqrt(total_x * total_z * total_q)
    scale_z = 3.0**1.5 / math.sqrt(total_x * cells_y * total_q)
    scale_core = 9.0 / math.sqrt(total_x * cells_y * total_z * total_q)
    return (
        sx * scale_x,
        sy.reshape(rows_each, K) * scale_y,
        sz.reshape(cols_each, cells_z).T * scale_z,
        core_out * scale_core,
    )


def solution(mesh):
    in_specs = (P("groups", "vert", None, "gx", None, "gz"), P("groups"), P("groups", "vert"))
    out_specs = (
        P(("groups", "gx"), None),
        P(("groups", "gx", "gz", "vert"), None),
        P(("groups", "gz"), ("gx", "vert")),
        P(("groups", "gx"), None, None),
    )
    return jax.shard_map(shards, mesh=mesh, in_specs=in_specs, out_specs=out_specs, check_vma=False)
```

```python
import math

import jax
import jax.numpy as jnp
from jax import lax
from jax.sharding import PartitionSpec as P

K = 128
S = 48
E = 2


def hash_index(index, stream, salt):
    mixed = index * -1640531535 + stream * -2048144777 + salt
    mixed = jnp.bitwise_xor(mixed, lax.shift_right_logical(mixed, jnp.int32(16)))
    mixed = mixed * 739982445
    mixed = jnp.bitwise_xor(mixed, lax.shift_right_logical(mixed, jnp.int32(13)))
    mixed = mixed * 695872825
    return jnp.bitwise_xor(mixed, lax.shift_right_logical(mixed, jnp.int32(16)))


def unit_value(index, stream, salt):
    upper = lax.shift_right_logical(hash_index(index, stream, salt), jnp.int32(9))
    return ((2 * upper + 1).astype(jnp.float32) * 2.0 ** (-24) - 1.0).astype(jnp.bfloat16)


def test_table(row_ids, col_ids, stride, stream, salt):
    return unit_value(row_ids[:, None] * stride + col_ids[None, :], stream, salt)


def digit_steps(n, widest=4):
    d, out = 1, []
    while d < n:
        r = widest if n // d >= widest else 2
        out.append((d, r))
        d *= r
    return out


def split_digit(arr, dim, r, digit):
    shape = arr.shape
    split = arr.reshape(shape[:dim] + (shape[dim] // r, r) + shape[dim + 1 :])

    def at(s):
        return lax.dynamic_index_in_dim(split, jnp.bitwise_xor(digit, s), dim + 1, keepdims=False)

    return at


def send_to(axes, n, shift, pieces):
    dense = all(p.size % 128 == 0 for p in pieces)
    if dense:
        flat = jnp.concatenate([p.reshape(-1, 128) for p in pieces], axis=0)
    else:
        flat = jnp.concatenate([p.reshape(-1) for p in pieces])
    got = lax.ppermute(flat, axes, [(i, i ^ shift) for i in range(n)])
    out, at = [], 0
    for p in pieces:
        rows = p.size // 128 if dense else p.size
        out.append(got[at : at + rows].reshape(p.shape))
        at += rows
    return out


def linear_index(axes):
    idx = 0
    for a in axes:
        idx = idx * lax.axis_size(a) + lax.axis_index(a)
    return idx


def shards(flow_field, test_streams, snapshot_ids):
    highest = lax.Precision.HIGHEST
    f32 = jnp.float32
    bf16 = jnp.bfloat16
    batches, local_snaps, variables, cells_x, cells_y, cells_z = flow_field.shape
    n_gx = lax.axis_size("gx")
    n_gz = lax.axis_size("gz")
    n_vert = lax.axis_size("vert")
    total_x = cells_x * n_gx
    total_z = cells_z * n_gz
    total_q = variables * batches * local_snaps * n_vert
    factor_stream = test_streams[0]
    core_stream = test_streams[1]
    gx_me = lax.axis_index("gx")
    rank_ids = jnp.arange(K, dtype=jnp.int32)
    sketch_ids = jnp.arange(S, dtype=jnp.int32)
    x_ids = gx_me * cells_x + jnp.arange(cells_x, dtype=jnp.int32)
    y_ids = jnp.arange(cells_y, dtype=jnp.int32)
    z_ids = lax.axis_index("gz") * cells_z + jnp.arange(cells_z, dtype=jnp.int32)
    q_ids = (
        snapshot_ids[:, :, None] * variables + jnp.arange(variables, dtype=jnp.int32)[None, None, :]
    ).reshape(-1)
    ax = test_table(x_ids, rank_ids, K, factor_stream, 1).astype(f32)
    ay = test_table(y_ids, rank_ids, K, factor_stream, 2)
    az = test_table(z_ids, rank_ids, K, factor_stream, 3)
    aq = test_table(q_ids, rank_ids, K, factor_stream, 4).astype(f32)
    phy = test_table(sketch_ids, y_ids, cells_y, core_stream, 6).astype(f32)
    phz = test_table(sketch_ids, z_ids, total_z, core_stream, 7)
    phq = test_table(q_ids, jnp.arange(E, dtype=jnp.int32), E, core_stream, 8).astype(f32)

    n_q = batches * local_snaps * variables
    field = flow_field.reshape(n_q, cells_x, cells_y, cells_z)
    rows_z = field.reshape(-1, cells_z)

    qz = aq[:, None, :] * az.astype(f32)[None, :, :]
    qz_hi = qz.astype(bf16)
    qz_lo = (qz - qz_hi.astype(f32)).astype(bf16)
    both = jnp.einsum(
        "qxyz,qzk->xyk", field, jnp.concatenate([qz_hi, qz_lo], axis=-1), preferred_element_type=f32
    )
    by_q = both[..., :K] + both[..., K:]
    part_y = jnp.sum(by_q * ax[:, None, :], axis=0)
    part_x = jnp.sum(by_q * ay.astype(f32)[None, :, :], axis=1)
    along_y = jnp.einsum("qxyz,yk->qxzk", field, ay, preferred_element_type=f32)
    weights = aq[:, None, :] * ax[None, :, :]
    part_z = jnp.sum(along_y * weights[:, :, None, :], axis=(0, 1))
    first = jnp.dot(rows_z, phz.T, preferred_element_type=f32).reshape(n_q, cells_x, cells_y, S)
    by_e = jnp.einsum("qxyn,qe->xeyn", first, phq, precision=highest)
    part_core = jnp.einsum("my,xeyn->xemn", phy, by_e, precision=highest)

    rows_each = cells_y // (n_gx * n_gz * n_vert)
    cols_each = K // (n_gx * n_vert)
    core_rows = S * S // n_gx
    n_gzv = n_gz * n_vert
    sy = part_y.reshape(n_gx, n_gzv, rows_each, K)
    sz = part_z.T.reshape(n_gx, n_vert, cols_each, cells_z)
    sx = part_x
    core = (
        part_core.reshape(cells_x, E, n_gx, core_rows)
        .transpose(2, 0, 1, 3)
        .reshape(1, n_gx, cells_x * E * core_rows)
    )

    v_me = lax.axis_index("vert")
    merge_sz = n_vert == 2
    for d, r in ([] if merge_sz else digit_steps(n_vert)):
        digit = (v_me // d) % r
        at = split_digit(sz, 1, r, digit)
        total = at(0)
        for s in range(1, r):
            (got,) = send_to("vert", n_vert, s * d, [at(s)])
            total = total + got
        sz = total
    gzv_me = linear_index(("gz", "vert"))
    for d, r in digit_steps(n_gzv, 2):
        digit = (gzv_me // d) % r
        at = split_digit(sy, 1, r, digit)
        sy_total, sx_total, core_total = at(0), sx, core
        with_sz = merge_sz and d == 1
        if with_sz:
            at_z = split_digit(sz, 1, 2, v_me)
            sz_total = at_z(0)
        for s in range(1, r):
            pieces = [at(s), sx, core] + ([at_z(1)] if with_sz and s == 1 else [])
            got = send_to(("gz", "vert"), n_gzv, s * d, pieces)
            sy_total, sx_total, core_total = sy_total + got[0], sx_total + got[1], core_total + got[2]
            if with_sz and s == 1:
                sz_total = sz_total + got[3]
        sy, sx, core = sy_total, sx_total, core_total
        if with_sz:
            sz = sz_total
    for d, r in digit_steps(n_gx):
        digit = (gx_me // d) % r
        at_y = split_digit(sy, 0, r, digit)
        at_z = split_digit(sz, 0, r, digit)
        at_c = split_digit(core, 1, r, digit)
        sy_total, sz_total, core_parts = at_y(0), at_z(0), [at_c(0)]
        for s in range(1, r):
            g_sy, g_sz, g_core = send_to("gx", n_gx, s * d, [at_y(s), at_z(s), at_c(s)])
            sy_total, sz_total = sy_total + g_sy, sz_total + g_sz
            core_parts.append(g_core)
        sy, sz = sy_total, sz_total
        core = jnp.concatenate(core_parts, axis=0)

    src = jnp.bitwise_xor(gx_me, jnp.arange(n_gx, dtype=jnp.int32))
    x_src = (src[:, None] * cells_x + jnp.arange(cells_x, dtype=jnp.int32)[None, :]).reshape(-1)
    phx = test_table(sketch_ids, x_src, total_x, core_stream, 5).astype(f32).reshape(S, n_gx, cells_x)
    held = core.reshape(n_gx, cells_x, E, core_rows)
    core_out = jnp.einsum("jxer,ajx->rea", held, phx, precision=highest)

    scale_x = 3.0**1.5 / math.sqrt(cells_y * total_z * total_q)
    scale_y = 3.0**1.5 / math.sqrt(total_x * total_z * total_q)
    scale_z = 3.0**1.5 / math.sqrt(total_x * cells_y * total_q)
    scale_core = 9.0 / math.sqrt(total_x * cells_y * total_z * total_q)
    return (
        sx * scale_x,
        sy.reshape(rows_each, K) * scale_y,
        sz.reshape(cols_each, cells_z).T * scale_z,
        core_out * scale_core,
    )


def solution(mesh):
    in_specs = (P("groups", "vert", None, "gx", None, "gz"), P("groups"), P("groups", "vert"))
    out_specs = (
        P(("groups", "gx"), None),
        P(("groups", "gx", "gz", "vert"), None),
        P(("groups", "gz"), ("gx", "vert")),
        P(("groups", "gx"), None, None),
    )
    return jax.shard_map(shards, mesh=mesh, in_specs=in_specs, out_specs=out_specs, check_vma=False)
```

```python
import math

import jax
import jax.numpy as jnp
from jax import lax
from jax.sharding import PartitionSpec as P

K = 128
S = 48
E = 2


def hash_index(index, stream, salt):
    mixed = index * -1640531535 + stream * -2048144777 + salt
    mixed = jnp.bitwise_xor(mixed, lax.shift_right_logical(mixed, jnp.int32(16)))
    mixed = mixed * 739982445
    mixed = jnp.bitwise_xor(mixed, lax.shift_right_logical(mixed, jnp.int32(13)))
    mixed = mixed * 695872825
    return jnp.bitwise_xor(mixed, lax.shift_right_logical(mixed, jnp.int32(16)))


def unit_value(index, stream, salt):
    upper = lax.shift_right_logical(hash_index(index, stream, salt), jnp.int32(9))
    return ((2 * upper + 1).astype(jnp.float32) * 2.0 ** (-24) - 1.0).astype(jnp.bfloat16)


def test_table(row_ids, col_ids, stride, stream, salt):
    return unit_value(row_ids[:, None] * stride + col_ids[None, :], stream, salt)


def digit_steps(n):
    d, out = 1, []
    while d < n:
        r = 4 if n // d >= 4 else 2
        out.append((d, r))
        d *= r
    return out


def split_digit(arr, dim, r, digit):
    shape = arr.shape
    split = arr.reshape(shape[:dim] + (shape[dim] // r, r) + shape[dim + 1 :])

    def at(s):
        return lax.dynamic_index_in_dim(split, jnp.bitwise_xor(digit, s), dim + 1, keepdims=False)

    return at


def send_to(axes, n, shift, pieces):
    dense = all(p.size % 128 == 0 for p in pieces)
    if dense:
        flat = jnp.concatenate([p.reshape(-1, 128) for p in pieces], axis=0)
    else:
        flat = jnp.concatenate([p.reshape(-1) for p in pieces])
    got = lax.ppermute(flat, axes, [(i, i ^ shift) for i in range(n)])
    out, at = [], 0
    for p in pieces:
        rows = p.size // 128 if dense else p.size
        out.append(got[at : at + rows].reshape(p.shape))
        at += rows
    return out


def linear_index(axes):
    idx = 0
    for a in axes:
        idx = idx * lax.axis_size(a) + lax.axis_index(a)
    return idx


def shards(flow_field, test_streams, snapshot_ids):
    highest = lax.Precision.HIGHEST
    f32 = jnp.float32
    bf16 = jnp.bfloat16
    batches, local_snaps, variables, cells_x, cells_y, cells_z = flow_field.shape
    n_gx = lax.axis_size("gx")
    n_gz = lax.axis_size("gz")
    n_vert = lax.axis_size("vert")
    total_x = cells_x * n_gx
    total_z = cells_z * n_gz
    total_q = variables * batches * local_snaps * n_vert
    factor_stream = test_streams[0]
    core_stream = test_streams[1]
    gx_me = lax.axis_index("gx")
    rank_ids = jnp.arange(K, dtype=jnp.int32)
    sketch_ids = jnp.arange(S, dtype=jnp.int32)
    x_ids = gx_me * cells_x + jnp.arange(cells_x, dtype=jnp.int32)
    y_ids = jnp.arange(cells_y, dtype=jnp.int32)
    z_ids = lax.axis_index("gz") * cells_z + jnp.arange(cells_z, dtype=jnp.int32)
    q_ids = (
        snapshot_ids[:, :, None] * variables + jnp.arange(variables, dtype=jnp.int32)[None, None, :]
    ).reshape(-1)
    ax = test_table(x_ids, rank_ids, K, factor_stream, 1).astype(f32)
    ay = test_table(y_ids, rank_ids, K, factor_stream, 2)
    az = test_table(z_ids, rank_ids, K, factor_stream, 3)
    aq = test_table(q_ids, rank_ids, K, factor_stream, 4).astype(f32)
    phy = test_table(sketch_ids, y_ids, cells_y, core_stream, 6).astype(f32)
    phz = test_table(sketch_ids, z_ids, total_z, core_stream, 7)
    phq = test_table(q_ids, jnp.arange(E, dtype=jnp.int32), E, core_stream, 8).astype(f32)
    src = jnp.bitwise_xor(gx_me, jnp.arange(n_gx, dtype=jnp.int32))
    x_src = (src[:, None] * cells_x + jnp.arange(cells_x, dtype=jnp.int32)[None, :]).reshape(-1)
    phx = test_table(sketch_ids, x_src, total_x, core_stream, 5).astype(f32).reshape(S, n_gx, cells_x)
    ax, ay, az, aq, phy, phz, phq, phx = lax.optimization_barrier((ax, ay, az, aq, phy, phz, phq, phx))

    n_q = batches * local_snaps * variables
    field = flow_field.reshape(n_q, cells_x, cells_y, cells_z)
    rows_z = field.reshape(-1, cells_z)

    qz = aq[:, None, :] * az.astype(f32)[None, :, :]
    qz_hi = qz.astype(bf16)
    qz_lo = (qz - qz_hi.astype(f32)).astype(bf16)
    both = jnp.einsum(
        "qxyz,qzk->xyk", field, jnp.concatenate([qz_hi, qz_lo], axis=-1), preferred_element_type=f32
    )
    by_q = both[..., :K] + both[..., K:]
    part_y = jnp.sum(by_q * ax[:, None, :], axis=0)
    part_x = jnp.sum(by_q * ay.astype(f32)[None, :, :], axis=1)
    along_y = jnp.einsum("qxyz,yk->qxzk", field, ay, preferred_element_type=f32)
    weights = aq[:, None, :] * ax[None, :, :]
    part_z = jnp.sum(along_y * weights[:, :, None, :], axis=(0, 1))
    first = jnp.dot(rows_z, phz.T, preferred_element_type=f32).reshape(n_q, cells_x, cells_y, S)
    by_e = jnp.einsum("qxyn,qe->xeyn", first, phq, precision=highest)
    part_core = jnp.einsum("my,xeyn->xemn", phy, by_e, precision=highest)

    rows_each = cells_y // (n_gx * n_gz * n_vert)
    cols_each = K // (n_gx * n_vert)
    core_rows = S * S // n_gx
    n_gzv = n_gz * n_vert
    sy = part_y.reshape(n_gx, n_gzv, rows_each, K)
    sz = part_z.T.reshape(n_gx, n_vert, cols_each, cells_z)
    sx = part_x
    core = (
        part_core.reshape(cells_x, E, n_gx, core_rows)
        .transpose(2, 0, 1, 3)
        .reshape(1, n_gx, cells_x * E * core_rows)
    )

    v_me = lax.axis_index("vert")
    merge_sz = n_vert == 2
    for d, r in ([] if merge_sz else digit_steps(n_vert)):
        digit = (v_me // d) % r
        at = split_digit(sz, 1, r, digit)
        total = at(0)
        for s in range(1, r):
            (got,) = send_to("vert", n_vert, s * d, [at(s)])
            total = total + got
        sz = total
    gzv_me = linear_index(("gz", "vert"))
    for d, r in digit_steps(n_gzv):
        digit = (gzv_me // d) % r
        at = split_digit(sy, 1, r, digit)
        sy_total, sx_total, core_total = at(0), sx, core
        with_sz = merge_sz and d == 1
        if with_sz:
            at_z = split_digit(sz, 1, 2, v_me)
            sz_total = at_z(0)
        for s in range(1, r):
            pieces = [at(s), sx, core] + ([at_z(1)] if with_sz and s == 1 else [])
            got = send_to(("gz", "vert"), n_gzv, s * d, pieces)
            sy_total, sx_total, core_total = sy_total + got[0], sx_total + got[1], core_total + got[2]
            if with_sz and s == 1:
                sz_total = sz_total + got[3]
        sy, sx, core = sy_total, sx_total, core_total
        if with_sz:
            sz = sz_total
    for d, r in digit_steps(n_gx):
        digit = (gx_me // d) % r
        at_y = split_digit(sy, 0, r, digit)
        at_z = split_digit(sz, 0, r, digit)
        at_c = split_digit(core, 1, r, digit)
        sy_total, sz_total, core_parts = at_y(0), at_z(0), [at_c(0)]
        for s in range(1, r):
            g_sy, g_sz, g_core = send_to("gx", n_gx, s * d, [at_y(s), at_z(s), at_c(s)])
            sy_total, sz_total = sy_total + g_sy, sz_total + g_sz
            core_parts.append(g_core)
        sy, sz = sy_total, sz_total
        core = jnp.concatenate(core_parts, axis=0)

    held = core.reshape(n_gx, cells_x, E, core_rows)
    core_out = jnp.einsum("jxer,ajx->rea", held, phx, precision=highest)

    scale_x = 3.0**1.5 / math.sqrt(cells_y * total_z * total_q)
    scale_y = 3.0**1.5 / math.sqrt(total_x * total_z * total_q)
    scale_z = 3.0**1.5 / math.sqrt(total_x * cells_y * total_q)
    scale_core = 9.0 / math.sqrt(total_x * cells_y * total_z * total_q)
    return (
        sx * scale_x,
        sy.reshape(rows_each, K) * scale_y,
        sz.reshape(cols_each, cells_z).T * scale_z,
        core_out * scale_core,
    )


def solution(mesh):
    in_specs = (P("groups", "vert", None, "gx", None, "gz"), P("groups"), P("groups", "vert"))
    out_specs = (
        P(("groups", "gx"), None),
        P(("groups", "gx", "gz", "vert"), None),
        P(("groups", "gz"), ("gx", "vert")),
        P(("groups", "gx"), None, None),
    )
    return jax.shard_map(shards, mesh=mesh, in_specs=in_specs, out_specs=out_specs, check_vma=False)
```

```python
import math

import jax
import jax.numpy as jnp
from jax import lax
from jax.sharding import PartitionSpec as P

K = 128
S = 48
E = 2


def mix_bits(mixed):
    mixed = jnp.bitwise_xor(mixed, lax.shift_right_logical(mixed, jnp.int32(16)))
    mixed = mixed * 739982445
    mixed = jnp.bitwise_xor(mixed, lax.shift_right_logical(mixed, jnp.int32(13)))
    mixed = mixed * 695872825
    return jnp.bitwise_xor(mixed, lax.shift_right_logical(mixed, jnp.int32(16)))


def test_table(row_ids, col_ids, stride, stream, salt):
    row_term = (row_ids * stride) * -1640531535
    col_term = col_ids * -1640531535 + stream * -2048144777 + salt
    upper = lax.shift_right_logical(mix_bits(row_term[:, None] + col_term[None, :]), jnp.int32(9))
    return ((2 * upper + 1).astype(jnp.float32) * 2.0 ** (-24) - 1.0).astype(jnp.bfloat16)


def digit_steps(n):
    d, out = 1, []
    while d < n:
        r = 4 if n // d >= 4 else 2
        out.append((d, r))
        d *= r
    return out


def split_digit(arr, dim, r, digit):
    shape = arr.shape
    split = arr.reshape(shape[:dim] + (shape[dim] // r, r) + shape[dim + 1 :])

    def at(s):
        return lax.dynamic_index_in_dim(split, jnp.bitwise_xor(digit, s), dim + 1, keepdims=False)

    return at


def send_to(axes, n, shift, pieces):
    dense = all(p.size % 128 == 0 for p in pieces)
    if dense:
        flat = jnp.concatenate([p.reshape(-1, 128) for p in pieces], axis=0)
    else:
        flat = jnp.concatenate([p.reshape(-1) for p in pieces])
    got = lax.ppermute(flat, axes, [(i, i ^ shift) for i in range(n)])
    out, at = [], 0
    for p in pieces:
        rows = p.size // 128 if dense else p.size
        out.append(got[at : at + rows].reshape(p.shape))
        at += rows
    return out


def linear_index(axes):
    idx = 0
    for a in axes:
        idx = idx * lax.axis_size(a) + lax.axis_index(a)
    return idx


def shards(flow_field, test_streams, snapshot_ids):
    highest = lax.Precision.HIGHEST
    f32 = jnp.float32
    bf16 = jnp.bfloat16
    batches, local_snaps, variables, cells_x, cells_y, cells_z = flow_field.shape
    n_gx = lax.axis_size("gx")
    n_gz = lax.axis_size("gz")
    n_vert = lax.axis_size("vert")
    total_x = cells_x * n_gx
    total_z = cells_z * n_gz
    total_q = variables * batches * local_snaps * n_vert
    factor_stream = test_streams[0]
    core_stream = test_streams[1]
    gx_me = lax.axis_index("gx")
    rank_ids = jnp.arange(K, dtype=jnp.int32)
    sketch_ids = jnp.arange(S, dtype=jnp.int32)
    x_ids = gx_me * cells_x + jnp.arange(cells_x, dtype=jnp.int32)
    y_ids = jnp.arange(cells_y, dtype=jnp.int32)
    z_ids = lax.axis_index("gz") * cells_z + jnp.arange(cells_z, dtype=jnp.int32)
    q_ids = (
        snapshot_ids[:, :, None] * variables + jnp.arange(variables, dtype=jnp.int32)[None, None, :]
    ).reshape(-1)
    ax = test_table(x_ids, rank_ids, K, factor_stream, 1).astype(f32)
    ay = test_table(y_ids, rank_ids, K, factor_stream, 2)
    az = test_table(z_ids, rank_ids, K, factor_stream, 3)
    aq = test_table(q_ids, rank_ids, K, factor_stream, 4).astype(f32)
    phy = test_table(sketch_ids, y_ids, cells_y, core_stream, 6).astype(f32)
    phz = test_table(sketch_ids, z_ids, total_z, core_stream, 7)
    phq = test_table(q_ids, jnp.arange(E, dtype=jnp.int32), E, core_stream, 8).astype(f32)

    n_q = batches * local_snaps * variables
    field = flow_field.reshape(n_q, cells_x, cells_y, cells_z)
    rows_z = field.reshape(-1, cells_z)

    qz = aq[:, None, :] * az.astype(f32)[None, :, :]
    qz_hi = qz.astype(bf16)
    qz_lo = (qz - qz_hi.astype(f32)).astype(bf16)
    both = jnp.einsum(
        "qxyz,qzk->xyk", field, jnp.concatenate([qz_hi, qz_lo], axis=-1), preferred_element_type=f32
    )
    by_q = both[..., :K] + both[..., K:]
    part_y = jnp.sum(by_q * ax[:, None, :], axis=0)
    part_x = jnp.sum(by_q * ay.astype(f32)[None, :, :], axis=1)
    along_y = jnp.einsum("qxyz,yk->qxzk", field, ay, preferred_element_type=f32)
    weights = aq[:, None, :] * ax[None, :, :]
    part_z = jnp.sum(along_y * weights[:, :, None, :], axis=(0, 1))
    first = jnp.dot(rows_z, phz.T, preferred_element_type=f32).reshape(n_q, cells_x, cells_y, S)
    by_e = jnp.einsum("qxyn,qe->xeyn", first, phq, precision=highest)
    part_core = jnp.einsum("my,xeyn->xemn", phy, by_e, precision=highest)

    rows_each = cells_y // (n_gx * n_gz * n_vert)
    cols_each = K // (n_gx * n_vert)
    core_rows = S * S // n_gx
    n_gzv = n_gz * n_vert
    sy = part_y.reshape(n_gx, n_gzv, rows_each, K)
    sz = part_z.T.reshape(n_gx, n_vert, cols_each, cells_z)
    sx = part_x
    core = (
        part_core.reshape(cells_x, E, n_gx, core_rows)
        .transpose(2, 0, 1, 3)
        .reshape(1, n_gx, cells_x * E * core_rows)
    )

    v_me = lax.axis_index("vert")
    merge_sz = n_vert == 2
    for d, r in ([] if merge_sz else digit_steps(n_vert)):
        digit = (v_me // d) % r
        at = split_digit(sz, 1, r, digit)
        total = at(0)
        for s in range(1, r):
            (got,) = send_to("vert", n_vert, s * d, [at(s)])
            total = total + got
        sz = total
    gzv_me = linear_index(("gz", "vert"))
    for d, r in digit_steps(n_gzv):
        digit = (gzv_me // d) % r
        at = split_digit(sy, 1, r, digit)
        sy_total, sx_total, core_total = at(0), sx, core
        with_sz = merge_sz and d == 1
        if with_sz:
            at_z = split_digit(sz, 1, 2, v_me)
            sz_total = at_z(0)
        for s in range(1, r):
            pieces = [at(s), sx, core] + ([at_z(1)] if with_sz and s == 1 else [])
            got = send_to(("gz", "vert"), n_gzv, s * d, pieces)
            sy_total, sx_total, core_total = sy_total + got[0], sx_total + got[1], core_total + got[2]
            if with_sz and s == 1:
                sz_total = sz_total + got[3]
        sy, sx, core = sy_total, sx_total, core_total
        if with_sz:
            sz = sz_total
    for d, r in digit_steps(n_gx):
        digit = (gx_me // d) % r
        at_y = split_digit(sy, 0, r, digit)
        at_z = split_digit(sz, 0, r, digit)
        at_c = split_digit(core, 1, r, digit)
        sy_total, sz_total, core_parts = at_y(0), at_z(0), [at_c(0)]
        for s in range(1, r):
            g_sy, g_sz, g_core = send_to("gx", n_gx, s * d, [at_y(s), at_z(s), at_c(s)])
            sy_total, sz_total = sy_total + g_sy, sz_total + g_sz
            core_parts.append(g_core)
        sy, sz = sy_total, sz_total
        core = jnp.concatenate(core_parts, axis=0)

    src = jnp.bitwise_xor(gx_me, jnp.arange(n_gx, dtype=jnp.int32))
    x_src = (src[:, None] * cells_x + jnp.arange(cells_x, dtype=jnp.int32)[None, :]).reshape(-1)
    phx = test_table(sketch_ids, x_src, total_x, core_stream, 5).astype(f32).reshape(S, n_gx, cells_x)
    held = core.reshape(n_gx, cells_x, E, core_rows)
    core_out = jnp.einsum("jxer,ajx->rea", held, phx, precision=highest)

    scale_x = 3.0**1.5 / math.sqrt(cells_y * total_z * total_q)
    scale_y = 3.0**1.5 / math.sqrt(total_x * total_z * total_q)
    scale_z = 3.0**1.5 / math.sqrt(total_x * cells_y * total_q)
    scale_core = 9.0 / math.sqrt(total_x * cells_y * total_z * total_q)
    return (
        sx * scale_x,
        sy.reshape(rows_each, K) * scale_y,
        sz.reshape(cols_each, cells_z).T * scale_z,
        core_out * scale_core,
    )


def solution(mesh):
    in_specs = (P("groups", "vert", None, "gx", None, "gz"), P("groups"), P("groups", "vert"))
    out_specs = (
        P(("groups", "gx"), None),
        P(("groups", "gx", "gz", "vert"), None),
        P(("groups", "gz"), ("gx", "vert")),
        P(("groups", "gx"), None, None),
    )
    return jax.shard_map(shards, mesh=mesh, in_specs=in_specs, out_specs=out_specs, check_vma=False)
```

```python
import math

import jax
import jax.numpy as jnp
from jax import lax
from jax.sharding import PartitionSpec as P

K = 128
S = 48
E = 2


def mix_bits(mixed):
    mixed = jnp.bitwise_xor(mixed, lax.shift_right_logical(mixed, jnp.int32(16)))
    mixed = mixed * 739982445
    mixed = jnp.bitwise_xor(mixed, lax.shift_right_logical(mixed, jnp.int32(13)))
    mixed = mixed * 695872825
    return jnp.bitwise_xor(mixed, lax.shift_right_logical(mixed, jnp.int32(16)))


def test_table(row_ids, col_ids, stride, stream, salt):
    row_term = (row_ids * stride) * -1640531535
    col_term = col_ids * -1640531535 + stream * -2048144777 + salt
    upper = lax.shift_right_logical(mix_bits(row_term[:, None] + col_term[None, :]), jnp.int32(9))
    return ((2 * upper + 1).astype(jnp.float32) * 2.0 ** (-24) - 1.0).astype(jnp.bfloat16)


def digit_steps(n):
    d, out = 1, []
    while d < n:
        r = 4 if n // d >= 4 else 2
        out.append((d, r))
        d *= r
    return out


def split_digit(arr, dim, r, digit):
    shape = arr.shape
    split = arr.reshape(shape[:dim] + (shape[dim] // r, r) + shape[dim + 1 :])

    def at(s):
        return lax.dynamic_index_in_dim(split, jnp.bitwise_xor(digit, s), dim + 1, keepdims=False)

    return at


def send_to(axes, n, shift, pieces):
    dense = all(p.size % 128 == 0 for p in pieces)
    if dense:
        flat = jnp.concatenate([p.reshape(-1, 128) for p in pieces], axis=0)
    else:
        flat = jnp.concatenate([p.reshape(-1) for p in pieces])
    got = lax.ppermute(flat, axes, [(i, i ^ shift) for i in range(n)])
    out, at = [], 0
    for p in pieces:
        rows = p.size // 128 if dense else p.size
        out.append(got[at : at + rows].reshape(p.shape))
        at += rows
    return out


def linear_index(axes):
    idx = 0
    for a in axes:
        idx = idx * lax.axis_size(a) + lax.axis_index(a)
    return idx


def shards(flow_field, test_streams, snapshot_ids):
    highest = lax.Precision.HIGHEST
    f32 = jnp.float32
    bf16 = jnp.bfloat16
    batches, local_snaps, variables, cells_x, cells_y, cells_z = flow_field.shape
    n_gx = lax.axis_size("gx")
    n_gz = lax.axis_size("gz")
    n_vert = lax.axis_size("vert")
    total_x = cells_x * n_gx
    total_z = cells_z * n_gz
    total_q = variables * batches * local_snaps * n_vert
    factor_stream = test_streams[0]
    core_stream = test_streams[1]
    gx_me = lax.axis_index("gx")
    rank_ids = jnp.arange(K, dtype=jnp.int32)
    sketch_ids = jnp.arange(S, dtype=jnp.int32)
    x_ids = gx_me * cells_x + jnp.arange(cells_x, dtype=jnp.int32)
    y_ids = jnp.arange(cells_y, dtype=jnp.int32)
    z_ids = lax.axis_index("gz") * cells_z + jnp.arange(cells_z, dtype=jnp.int32)
    q_ids = (
        snapshot_ids[:, :, None] * variables + jnp.arange(variables, dtype=jnp.int32)[None, None, :]
    ).reshape(-1)
    ax = test_table(x_ids, rank_ids, K, factor_stream, 1).astype(f32)
    ay = test_table(y_ids, rank_ids, K, factor_stream, 2)
    az = test_table(z_ids, rank_ids, K, factor_stream, 3)
    aq = test_table(q_ids, rank_ids, K, factor_stream, 4).astype(f32)
    phy = test_table(sketch_ids, y_ids, cells_y, core_stream, 6).astype(f32)
    phz = test_table(sketch_ids, z_ids, total_z, core_stream, 7)
    phq = test_table(q_ids, jnp.arange(E, dtype=jnp.int32), E, core_stream, 8).astype(f32)

    n_q = batches * local_snaps * variables
    field = flow_field.reshape(n_q, cells_x, cells_y, cells_z)
    rows_z = field.reshape(-1, cells_z)

    qz = aq[:, None, :] * az.astype(f32)[None, :, :]
    qz_hi = qz.astype(bf16)
    qz_lo = (qz - qz_hi.astype(f32)).astype(bf16)
    both = jnp.einsum(
        "qxyz,qzk->xyk", field, jnp.concatenate([qz_hi, qz_lo], axis=-1), preferred_element_type=f32
    )
    by_q = both[..., :K] + both[..., K:]
    part_y = jnp.sum(by_q * ax[:, None, :], axis=0)
    part_x = jnp.sum(by_q * ay.astype(f32)[None, :, :], axis=1)
    along_y = jnp.einsum("qxyz,yk->qxzk", field, ay, preferred_element_type=f32)
    weights = aq[:, None, :] * ax[None, :, :]
    part_z = jnp.sum(along_y * weights[:, :, None, :], axis=(0, 1))
    first = jnp.dot(rows_z, phz.T, preferred_element_type=f32).reshape(n_q, cells_x, cells_y, S)
    by_e = jnp.einsum("qxyn,qe->xeyn", first, phq, precision=highest)
    part_core = jnp.einsum("my,xeyn->xemn", phy, by_e, precision=highest)

    rows_each = cells_y // (n_gx * n_gz * n_vert)
    cols_each = K // (n_gx * n_vert)
    core_rows = S * S // n_gx
    n_gzv = n_gz * n_vert
    sy = part_y.reshape(n_gx, n_gzv, rows_each, K)
    sz = part_z.T.reshape(n_gx, n_vert, cols_each, cells_z)
    sx = part_x
    core = (
        part_core.reshape(cells_x, E, n_gx, core_rows)
        .transpose(2, 0, 1, 3)
        .reshape(1, n_gx, cells_x * E * core_rows)
    )

    v_me = lax.axis_index("vert")
    merge_sz = n_vert == 2
    for d, r in ([] if merge_sz else digit_steps(n_vert)):
        digit = (v_me // d) % r
        at = split_digit(sz, 1, r, digit)
        total = at(0)
        for s in range(1, r):
            (got,) = send_to("vert", n_vert, s * d, [at(s)])
            total = total + got
        sz = total
    gzv_me = linear_index(("gz", "vert"))
    for d, r in digit_steps(n_gzv):
        digit = (gzv_me // d) % r
        at = split_digit(sy, 1, r, digit)
        sy_total, sx_total, core_total = at(0), sx, core
        with_sz = merge_sz and d == 1
        if with_sz:
            at_z = split_digit(sz, 1, 2, v_me)
            sz_total = at_z(0)
        for s in range(1, r):
            pieces = [at(s), sx, core] + ([at_z(1)] if with_sz and s == 1 else [])
            got = send_to(("gz", "vert"), n_gzv, s * d, pieces)
            sy_total, sx_total, core_total = sy_total + got[0], sx_total + got[1], core_total + got[2]
            if with_sz and s == 1:
                sz_total = sz_total + got[3]
        sy, sx, core = sy_total, sx_total, core_total
        if with_sz:
            sz = sz_total
    for d, r in digit_steps(n_gx):
        digit = (gx_me // d) % r
        at_y = split_digit(sy, 0, r, digit)
        at_z = split_digit(sz, 0, r, digit)
        at_c = split_digit(core, 1, r, digit)
        sy_total, sz_total, core_parts = at_y(0), at_z(0), [at_c(0)]
        for s in range(1, r):
            g_sy, g_sz, g_core = send_to("gx", n_gx, s * d, [at_y(s), at_z(s), at_c(s)])
            sy_total, sz_total = sy_total + g_sy, sz_total + g_sz
            core_parts.append(g_core)
        sy, sz = sy_total, sz_total
        core = jnp.concatenate(core_parts, axis=0)

    src = jnp.bitwise_xor(gx_me, jnp.arange(n_gx, dtype=jnp.int32))
    x_src = (src[:, None] * cells_x + jnp.arange(cells_x, dtype=jnp.int32)[None, :]).reshape(-1)
    phx = test_table(sketch_ids, x_src, total_x, core_stream, 5).astype(f32).reshape(S, n_gx, cells_x)
    held = core.reshape(n_gx * cells_x, E, core_rows)
    weights_x = phx.reshape(S, n_gx * cells_x)
    core_out = jnp.sum(held[:, None, :, :] * weights_x.T[:, :, None, None], axis=0).transpose(2, 1, 0)

    scale_x = 3.0**1.5 / math.sqrt(cells_y * total_z * total_q)
    scale_y = 3.0**1.5 / math.sqrt(total_x * total_z * total_q)
    scale_z = 3.0**1.5 / math.sqrt(total_x * cells_y * total_q)
    scale_core = 9.0 / math.sqrt(total_x * cells_y * total_z * total_q)
    return (
        sx * scale_x,
        sy.reshape(rows_each, K) * scale_y,
        sz.reshape(cols_each, cells_z).T * scale_z,
        core_out * scale_core,
    )


def solution(mesh):
    in_specs = (P("groups", "vert", None, "gx", None, "gz"), P("groups"), P("groups", "vert"))
    out_specs = (
        P(("groups", "gx"), None),
        P(("groups", "gx", "gz", "vert"), None),
        P(("groups", "gz"), ("gx", "vert")),
        P(("groups", "gx"), None, None),
    )
    return jax.shard_map(shards, mesh=mesh, in_specs=in_specs, out_specs=out_specs, check_vma=False)
```

```python
import math

import jax
import jax.numpy as jnp
from jax import lax
from jax.sharding import PartitionSpec as P

K = 128
S = 48
E = 2


def mix_bits(mixed):
    mixed = jnp.bitwise_xor(mixed, lax.shift_right_logical(mixed, jnp.int32(16)))
    mixed = mixed * 739982445
    mixed = jnp.bitwise_xor(mixed, lax.shift_right_logical(mixed, jnp.int32(13)))
    mixed = mixed * 695872825
    return jnp.bitwise_xor(mixed, lax.shift_right_logical(mixed, jnp.int32(16)))


def test_table(row_ids, col_ids, stride, stream, salt):
    row_term = (row_ids * stride) * -1640531535
    col_term = col_ids * -1640531535 + stream * -2048144777 + salt
    upper = lax.shift_right_logical(mix_bits(row_term[:, None] + col_term[None, :]), jnp.int32(9))
    return ((2 * upper + 1).astype(jnp.float32) * 2.0 ** (-24) - 1.0).astype(jnp.bfloat16)


def digit_steps(n):
    d, out = 1, []
    while d < n:
        r = 4 if n // d >= 4 else 2
        out.append((d, r))
        d *= r
    return out


def split_digit(arr, dim, r, digit):
    shape = arr.shape
    split = arr.reshape(shape[:dim] + (shape[dim] // r, r) + shape[dim + 1 :])

    def at(s):
        return lax.dynamic_index_in_dim(split, jnp.bitwise_xor(digit, s), dim + 1, keepdims=False)

    return at


def send_to(axes, n, shift, pieces):
    dense = all(p.size % 128 == 0 for p in pieces)
    if dense:
        flat = jnp.concatenate([p.reshape(-1, 128) for p in pieces], axis=0)
    else:
        flat = jnp.concatenate([p.reshape(-1) for p in pieces])
    got = lax.ppermute(flat, axes, [(i, i ^ shift) for i in range(n)])
    out, at = [], 0
    for p in pieces:
        rows = p.size // 128 if dense else p.size
        out.append(got[at : at + rows].reshape(p.shape))
        at += rows
    return out


def linear_index(axes):
    idx = 0
    for a in axes:
        idx = idx * lax.axis_size(a) + lax.axis_index(a)
    return idx


def shards(flow_field, test_streams, snapshot_ids):
    highest = lax.Precision.HIGHEST
    f32 = jnp.float32
    bf16 = jnp.bfloat16
    batches, local_snaps, variables, cells_x, cells_y, cells_z = flow_field.shape
    n_gx = lax.axis_size("gx")
    n_gz = lax.axis_size("gz")
    n_vert = lax.axis_size("vert")
    total_x = cells_x * n_gx
    total_z = cells_z * n_gz
    total_q = variables * batches * local_snaps * n_vert
    factor_stream = test_streams[0]
    core_stream = test_streams[1]
    gx_me = lax.axis_index("gx")
    rank_ids = jnp.arange(K, dtype=jnp.int32)
    sketch_ids = jnp.arange(S, dtype=jnp.int32)
    x_ids = gx_me * cells_x + jnp.arange(cells_x, dtype=jnp.int32)
    y_ids = jnp.arange(cells_y, dtype=jnp.int32)
    z_ids = lax.axis_index("gz") * cells_z + jnp.arange(cells_z, dtype=jnp.int32)
    q_ids = (
        snapshot_ids[:, :, None] * variables + jnp.arange(variables, dtype=jnp.int32)[None, None, :]
    ).reshape(-1)
    ax = test_table(x_ids, rank_ids, K, factor_stream, 1).astype(f32)
    ay = test_table(y_ids, rank_ids, K, factor_stream, 2)
    az = test_table(z_ids, rank_ids, K, factor_stream, 3)
    aq = test_table(q_ids, rank_ids, K, factor_stream, 4).astype(f32)
    phy = test_table(sketch_ids, y_ids, cells_y, core_stream, 6).astype(f32)
    phz = test_table(sketch_ids, z_ids, total_z, core_stream, 7)
    phq = test_table(q_ids, jnp.arange(E, dtype=jnp.int32), E, core_stream, 8).astype(f32)

    n_q = batches * local_snaps * variables
    field = flow_field.reshape(n_q, cells_x, cells_y, cells_z)
    rows_z = field.reshape(-1, cells_z)

    qz = aq[:, None, :] * az.astype(f32)[None, :, :]
    qz_hi = qz.astype(bf16)
    qz_lo = (qz - qz_hi.astype(f32)).astype(bf16)
    both = jnp.einsum(
        "qxyz,qzk->xyk", field, jnp.concatenate([qz_hi, qz_lo], axis=-1), preferred_element_type=f32
    )
    by_q = both[..., :K] + both[..., K:]
    part_y = jnp.sum(by_q * ax[:, None, :], axis=0)
    part_x = jnp.sum(by_q * ay.astype(f32)[None, :, :], axis=1)
    along_y = jnp.einsum("qxyz,yk->qxzk", field, ay, preferred_element_type=f32)
    weights = aq[:, None, :] * ax[None, :, :]
    part_z = jnp.sum(along_y * weights[:, :, None, :], axis=(0, 1))
    first = jnp.dot(rows_z, phz.T, preferred_element_type=f32).reshape(n_q, cells_x, cells_y, S)
    by_e = jnp.einsum("qxyn,qe->xeyn", first, phq, precision=highest)
    part_core = jnp.einsum("my,xeyn->xemn", phy, by_e, precision=highest)

    rows_each = cells_y // (n_gx * n_gz * n_vert)
    cols_each = K // (n_gx * n_vert)
    core_rows = S * S // n_gx
    n_gzv = n_gz * n_vert
    sy = part_y.reshape(n_gx, n_gzv, rows_each, K)
    sz = part_z.T.reshape(n_gx, n_vert, cols_each, cells_z)
    sx = part_x
    core = (
        part_core.reshape(cells_x, E, n_gx, core_rows)
        .transpose(2, 0, 1, 3)
        .reshape(1, n_gx, cells_x * E * core_rows)
    )

    v_me = lax.axis_index("vert")
    merge_sz = n_vert == 2
    for d, r in ([] if merge_sz else digit_steps(n_vert)):
        digit = (v_me // d) % r
        at = split_digit(sz, 1, r, digit)
        total = at(0)
        for s in range(1, r):
            (got,) = send_to("vert", n_vert, s * d, [at(s)])
            total = total + got
        sz = total
    for d, r in digit_steps(n_gx):
        digit = (gx_me // d) % r
        at_y = split_digit(sy, 0, r, digit)
        at_z = split_digit(sz, 0, r, digit)
        at_c = split_digit(core, 1, r, digit)
        sy_total, sz_total, core_parts = at_y(0), at_z(0), [at_c(0)]
        for s in range(1, r):
            g_sy, g_sz, g_core = send_to("gx", n_gx, s * d, [at_y(s), at_z(s), at_c(s)])
            sy_total, sz_total = sy_total + g_sy, sz_total + g_sz
            core_parts.append(g_core)
        sy, sz = sy_total, sz_total
        core = jnp.concatenate(core_parts, axis=0)

    src = jnp.bitwise_xor(gx_me, jnp.arange(n_gx, dtype=jnp.int32))
    x_src = (src[:, None] * cells_x + jnp.arange(cells_x, dtype=jnp.int32)[None, :]).reshape(-1)
    phx = test_table(sketch_ids, x_src, total_x, core_stream, 5).astype(f32).reshape(S, n_gx, cells_x)
    gzv_me = linear_index(("gz", "vert"))
    for d, r in digit_steps(n_gzv):
        digit = (gzv_me // d) % r
        at = split_digit(sy, 1, r, digit)
        sy_total, sx_total, core_total = at(0), sx, core
        with_sz = merge_sz and d == 1
        if with_sz:
            at_z = split_digit(sz, 1, 2, v_me)
            sz_total = at_z(0)
        for s in range(1, r):
            pieces = [at(s), sx, core] + ([at_z(1)] if with_sz and s == 1 else [])
            got = send_to(("gz", "vert"), n_gzv, s * d, pieces)
            sy_total, sx_total, core_total = sy_total + got[0], sx_total + got[1], core_total + got[2]
            if with_sz and s == 1:
                sz_total = sz_total + got[3]
        sy, sx, core = sy_total, sx_total, core_total
        if with_sz:
            sz = sz_total
    held = core.reshape(n_gx * cells_x, E, core_rows)
    weights_x = phx.reshape(S, n_gx * cells_x)
    core_out = jnp.sum(held[:, None, :, :] * weights_x.T[:, :, None, None], axis=0).transpose(2, 1, 0)

    scale_x = 3.0**1.5 / math.sqrt(cells_y * total_z * total_q)
    scale_y = 3.0**1.5 / math.sqrt(total_x * total_z * total_q)
    scale_z = 3.0**1.5 / math.sqrt(total_x * cells_y * total_q)
    scale_core = 9.0 / math.sqrt(total_x * cells_y * total_z * total_q)
    return (
        sx * scale_x,
        sy.reshape(rows_each, K) * scale_y,
        sz.reshape(cols_each, cells_z).T * scale_z,
        core_out * scale_core,
    )


def solution(mesh):
    in_specs = (P("groups", "vert", None, "gx", None, "gz"), P("groups"), P("groups", "vert"))
    out_specs = (
        P(("groups", "gx"), None),
        P(("groups", "gx", "gz", "vert"), None),
        P(("groups", "gz"), ("gx", "vert")),
        P(("groups", "gx"), None, None),
    )
    return jax.shard_map(shards, mesh=mesh, in_specs=in_specs, out_specs=out_specs, check_vma=False)
```

```python
import math

import jax
import jax.numpy as jnp
from jax import lax
from jax.sharding import PartitionSpec as P

K = 128
S = 48
E = 2


def mix_bits(mixed):
    mixed = jnp.bitwise_xor(mixed, lax.shift_right_logical(mixed, jnp.int32(16)))
    mixed = mixed * 739982445
    mixed = jnp.bitwise_xor(mixed, lax.shift_right_logical(mixed, jnp.int32(13)))
    mixed = mixed * 695872825
    return jnp.bitwise_xor(mixed, lax.shift_right_logical(mixed, jnp.int32(16)))


def test_table(row_ids, col_ids, stride, stream, salt):
    row_term = (row_ids * stride) * -1640531535
    col_term = col_ids * -1640531535 + stream * -2048144777 + salt
    upper = lax.shift_right_logical(mix_bits(row_term[:, None] + col_term[None, :]), jnp.int32(9))
    return ((2 * upper + 1).astype(jnp.float32) * 2.0 ** (-24) - 1.0).astype(jnp.bfloat16)


def digit_steps(n):
    d, out = 1, []
    while d < n:
        r = 4 if n // d >= 4 else 2
        out.append((d, r))
        d *= r
    return out


def split_digit(arr, dim, r, digit):
    shape = arr.shape
    split = arr.reshape(shape[:dim] + (shape[dim] // r, r) + shape[dim + 1 :])

    def at(s):
        return lax.dynamic_index_in_dim(split, jnp.bitwise_xor(digit, s), dim + 1, keepdims=False)

    return at


def send_to(axes, n, shift, pieces):
    dense = all(p.size % 128 == 0 for p in pieces)
    if dense:
        flat = jnp.concatenate([p.reshape(-1, 128) for p in pieces], axis=0)
    else:
        flat = jnp.concatenate([p.reshape(-1) for p in pieces])
    got = lax.ppermute(flat, axes, [(i, i ^ shift) for i in range(n)])
    out, at = [], 0
    for p in pieces:
        rows = p.size // 128 if dense else p.size
        out.append(got[at : at + rows].reshape(p.shape))
        at += rows
    return out


def linear_index(axes):
    idx = 0
    for a in axes:
        idx = idx * lax.axis_size(a) + lax.axis_index(a)
    return idx


def shards(flow_field, test_streams, snapshot_ids):
    highest = lax.Precision.HIGHEST
    f32 = jnp.float32
    bf16 = jnp.bfloat16
    batches, local_snaps, variables, cells_x, cells_y, cells_z = flow_field.shape
    n_gx = lax.axis_size("gx")
    n_gz = lax.axis_size("gz")
    n_vert = lax.axis_size("vert")
    total_x = cells_x * n_gx
    total_z = cells_z * n_gz
    total_q = variables * batches * local_snaps * n_vert
    factor_stream = test_streams[0]
    core_stream = test_streams[1]
    gx_me = lax.axis_index("gx")
    rank_ids = jnp.arange(K, dtype=jnp.int32)
    sketch_ids = jnp.arange(S, dtype=jnp.int32)
    x_ids = gx_me * cells_x + jnp.arange(cells_x, dtype=jnp.int32)
    y_ids = jnp.arange(cells_y, dtype=jnp.int32)
    z_ids = lax.axis_index("gz") * cells_z + jnp.arange(cells_z, dtype=jnp.int32)
    q_ids = (
        snapshot_ids[:, :, None] * variables + jnp.arange(variables, dtype=jnp.int32)[None, None, :]
    ).reshape(-1)
    ax = test_table(x_ids, rank_ids, K, factor_stream, 1).astype(f32)
    ay = test_table(y_ids, rank_ids, K, factor_stream, 2)
    az = test_table(z_ids, rank_ids, K, factor_stream, 3)
    aq = test_table(q_ids, rank_ids, K, factor_stream, 4).astype(f32)
    phy = test_table(sketch_ids, y_ids, cells_y, core_stream, 6).astype(f32)
    phz = test_table(sketch_ids, z_ids, total_z, core_stream, 7)
    phq = test_table(q_ids, jnp.arange(E, dtype=jnp.int32), E, core_stream, 8).astype(f32)

    n_q = batches * local_snaps * variables
    field = flow_field.reshape(n_q, cells_x, cells_y, cells_z)

    qz = aq[:, None, :] * az.astype(f32)[None, :, :]
    qz_core = (phq[:, None, :, None] * phz.T.astype(f32)[None, :, None, :]).reshape(n_q, cells_z, E * S)
    tab = jnp.concatenate([qz, qz_core], axis=-1)
    tab_hi = tab.astype(bf16)
    tab_lo = (tab - tab_hi.astype(f32)).astype(bf16)
    width = K + E * S
    both = jnp.einsum(
        "qxyz,qzk->xyk", field, jnp.concatenate([tab_hi, tab_lo], axis=-1), preferred_element_type=f32
    )
    summed = both[..., :width] + both[..., width:]
    by_q = summed[..., :K]
    by_e = summed[..., K:].reshape(cells_x, cells_y, E, S)
    part_y = jnp.sum(by_q * ax[:, None, :], axis=0)
    part_x = jnp.sum(by_q * ay.astype(f32)[None, :, :], axis=1)
    along_y = jnp.einsum("qxyz,yk->qxzk", field, ay, preferred_element_type=f32)
    weights = aq[:, None, :] * ax[None, :, :]
    part_z = jnp.sum(along_y * weights[:, :, None, :], axis=(0, 1))
    part_core = jnp.einsum("my,xyen->xemn", phy, by_e, precision=highest)

    rows_each = cells_y // (n_gx * n_gz * n_vert)
    cols_each = K // (n_gx * n_vert)
    core_rows = S * S // n_gx
    n_gzv = n_gz * n_vert
    sy = part_y.reshape(n_gx, n_gzv, rows_each, K)
    sz = part_z.T.reshape(n_gx, n_vert, cols_each, cells_z)
    sx = part_x
    core = (
        part_core.reshape(cells_x, E, n_gx, core_rows)
        .transpose(2, 0, 1, 3)
        .reshape(1, n_gx, cells_x * E * core_rows)
    )

    v_me = lax.axis_index("vert")
    merge_sz = n_vert == 2
    for d, r in ([] if merge_sz else digit_steps(n_vert)):
        digit = (v_me // d) % r
        at = split_digit(sz, 1, r, digit)
        total = at(0)
        for s in range(1, r):
            (got,) = send_to("vert", n_vert, s * d, [at(s)])
            total = total + got
        sz = total
    gzv_me = linear_index(("gz", "vert"))
    for d, r in digit_steps(n_gzv):
        digit = (gzv_me // d) % r
        at = split_digit(sy, 1, r, digit)
        sy_total, sx_total, core_total = at(0), sx, core
        with_sz = merge_sz and d == 1
        if with_sz:
            at_z = split_digit(sz, 1, 2, v_me)
            sz_total = at_z(0)
        for s in range(1, r):
            pieces = [at(s), sx, core] + ([at_z(1)] if with_sz and s == 1 else [])
            got = send_to(("gz", "vert"), n_gzv, s * d, pieces)
            sy_total, sx_total, core_total = sy_total + got[0], sx_total + got[1], core_total + got[2]
            if with_sz and s == 1:
                sz_total = sz_total + got[3]
        sy, sx, core = sy_total, sx_total, core_total
        if with_sz:
            sz = sz_total
    for d, r in digit_steps(n_gx):
        digit = (gx_me // d) % r
        at_y = split_digit(sy, 0, r, digit)
        at_z = split_digit(sz, 0, r, digit)
        at_c = split_digit(core, 1, r, digit)
        sy_total, sz_total, core_parts = at_y(0), at_z(0), [at_c(0)]
        for s in range(1, r):
            g_sy, g_sz, g_core = send_to("gx", n_gx, s * d, [at_y(s), at_z(s), at_c(s)])
            sy_total, sz_total = sy_total + g_sy, sz_total + g_sz
            core_parts.append(g_core)
        sy, sz = sy_total, sz_total
        core = jnp.concatenate(core_parts, axis=0)

    src = jnp.bitwise_xor(gx_me, jnp.arange(n_gx, dtype=jnp.int32))
    x_src = (src[:, None] * cells_x + jnp.arange(cells_x, dtype=jnp.int32)[None, :]).reshape(-1)
    phx = test_table(sketch_ids, x_src, total_x, core_stream, 5).astype(f32).reshape(S, n_gx, cells_x)
    held = core.reshape(n_gx * cells_x, E, core_rows)
    weights_x = phx.reshape(S, n_gx * cells_x)
    core_out = jnp.sum(held[:, None, :, :] * weights_x.T[:, :, None, None], axis=0).transpose(2, 1, 0)

    scale_x = 3.0**1.5 / math.sqrt(cells_y * total_z * total_q)
    scale_y = 3.0**1.5 / math.sqrt(total_x * total_z * total_q)
    scale_z = 3.0**1.5 / math.sqrt(total_x * cells_y * total_q)
    scale_core = 9.0 / math.sqrt(total_x * cells_y * total_z * total_q)
    return (
        sx * scale_x,
        sy.reshape(rows_each, K) * scale_y,
        sz.reshape(cols_each, cells_z).T * scale_z,
        core_out * scale_core,
    )


def solution(mesh):
    in_specs = (P("groups", "vert", None, "gx", None, "gz"), P("groups"), P("groups", "vert"))
    out_specs = (
        P(("groups", "gx"), None),
        P(("groups", "gx", "gz", "vert"), None),
        P(("groups", "gz"), ("gx", "vert")),
        P(("groups", "gx"), None, None),
    )
    return jax.shard_map(shards, mesh=mesh, in_specs=in_specs, out_specs=out_specs, check_vma=False)
```

```python
import math

import jax
import jax.numpy as jnp
from jax import lax
from jax.sharding import PartitionSpec as P

K = 128
S = 48
E = 2


def mix_bits(mixed):
    mixed = jnp.bitwise_xor(mixed, lax.shift_right_logical(mixed, jnp.int32(16)))
    mixed = mixed * 739982445
    mixed = jnp.bitwise_xor(mixed, lax.shift_right_logical(mixed, jnp.int32(13)))
    mixed = mixed * 695872825
    return jnp.bitwise_xor(mixed, lax.shift_right_logical(mixed, jnp.int32(16)))


def test_table(row_ids, col_ids, stride, stream, salt):
    row_term = (row_ids * stride) * -1640531535
    col_term = col_ids * -1640531535 + stream * -2048144777 + salt
    upper = lax.shift_right_logical(mix_bits(row_term[:, None] + col_term[None, :]), jnp.int32(9))
    return ((2 * upper + 1).astype(jnp.float32) * 2.0 ** (-24) - 1.0).astype(jnp.bfloat16)


def digit_steps(n):
    d, out = 1, []
    while d < n:
        r = 4 if n // d >= 4 else 2
        out.append((d, r))
        d *= r
    return out


def split_digit(arr, dim, r, digit):
    shape = arr.shape
    split = arr.reshape(shape[:dim] + (shape[dim] // r, r) + shape[dim + 1 :])

    def at(s):
        return lax.dynamic_index_in_dim(split, jnp.bitwise_xor(digit, s), dim + 1, keepdims=False)

    return at


def send_to(axes, n, shift, pieces):
    dense = all(p.size % 128 == 0 for p in pieces)
    if dense:
        flat = jnp.concatenate([p.reshape(-1, 128) for p in pieces], axis=0)
    else:
        flat = jnp.concatenate([p.reshape(-1) for p in pieces])
    got = lax.ppermute(flat, axes, [(i, i ^ shift) for i in range(n)])
    out, at = [], 0
    for p in pieces:
        rows = p.size // 128 if dense else p.size
        out.append(got[at : at + rows].reshape(p.shape))
        at += rows
    return out


def linear_index(axes):
    idx = 0
    for a in axes:
        idx = idx * lax.axis_size(a) + lax.axis_index(a)
    return idx


def shards(flow_field, test_streams, snapshot_ids):
    highest = lax.Precision.HIGHEST
    f32 = jnp.float32
    bf16 = jnp.bfloat16
    batches, local_snaps, variables, cells_x, cells_y, cells_z = flow_field.shape
    n_gx = lax.axis_size("gx")
    n_gz = lax.axis_size("gz")
    n_vert = lax.axis_size("vert")
    total_x = cells_x * n_gx
    total_z = cells_z * n_gz
    total_q = variables * batches * local_snaps * n_vert
    factor_stream = test_streams[0]
    core_stream = test_streams[1]
    gx_me = lax.axis_index("gx")
    rank_ids = jnp.arange(K, dtype=jnp.int32)
    sketch_ids = jnp.arange(S, dtype=jnp.int32)
    x_ids = gx_me * cells_x + jnp.arange(cells_x, dtype=jnp.int32)
    y_ids = jnp.arange(cells_y, dtype=jnp.int32)
    z_ids = lax.axis_index("gz") * cells_z + jnp.arange(cells_z, dtype=jnp.int32)
    q_ids = (
        snapshot_ids[:, :, None] * variables + jnp.arange(variables, dtype=jnp.int32)[None, None, :]
    ).reshape(-1)
    n_q = batches * local_snaps * variables
    field, q_ids = lax.optimization_barrier((flow_field.reshape(n_q, cells_x, cells_y, cells_z), q_ids))
    ax = test_table(x_ids, rank_ids, K, factor_stream, 1).astype(f32)
    ay = test_table(y_ids, rank_ids, K, factor_stream, 2)
    az = test_table(z_ids, rank_ids, K, factor_stream, 3)
    aq = test_table(q_ids, rank_ids, K, factor_stream, 4).astype(f32)
    phy = test_table(sketch_ids, y_ids, cells_y, core_stream, 6).astype(f32)
    phz = test_table(sketch_ids, z_ids, total_z, core_stream, 7)
    phq = test_table(q_ids, jnp.arange(E, dtype=jnp.int32), E, core_stream, 8).astype(f32)

    rows_z = field.reshape(-1, cells_z)

    qz = aq[:, None, :] * az.astype(f32)[None, :, :]
    qz_hi = qz.astype(bf16)
    qz_lo = (qz - qz_hi.astype(f32)).astype(bf16)
    both = jnp.einsum(
        "qxyz,qzk->xyk", field, jnp.concatenate([qz_hi, qz_lo], axis=-1), preferred_element_type=f32
    )
    by_q = both[..., :K] + both[..., K:]
    part_y = jnp.sum(by_q * ax[:, None, :], axis=0)
    part_x = jnp.sum(by_q * ay.astype(f32)[None, :, :], axis=1)
    along_y = jnp.einsum("qxyz,yk->qxzk", field, ay, preferred_element_type=f32)
    weights = aq[:, None, :] * ax[None, :, :]
    part_z = jnp.sum(along_y * weights[:, :, None, :], axis=(0, 1))
    first = jnp.dot(rows_z, phz.T, preferred_element_type=f32).reshape(n_q, cells_x, cells_y, S)
    by_e = jnp.einsum("qxyn,qe->xeyn", first, phq, precision=highest)
    part_core = jnp.einsum("my,xeyn->xemn", phy, by_e, precision=highest)

    rows_each = cells_y // (n_gx * n_gz * n_vert)
    cols_each = K // (n_gx * n_vert)
    core_rows = S * S // n_gx
    n_gzv = n_gz * n_vert
    sy = part_y.reshape(n_gx, n_gzv, rows_each, K)
    sz = part_z.T.reshape(n_gx, n_vert, cols_each, cells_z)
    sx = part_x
    core = (
        part_core.reshape(cells_x, E, n_gx, core_rows)
        .transpose(2, 0, 1, 3)
        .reshape(1, n_gx, cells_x * E * core_rows)
    )

    v_me = lax.axis_index("vert")
    merge_sz = n_vert == 2
    for d, r in ([] if merge_sz else digit_steps(n_vert)):
        digit = (v_me // d) % r
        at = split_digit(sz, 1, r, digit)
        total = at(0)
        for s in range(1, r):
            (got,) = send_to("vert", n_vert, s * d, [at(s)])
            total = total + got
        sz = total
    gzv_me = linear_index(("gz", "vert"))
    for d, r in digit_steps(n_gzv):
        digit = (gzv_me // d) % r
        at = split_digit(sy, 1, r, digit)
        sy_total, sx_total, core_total = at(0), sx, core
        with_sz = merge_sz and d == 1
        if with_sz:
            at_z = split_digit(sz, 1, 2, v_me)
            sz_total = at_z(0)
        for s in range(1, r):
            pieces = [at(s), sx, core] + ([at_z(1)] if with_sz and s == 1 else [])
            got = send_to(("gz", "vert"), n_gzv, s * d, pieces)
            sy_total, sx_total, core_total = sy_total + got[0], sx_total + got[1], core_total + got[2]
            if with_sz and s == 1:
                sz_total = sz_total + got[3]
        sy, sx, core = sy_total, sx_total, core_total
        if with_sz:
            sz = sz_total
    for d, r in digit_steps(n_gx):
        digit = (gx_me // d) % r
        at_y = split_digit(sy, 0, r, digit)
        at_z = split_digit(sz, 0, r, digit)
        at_c = split_digit(core, 1, r, digit)
        sy_total, sz_total, core_parts = at_y(0), at_z(0), [at_c(0)]
        for s in range(1, r):
            g_sy, g_sz, g_core = send_to("gx", n_gx, s * d, [at_y(s), at_z(s), at_c(s)])
            sy_total, sz_total = sy_total + g_sy, sz_total + g_sz
            core_parts.append(g_core)
        sy, sz = sy_total, sz_total
        core = jnp.concatenate(core_parts, axis=0)

    src = jnp.bitwise_xor(gx_me, jnp.arange(n_gx, dtype=jnp.int32))
    x_src = (src[:, None] * cells_x + jnp.arange(cells_x, dtype=jnp.int32)[None, :]).reshape(-1)
    phx = test_table(sketch_ids, x_src, total_x, core_stream, 5).astype(f32).reshape(S, n_gx, cells_x)
    held = core.reshape(n_gx * cells_x, E, core_rows)
    weights_x = phx.reshape(S, n_gx * cells_x)
    core_out = jnp.sum(held[:, None, :, :] * weights_x.T[:, :, None, None], axis=0).transpose(2, 1, 0)

    scale_x = 3.0**1.5 / math.sqrt(cells_y * total_z * total_q)
    scale_y = 3.0**1.5 / math.sqrt(total_x * total_z * total_q)
    scale_z = 3.0**1.5 / math.sqrt(total_x * cells_y * total_q)
    scale_core = 9.0 / math.sqrt(total_x * cells_y * total_z * total_q)
    return (
        sx * scale_x,
        sy.reshape(rows_each, K) * scale_y,
        sz.reshape(cols_each, cells_z).T * scale_z,
        core_out * scale_core,
    )


def solution(mesh):
    in_specs = (P("groups", "vert", None, "gx", None, "gz"), P("groups"), P("groups", "vert"))
    out_specs = (
        P(("groups", "gx"), None),
        P(("groups", "gx", "gz", "vert"), None),
        P(("groups", "gz"), ("gx", "vert")),
        P(("groups", "gx"), None, None),
    )
    return jax.shard_map(shards, mesh=mesh, in_specs=in_specs, out_specs=out_specs, check_vma=False)
```

```python
import math

import jax
import jax.numpy as jnp
from jax import lax
from jax.sharding import PartitionSpec as P

K = 128
S = 48
E = 2


def mix_bits(mixed):
    mixed = jnp.bitwise_xor(mixed, lax.shift_right_logical(mixed, jnp.int32(16)))
    mixed = mixed * 739982445
    mixed = jnp.bitwise_xor(mixed, lax.shift_right_logical(mixed, jnp.int32(13)))
    mixed = mixed * 695872825
    return jnp.bitwise_xor(mixed, lax.shift_right_logical(mixed, jnp.int32(16)))


def test_table(row_ids, col_ids, stride, stream, salt):
    row_term = (row_ids * stride) * -1640531535
    col_term = col_ids * -1640531535 + stream * -2048144777 + salt
    upper = lax.shift_right_logical(mix_bits(row_term[:, None] + col_term[None, :]), jnp.int32(9))
    return ((2 * upper + 1).astype(jnp.float32) * 2.0 ** (-24) - 1.0).astype(jnp.bfloat16)


def digit_steps(n):
    d, out = 1, []
    while d < n:
        r = 4 if n // d >= 4 else 2
        out.append((d, r))
        d *= r
    return out


def split_digit(arr, dim, r, digit):
    shape = arr.shape
    split = arr.reshape(shape[:dim] + (shape[dim] // r, r) + shape[dim + 1 :])

    def at(s):
        return lax.dynamic_index_in_dim(split, jnp.bitwise_xor(digit, s), dim + 1, keepdims=False)

    return at


def send_to(axes, n, shift, pieces):
    dense = all(p.size % 128 == 0 for p in pieces)
    if dense:
        flat = jnp.concatenate([p.reshape(-1, 128) for p in pieces], axis=0)
    else:
        flat = jnp.concatenate([p.reshape(-1) for p in pieces])
    got = lax.ppermute(flat, axes, [(i, i ^ shift) for i in range(n)])
    out, at = [], 0
    for p in pieces:
        rows = p.size // 128 if dense else p.size
        out.append(got[at : at + rows].reshape(p.shape))
        at += rows
    return out


def linear_index(axes):
    idx = 0
    for a in axes:
        idx = idx * lax.axis_size(a) + lax.axis_index(a)
    return idx


def shards(flow_field, test_streams, snapshot_ids):
    highest = lax.Precision.HIGHEST
    f32 = jnp.float32
    bf16 = jnp.bfloat16
    batches, local_snaps, variables, cells_x, cells_y, cells_z = flow_field.shape
    n_gx = lax.axis_size("gx")
    n_gz = lax.axis_size("gz")
    n_vert = lax.axis_size("vert")
    total_x = cells_x * n_gx
    total_z = cells_z * n_gz
    total_q = variables * batches * local_snaps * n_vert
    factor_stream = test_streams[0]
    core_stream = test_streams[1]
    gx_me = lax.axis_index("gx")
    rank_ids = jnp.arange(K, dtype=jnp.int32)
    sketch_ids = jnp.arange(S, dtype=jnp.int32)
    x_ids = gx_me * cells_x + jnp.arange(cells_x, dtype=jnp.int32)
    y_ids = jnp.arange(cells_y, dtype=jnp.int32)
    z_ids = lax.axis_index("gz") * cells_z + jnp.arange(cells_z, dtype=jnp.int32)
    q_ids = (
        snapshot_ids[:, :, None] * variables + jnp.arange(variables, dtype=jnp.int32)[None, None, :]
    ).reshape(-1)
    ax = test_table(x_ids, rank_ids, K, factor_stream, 1).astype(f32)
    ay = test_table(y_ids, rank_ids, K, factor_stream, 2)
    az = test_table(z_ids, rank_ids, K, factor_stream, 3)
    aq = test_table(q_ids, rank_ids, K, factor_stream, 4).astype(f32)
    phy = test_table(sketch_ids, y_ids, cells_y, core_stream, 6).astype(f32)
    phz = test_table(sketch_ids, z_ids, total_z, core_stream, 7)
    phq = test_table(q_ids, jnp.arange(E, dtype=jnp.int32), E, core_stream, 8).astype(f32)

    n_q = batches * local_snaps * variables
    field = flow_field.reshape(n_q, cells_x, cells_y, cells_z)
    rows_z = field.reshape(-1, cells_z)

    qz = aq[:, None, :] * az.astype(f32)[None, :, :]
    qz_hi = qz.astype(bf16)
    qz_lo = (qz - qz_hi.astype(f32)).astype(bf16)
    both = jnp.einsum(
        "qxyz,qzk->xyk", field, jnp.concatenate([qz_hi, qz_lo], axis=-1), preferred_element_type=f32
    )
    by_q = both[..., :K] + both[..., K:]
    part_y = jnp.sum(by_q * ax[:, None, :], axis=0)
    part_x = jnp.sum(by_q * ay.astype(f32)[None, :, :], axis=1)
    along_y = jnp.einsum("qxyz,yk->qxzk", field, ay, preferred_element_type=f32)
    weights = aq[:, None, :] * ax[None, :, :]
    part_z = jnp.sum(along_y * weights[:, :, None, :], axis=(0, 1))
    first = jnp.dot(rows_z, phz.T, preferred_element_type=f32).reshape(n_q, cells_x, cells_y, S)
    by_e = jnp.einsum("qxyn,qe->xeyn", first, phq, precision=highest)
    part_core = jnp.einsum("my,xeyn->xemn", phy, by_e, precision=highest)

    scale_x = 3.0**1.5 / math.sqrt(cells_y * total_z * total_q)
    scale_y = 3.0**1.5 / math.sqrt(total_x * total_z * total_q)
    scale_z = 3.0**1.5 / math.sqrt(total_x * cells_y * total_q)
    scale_core = 9.0 / math.sqrt(total_x * cells_y * total_z * total_q)
    rows_each = cells_y // (n_gx * n_gz * n_vert)
    cols_each = K // (n_gx * n_vert)
    core_rows = S * S // n_gx
    n_gzv = n_gz * n_vert
    sy = (part_y * scale_y).reshape(n_gx, n_gzv, rows_each, K)
    sz = (part_z * scale_z).T.reshape(n_gx, n_vert, cols_each, cells_z)
    sx = part_x * scale_x
    core = (
        part_core.reshape(cells_x, E, n_gx, core_rows)
        .transpose(2, 0, 1, 3)
        .reshape(1, n_gx, cells_x * E * core_rows)
    )

    v_me = lax.axis_index("vert")
    merge_sz = n_vert == 2
    for d, r in ([] if merge_sz else digit_steps(n_vert)):
        digit = (v_me // d) % r
        at = split_digit(sz, 1, r, digit)
        total = at(0)
        for s in range(1, r):
            (got,) = send_to("vert", n_vert, s * d, [at(s)])
            total = total + got
        sz = total
    gzv_me = linear_index(("gz", "vert"))
    for d, r in digit_steps(n_gzv):
        digit = (gzv_me // d) % r
        at = split_digit(sy, 1, r, digit)
        sy_total, sx_total, core_total = at(0), sx, core
        with_sz = merge_sz and d == 1
        if with_sz:
            at_z = split_digit(sz, 1, 2, v_me)
            sz_total = at_z(0)
        for s in range(1, r):
            pieces = [at(s), sx, core] + ([at_z(1)] if with_sz and s == 1 else [])
            got = send_to(("gz", "vert"), n_gzv, s * d, pieces)
            sy_total, sx_total, core_total = sy_total + got[0], sx_total + got[1], core_total + got[2]
            if with_sz and s == 1:
                sz_total = sz_total + got[3]
        sy, sx, core = sy_total, sx_total, core_total
        if with_sz:
            sz = sz_total
    for d, r in digit_steps(n_gx):
        digit = (gx_me // d) % r
        at_y = split_digit(sy, 0, r, digit)
        at_z = split_digit(sz, 0, r, digit)
        at_c = split_digit(core, 1, r, digit)
        sy_total, sz_total, core_parts = at_y(0), at_z(0), [at_c(0)]
        for s in range(1, r):
            g_sy, g_sz, g_core = send_to("gx", n_gx, s * d, [at_y(s), at_z(s), at_c(s)])
            sy_total, sz_total = sy_total + g_sy, sz_total + g_sz
            core_parts.append(g_core)
        sy, sz = sy_total, sz_total
        core = jnp.concatenate(core_parts, axis=0)

    src = jnp.bitwise_xor(gx_me, jnp.arange(n_gx, dtype=jnp.int32))
    x_src = (src[:, None] * cells_x + jnp.arange(cells_x, dtype=jnp.int32)[None, :]).reshape(-1)
    phx = test_table(sketch_ids, x_src, total_x, core_stream, 5).astype(f32).reshape(S, n_gx, cells_x)
    held = core.reshape(n_gx * cells_x, E, core_rows)
    weights_x = phx.reshape(S, n_gx * cells_x) * scale_core
    core_out = jnp.sum(held[:, None, :, :] * weights_x.T[:, :, None, None], axis=0).transpose(2, 1, 0)

    return (
        sx,
        sy.reshape(rows_each, K),
        sz.reshape(cols_each, cells_z).T,
        core_out,
    )


def solution(mesh):
    in_specs = (P("groups", "vert", None, "gx", None, "gz"), P("groups"), P("groups", "vert"))
    out_specs = (
        P(("groups", "gx"), None),
        P(("groups", "gx", "gz", "vert"), None),
        P(("groups", "gz"), ("gx", "vert")),
        P(("groups", "gx"), None, None),
    )
    return jax.shard_map(shards, mesh=mesh, in_specs=in_specs, out_specs=out_specs, check_vma=False)
```

```python
import math

import jax
import jax.numpy as jnp
from jax import lax
from jax.sharding import PartitionSpec as P

K = 128
S = 48
E = 2


def mix_bits(mixed):
    mixed = jnp.bitwise_xor(mixed, lax.shift_right_logical(mixed, jnp.int32(16)))
    mixed = mixed * 739982445
    mixed = jnp.bitwise_xor(mixed, lax.shift_right_logical(mixed, jnp.int32(13)))
    mixed = mixed * 695872825
    return jnp.bitwise_xor(mixed, lax.shift_right_logical(mixed, jnp.int32(16)))


def test_table(row_ids, col_ids, stride, stream, salt):
    row_term = (row_ids * stride) * -1640531535
    col_term = col_ids * -1640531535 + stream * -2048144777 + salt
    upper = lax.shift_right_logical(mix_bits(row_term[:, None] + col_term[None, :]), jnp.int32(9))
    return ((2 * upper + 1).astype(jnp.float32) * 2.0 ** (-24) - 1.0).astype(jnp.bfloat16)


def digit_steps(n):
    d, out = 1, []
    while d < n:
        r = 4 if n // d >= 4 else 2
        out.append((d, r))
        d *= r
    return out


def split_digit(arr, dim, r, digit):
    shape = arr.shape
    split = arr.reshape(shape[:dim] + (shape[dim] // r, r) + shape[dim + 1 :])

    def at(s):
        return lax.dynamic_index_in_dim(split, jnp.bitwise_xor(digit, s), dim + 1, keepdims=False)

    return at


def send_to(axes, n, shift, pieces):
    dense = all(p.size % 128 == 0 for p in pieces)
    if dense:
        flat = jnp.concatenate([p.reshape(-1, 128) for p in pieces], axis=0)
    else:
        flat = jnp.concatenate([p.reshape(-1) for p in pieces])
    got = lax.ppermute(flat, axes, [(i, i ^ shift) for i in range(n)])
    out, at = [], 0
    for p in pieces:
        rows = p.size // 128 if dense else p.size
        out.append(got[at : at + rows].reshape(p.shape))
        at += rows
    return out


def linear_index(axes):
    idx = 0
    for a in axes:
        idx = idx * lax.axis_size(a) + lax.axis_index(a)
    return idx


def shards(flow_field, test_streams, snapshot_ids):
    highest = lax.Precision.HIGHEST
    f32 = jnp.float32
    bf16 = jnp.bfloat16
    batches, local_snaps, variables, cells_x, cells_y, cells_z = flow_field.shape
    n_gx = lax.axis_size("gx")
    n_gz = lax.axis_size("gz")
    n_vert = lax.axis_size("vert")
    total_x = cells_x * n_gx
    total_z = cells_z * n_gz
    total_q = variables * batches * local_snaps * n_vert
    factor_stream = test_streams[0]
    core_stream = test_streams[1]
    gx_me = lax.axis_index("gx")
    rank_ids = jnp.arange(K, dtype=jnp.int32)
    sketch_ids = jnp.arange(S, dtype=jnp.int32)
    x_ids = gx_me * cells_x + jnp.arange(cells_x, dtype=jnp.int32)
    y_ids = jnp.arange(cells_y, dtype=jnp.int32)
    z_ids = lax.axis_index("gz") * cells_z + jnp.arange(cells_z, dtype=jnp.int32)
    q_ids = (
        snapshot_ids[:, :, None] * variables + jnp.arange(variables, dtype=jnp.int32)[None, None, :]
    ).reshape(-1)
    ax = test_table(x_ids, rank_ids, K, factor_stream, 1).astype(f32)
    ay = test_table(y_ids, rank_ids, K, factor_stream, 2)
    az = test_table(z_ids, rank_ids, K, factor_stream, 3)
    aq = test_table(q_ids, rank_ids, K, factor_stream, 4).astype(f32)
    phy = test_table(sketch_ids, y_ids, cells_y, core_stream, 6).astype(f32)
    phz = test_table(sketch_ids, z_ids, total_z, core_stream, 7)
    phq = test_table(q_ids, jnp.arange(E, dtype=jnp.int32), E, core_stream, 8).astype(f32)

    n_q = batches * local_snaps * variables
    field = flow_field.reshape(n_q, cells_x, cells_y, cells_z)
    rows_z = field.reshape(-1, cells_z)

    qz = aq[:, None, :] * az.astype(f32)[None, :, :]
    qz_hi = qz.astype(bf16)
    qz_lo = (qz - qz_hi.astype(f32)).astype(bf16)
    both = jnp.einsum(
        "qxyz,qzk->xyk", field, jnp.concatenate([qz_hi, qz_lo], axis=-1), preferred_element_type=f32
    )
    by_q = both[..., :K] + both[..., K:]
    part_y = jnp.sum(by_q * ax[:, None, :], axis=0)
    part_x = jnp.sum(by_q * ay.astype(f32)[None, :, :], axis=1)
    along_y = jnp.einsum("qxyz,yk->qxzk", field, ay, preferred_element_type=f32)
    weights = aq[:, None, :] * ax[None, :, :]
    part_z = jnp.sum(along_y * weights[:, :, None, :], axis=(0, 1))
    first = jnp.dot(rows_z, phz.T, preferred_element_type=f32).reshape(n_q, cells_x, cells_y, S)
    high = lax.Precision.HIGH
    by_e = jnp.einsum("qxyn,qe->xeyn", first, phq, precision=high)
    part_core = jnp.einsum("my,xeyn->xemn", phy, by_e, precision=high)

    rows_each = cells_y // (n_gx * n_gz * n_vert)
    cols_each = K // (n_gx * n_vert)
    core_rows = S * S // n_gx
    n_gzv = n_gz * n_vert
    sy = part_y.reshape(n_gx, n_gzv, rows_each, K)
    sz = part_z.T.reshape(n_gx, n_vert, cols_each, cells_z)
    sx = part_x
    core = (
        part_core.reshape(cells_x, E, n_gx, core_rows)
        .transpose(2, 0, 1, 3)
        .reshape(1, n_gx, cells_x * E * core_rows)
    )

    v_me = lax.axis_index("vert")
    merge_sz = n_vert == 2
    for d, r in ([] if merge_sz else digit_steps(n_vert)):
        digit = (v_me // d) % r
        at = split_digit(sz, 1, r, digit)
        total = at(0)
        for s in range(1, r):
            (got,) = send_to("vert", n_vert, s * d, [at(s)])
            total = total + got
        sz = total
    gzv_me = linear_index(("gz", "vert"))
    for d, r in digit_steps(n_gzv):
        digit = (gzv_me // d) % r
        at = split_digit(sy, 1, r, digit)
        sy_total, sx_total, core_total = at(0), sx, core
        with_sz = merge_sz and d == 1
        if with_sz:
            at_z = split_digit(sz, 1, 2, v_me)
            sz_total = at_z(0)
        for s in range(1, r):
            pieces = [at(s), sx, core] + ([at_z(1)] if with_sz and s == 1 else [])
            got = send_to(("gz", "vert"), n_gzv, s * d, pieces)
            sy_total, sx_total, core_total = sy_total + got[0], sx_total + got[1], core_total + got[2]
            if with_sz and s == 1:
                sz_total = sz_total + got[3]
        sy, sx, core = sy_total, sx_total, core_total
        if with_sz:
            sz = sz_total
    for d, r in digit_steps(n_gx):
        digit = (gx_me // d) % r
        at_y = split_digit(sy, 0, r, digit)
        at_z = split_digit(sz, 0, r, digit)
        at_c = split_digit(core, 1, r, digit)
        sy_total, sz_total, core_parts = at_y(0), at_z(0), [at_c(0)]
        for s in range(1, r):
            g_sy, g_sz, g_core = send_to("gx", n_gx, s * d, [at_y(s), at_z(s), at_c(s)])
            sy_total, sz_total = sy_total + g_sy, sz_total + g_sz
            core_parts.append(g_core)
        sy, sz = sy_total, sz_total
        core = jnp.concatenate(core_parts, axis=0)

    src = jnp.bitwise_xor(gx_me, jnp.arange(n_gx, dtype=jnp.int32))
    x_src = (src[:, None] * cells_x + jnp.arange(cells_x, dtype=jnp.int32)[None, :]).reshape(-1)
    phx = test_table(sketch_ids, x_src, total_x, core_stream, 5).astype(f32).reshape(S, n_gx, cells_x)
    held = core.reshape(n_gx * cells_x, E, core_rows)
    weights_x = phx.reshape(S, n_gx * cells_x)
    core_out = jnp.sum(held[:, None, :, :] * weights_x.T[:, :, None, None], axis=0).transpose(2, 1, 0)

    scale_x = 3.0**1.5 / math.sqrt(cells_y * total_z * total_q)
    scale_y = 3.0**1.5 / math.sqrt(total_x * total_z * total_q)
    scale_z = 3.0**1.5 / math.sqrt(total_x * cells_y * total_q)
    scale_core = 9.0 / math.sqrt(total_x * cells_y * total_z * total_q)
    return (
        sx * scale_x,
        sy.reshape(rows_each, K) * scale_y,
        sz.reshape(cols_each, cells_z).T * scale_z,
        core_out * scale_core,
    )


def solution(mesh):
    in_specs = (P("groups", "vert", None, "gx", None, "gz"), P("groups"), P("groups", "vert"))
    out_specs = (
        P(("groups", "gx"), None),
        P(("groups", "gx", "gz", "vert"), None),
        P(("groups", "gz"), ("gx", "vert")),
        P(("groups", "gx"), None, None),
    )
    return jax.shard_map(shards, mesh=mesh, in_specs=in_specs, out_specs=out_specs, check_vma=False)
```

```python
import math

import jax
import jax.numpy as jnp
from jax import lax
from jax.sharding import PartitionSpec as P

K = 128
S = 48
E = 2


def mix_bits(mixed):
    mixed = jnp.bitwise_xor(mixed, lax.shift_right_logical(mixed, jnp.int32(16)))
    mixed = mixed * 739982445
    mixed = jnp.bitwise_xor(mixed, lax.shift_right_logical(mixed, jnp.int32(13)))
    mixed = mixed * 695872825
    return jnp.bitwise_xor(mixed, lax.shift_right_logical(mixed, jnp.int32(16)))


def unit_from_terms(row_term, col_term):
    upper = lax.shift_right_logical(mix_bits(row_term[:, None] + col_term[None, :]), jnp.int32(9))
    return ((2 * upper + 1).astype(jnp.float32) * 2.0 ** (-24) - 1.0).astype(jnp.bfloat16)


def row_terms(row_ids, stride):
    return (row_ids * stride) * -1640531535


def column_terms(test_streams, columns):
    ids = jnp.concatenate([c for c, _, _ in columns])
    which = jnp.concatenate([jnp.full(c.shape, w, jnp.int32) for c, w, _ in columns])
    salts = jnp.concatenate([jnp.full(c.shape, s, jnp.int32) for c, _, s in columns])
    streams = jnp.where(which == 1, test_streams[1], test_streams[0])
    terms = ids * -1640531535 + streams * -2048144777 + salts
    out, at = [], 0
    for c, _, _ in columns:
        out.append(terms[at : at + c.shape[0]])
        at += c.shape[0]
    return out


def digit_steps(n):
    d, out = 1, []
    while d < n:
        r = 4 if n // d >= 4 else 2
        out.append((d, r))
        d *= r
    return out


def split_digit(arr, dim, r, digit):
    shape = arr.shape
    split = arr.reshape(shape[:dim] + (shape[dim] // r, r) + shape[dim + 1 :])

    def at(s):
        return lax.dynamic_index_in_dim(split, jnp.bitwise_xor(digit, s), dim + 1, keepdims=False)

    return at


def send_to(axes, n, shift, pieces):
    dense = all(p.size % 128 == 0 for p in pieces)
    if dense:
        flat = jnp.concatenate([p.reshape(-1, 128) for p in pieces], axis=0)
    else:
        flat = jnp.concatenate([p.reshape(-1) for p in pieces])
    got = lax.ppermute(flat, axes, [(i, i ^ shift) for i in range(n)])
    out, at = [], 0
    for p in pieces:
        rows = p.size // 128 if dense else p.size
        out.append(got[at : at + rows].reshape(p.shape))
        at += rows
    return out


def linear_index(axes):
    idx = 0
    for a in axes:
        idx = idx * lax.axis_size(a) + lax.axis_index(a)
    return idx


def shards(flow_field, test_streams, snapshot_ids):
    highest = lax.Precision.HIGHEST
    f32 = jnp.float32
    bf16 = jnp.bfloat16
    batches, local_snaps, variables, cells_x, cells_y, cells_z = flow_field.shape
    n_gx = lax.axis_size("gx")
    n_gz = lax.axis_size("gz")
    n_vert = lax.axis_size("vert")
    total_x = cells_x * n_gx
    total_z = cells_z * n_gz
    total_q = variables * batches * local_snaps * n_vert
    gx_me = lax.axis_index("gx")
    rank_ids = jnp.arange(K, dtype=jnp.int32)
    sketch_ids = jnp.arange(S, dtype=jnp.int32)
    x_ids = gx_me * cells_x + jnp.arange(cells_x, dtype=jnp.int32)
    y_ids = jnp.arange(cells_y, dtype=jnp.int32)
    z_ids = lax.axis_index("gz") * cells_z + jnp.arange(cells_z, dtype=jnp.int32)
    q_ids = (
        snapshot_ids[:, :, None] * variables + jnp.arange(variables, dtype=jnp.int32)[None, None, :]
    ).reshape(-1)
    src_gx = jnp.bitwise_xor(gx_me, jnp.arange(n_gx, dtype=jnp.int32))
    x_src = (src_gx[:, None] * cells_x + jnp.arange(cells_x, dtype=jnp.int32)[None, :]).reshape(-1)
    e_ids = jnp.arange(E, dtype=jnp.int32)
    c_ax, c_ay, c_az, c_aq, c_phy, c_phz, c_phq, c_phx = column_terms(
        test_streams,
        [(rank_ids, 0, 1), (rank_ids, 0, 2), (rank_ids, 0, 3), (rank_ids, 0, 4),
         (y_ids, 1, 6), (z_ids, 1, 7), (e_ids, 1, 8), (x_src, 1, 5)],
    )
    ax = unit_from_terms(row_terms(x_ids, K), c_ax).astype(f32)
    ay = unit_from_terms(row_terms(y_ids, K), c_ay)
    az = unit_from_terms(row_terms(z_ids, K), c_az)
    aq = unit_from_terms(row_terms(q_ids, K), c_aq).astype(f32)
    phy = unit_from_terms(row_terms(sketch_ids, cells_y), c_phy).astype(f32)
    phz = unit_from_terms(row_terms(sketch_ids, total_z), c_phz)
    phq = unit_from_terms(row_terms(q_ids, E), c_phq).astype(f32)
    phx = unit_from_terms(row_terms(sketch_ids, total_x), c_phx).astype(f32).reshape(S, n_gx, cells_x)

    n_q = batches * local_snaps * variables
    field = flow_field.reshape(n_q, cells_x, cells_y, cells_z)
    rows_z = field.reshape(-1, cells_z)

    qz = aq[:, None, :] * az.astype(f32)[None, :, :]
    qz_hi = qz.astype(bf16)
    qz_lo = (qz - qz_hi.astype(f32)).astype(bf16)
    both = jnp.einsum(
        "qxyz,qzk->xyk", field, jnp.concatenate([qz_hi, qz_lo], axis=-1), preferred_element_type=f32
    )
    by_q = both[..., :K] + both[..., K:]
    part_y = jnp.sum(by_q * ax[:, None, :], axis=0)
    part_x = jnp.sum(by_q * ay.astype(f32)[None, :, :], axis=1)
    along_y = jnp.einsum("qxyz,yk->qxzk", field, ay, preferred_element_type=f32)
    weights = aq[:, None, :] * ax[None, :, :]
    part_z = jnp.sum(along_y * weights[:, :, None, :], axis=(0, 1))
    first = jnp.dot(rows_z, phz.T, preferred_element_type=f32).reshape(n_q, cells_x, cells_y, S)
    high = lax.Precision.HIGH
    by_e = jnp.einsum("qxyn,qe->xeyn", first, phq, precision=high)
    part_core = jnp.einsum("my,xeyn->xemn", phy, by_e, precision=high)

    rows_each = cells_y // (n_gx * n_gz * n_vert)
    cols_each = K // (n_gx * n_vert)
    core_rows = S * S // n_gx
    n_gzv = n_gz * n_vert
    sy = part_y.reshape(n_gx, n_gzv, rows_each, K)
    sz = part_z.T.reshape(n_gx, n_vert, cols_each, cells_z)
    sx = part_x
    core = (
        part_core.reshape(cells_x, E, n_gx, core_rows)
        .transpose(2, 0, 1, 3)
        .reshape(1, n_gx, cells_x * E * core_rows)
    )

    v_me = lax.axis_index("vert")
    merge_sz = n_vert == 2
    for d, r in ([] if merge_sz else digit_steps(n_vert)):
        digit = (v_me // d) % r
        at = split_digit(sz, 1, r, digit)
        total = at(0)
        for s in range(1, r):
            (got,) = send_to("vert", n_vert, s * d, [at(s)])
            total = total + got
        sz = total
    gzv_me = linear_index(("gz", "vert"))
    for d, r in digit_steps(n_gzv):
        digit = (gzv_me // d) % r
        at = split_digit(sy, 1, r, digit)
        sy_total, sx_total, core_total = at(0), sx, core
        with_sz = merge_sz and d == 1
        if with_sz:
            at_z = split_digit(sz, 1, 2, v_me)
            sz_total = at_z(0)
        for s in range(1, r):
            pieces = [at(s), sx, core] + ([at_z(1)] if with_sz and s == 1 else [])
            got = send_to(("gz", "vert"), n_gzv, s * d, pieces)
            sy_total, sx_total, core_total = sy_total + got[0], sx_total + got[1], core_total + got[2]
            if with_sz and s == 1:
                sz_total = sz_total + got[3]
        sy, sx, core = sy_total, sx_total, core_total
        if with_sz:
            sz = sz_total
    for d, r in digit_steps(n_gx):
        digit = (gx_me // d) % r
        at_y = split_digit(sy, 0, r, digit)
        at_z = split_digit(sz, 0, r, digit)
        at_c = split_digit(core, 1, r, digit)
        sy_total, sz_total, core_parts = at_y(0), at_z(0), [at_c(0)]
        for s in range(1, r):
            g_sy, g_sz, g_core = send_to("gx", n_gx, s * d, [at_y(s), at_z(s), at_c(s)])
            sy_total, sz_total = sy_total + g_sy, sz_total + g_sz
            core_parts.append(g_core)
        sy, sz = sy_total, sz_total
        core = jnp.concatenate(core_parts, axis=0)

    held = core.reshape(n_gx * cells_x, E, core_rows)
    weights_x = phx.reshape(S, n_gx * cells_x)
    core_out = jnp.sum(held[:, None, :, :] * weights_x.T[:, :, None, None], axis=0).transpose(2, 1, 0)

    scale_x = 3.0**1.5 / math.sqrt(cells_y * total_z * total_q)
    scale_y = 3.0**1.5 / math.sqrt(total_x * total_z * total_q)
    scale_z = 3.0**1.5 / math.sqrt(total_x * cells_y * total_q)
    scale_core = 9.0 / math.sqrt(total_x * cells_y * total_z * total_q)
    return (
        sx * scale_x,
        sy.reshape(rows_each, K) * scale_y,
        sz.reshape(cols_each, cells_z).T * scale_z,
        core_out * scale_core,
    )


def solution(mesh):
    in_specs = (P("groups", "vert", None, "gx", None, "gz"), P("groups"), P("groups", "vert"))
    out_specs = (
        P(("groups", "gx"), None),
        P(("groups", "gx", "gz", "vert"), None),
        P(("groups", "gz"), ("gx", "vert")),
        P(("groups", "gx"), None, None),
    )
    return jax.shard_map(shards, mesh=mesh, in_specs=in_specs, out_specs=out_specs, check_vma=False)
```

```python
import math

import jax
import jax.numpy as jnp
from jax import lax
from jax.sharding import PartitionSpec as P

K = 128
S = 48
E = 2


def mix_bits(mixed):
    mixed = jnp.bitwise_xor(mixed, lax.shift_right_logical(mixed, jnp.int32(16)))
    mixed = mixed * 739982445
    mixed = jnp.bitwise_xor(mixed, lax.shift_right_logical(mixed, jnp.int32(13)))
    mixed = mixed * 695872825
    return jnp.bitwise_xor(mixed, lax.shift_right_logical(mixed, jnp.int32(16)))


def test_table(row_ids, col_ids, stride, stream, salt):
    row_term = (row_ids * stride) * -1640531535
    col_term = col_ids * -1640531535
    mixed = row_term[:, None] + col_term[None, :] + (stream * -2048144777 + salt)
    upper = lax.shift_right_logical(mix_bits(mixed), jnp.int32(9))
    return ((2 * upper + 1).astype(jnp.float32) * 2.0 ** (-24) - 1.0).astype(jnp.bfloat16)


def digit_steps(n):
    d, out = 1, []
    while d < n:
        r = 4 if n // d >= 4 else 2
        out.append((d, r))
        d *= r
    return out


def split_digit(arr, dim, r, digit):
    shape = arr.shape
    split = arr.reshape(shape[:dim] + (shape[dim] // r, r) + shape[dim + 1 :])

    def at(s):
        return lax.dynamic_index_in_dim(split, jnp.bitwise_xor(digit, s), dim + 1, keepdims=False)

    return at


def send_to(axes, n, shift, pieces):
    dense = all(p.size % 128 == 0 for p in pieces)
    if dense:
        flat = jnp.concatenate([p.reshape(-1, 128) for p in pieces], axis=0)
    else:
        flat = jnp.concatenate([p.reshape(-1) for p in pieces])
    got = lax.ppermute(flat, axes, [(i, i ^ shift) for i in range(n)])
    out, at = [], 0
    for p in pieces:
        rows = p.size // 128 if dense else p.size
        out.append(got[at : at + rows].reshape(p.shape))
        at += rows
    return out


def linear_index(axes):
    idx = 0
    for a in axes:
        idx = idx * lax.axis_size(a) + lax.axis_index(a)
    return idx


def shards(flow_field, test_streams, snapshot_ids):
    highest = lax.Precision.HIGHEST
    f32 = jnp.float32
    bf16 = jnp.bfloat16
    batches, local_snaps, variables, cells_x, cells_y, cells_z = flow_field.shape
    n_gx = lax.axis_size("gx")
    n_gz = lax.axis_size("gz")
    n_vert = lax.axis_size("vert")
    total_x = cells_x * n_gx
    total_z = cells_z * n_gz
    total_q = variables * batches * local_snaps * n_vert
    factor_stream = test_streams[0]
    core_stream = test_streams[1]
    gx_me = lax.axis_index("gx")
    rank_ids = jnp.arange(K, dtype=jnp.int32)
    sketch_ids = jnp.arange(S, dtype=jnp.int32)
    x_ids = gx_me * cells_x + jnp.arange(cells_x, dtype=jnp.int32)
    y_ids = jnp.arange(cells_y, dtype=jnp.int32)
    z_ids = lax.axis_index("gz") * cells_z + jnp.arange(cells_z, dtype=jnp.int32)
    q_ids = (
        snapshot_ids[:, :, None] * variables + jnp.arange(variables, dtype=jnp.int32)[None, None, :]
    ).reshape(-1)
    ax = test_table(x_ids, rank_ids, K, factor_stream, 1).astype(f32)
    ay = test_table(y_ids, rank_ids, K, factor_stream, 2)
    az = test_table(z_ids, rank_ids, K, factor_stream, 3)
    aq = test_table(q_ids, rank_ids, K, factor_stream, 4).astype(f32)
    phy = test_table(sketch_ids, y_ids, cells_y, core_stream, 6).astype(f32)
    phz = test_table(sketch_ids, z_ids, total_z, core_stream, 7)
    phq = test_table(q_ids, jnp.arange(E, dtype=jnp.int32), E, core_stream, 8).astype(f32)

    n_q = batches * local_snaps * variables
    field = flow_field.reshape(n_q, cells_x, cells_y, cells_z)
    rows_z = field.reshape(-1, cells_z)

    qz = aq[:, None, :] * az.astype(f32)[None, :, :]
    qz_hi = qz.astype(bf16)
    qz_lo = (qz - qz_hi.astype(f32)).astype(bf16)
    both = jnp.einsum(
        "qxyz,qzk->xyk", field, jnp.concatenate([qz_hi, qz_lo], axis=-1), preferred_element_type=f32
    )
    by_q = both[..., :K] + both[..., K:]
    part_y = jnp.sum(by_q * ax[:, None, :], axis=0)
    part_x = jnp.sum(by_q * ay.astype(f32)[None, :, :], axis=1)
    along_y = jnp.einsum("qxyz,yk->qxzk", field, ay, preferred_element_type=f32)
    weights = aq[:, None, :] * ax[None, :, :]
    part_z = jnp.sum(along_y * weights[:, :, None, :], axis=(0, 1))
    first = jnp.dot(rows_z, phz.T, preferred_element_type=f32).reshape(n_q, cells_x, cells_y, S)
    high = lax.Precision.HIGH
    by_e = jnp.einsum("qxyn,qe->xeyn", first, phq, precision=high)
    part_core = jnp.einsum("my,xeyn->xemn", phy, by_e, precision=high)

    rows_each = cells_y // (n_gx * n_gz * n_vert)
    cols_each = K // (n_gx * n_vert)
    core_rows = S * S // n_gx
    n_gzv = n_gz * n_vert
    sy = part_y.reshape(n_gx, n_gzv, rows_each, K)
    sz = part_z.T.reshape(n_gx, n_vert, cols_each, cells_z)
    sx = part_x
    core = (
        part_core.reshape(cells_x, E, n_gx, core_rows)
        .transpose(2, 0, 1, 3)
        .reshape(1, n_gx, cells_x * E * core_rows)
    )

    v_me = lax.axis_index("vert")
    merge_sz = n_vert == 2
    for d, r in ([] if merge_sz else digit_steps(n_vert)):
        digit = (v_me // d) % r
        at = split_digit(sz, 1, r, digit)
        total = at(0)
        for s in range(1, r):
            (got,) = send_to("vert", n_vert, s * d, [at(s)])
            total = total + got
        sz = total
    gzv_me = linear_index(("gz", "vert"))
    for d, r in digit_steps(n_gzv):
        digit = (gzv_me // d) % r
        at = split_digit(sy, 1, r, digit)
        sy_total, sx_total, core_total = at(0), sx, core
        with_sz = merge_sz and d == 1
        if with_sz:
            at_z = split_digit(sz, 1, 2, v_me)
            sz_total = at_z(0)
        for s in range(1, r):
            pieces = [at(s), sx, core] + ([at_z(1)] if with_sz and s == 1 else [])
            got = send_to(("gz", "vert"), n_gzv, s * d, pieces)
            sy_total, sx_total, core_total = sy_total + got[0], sx_total + got[1], core_total + got[2]
            if with_sz and s == 1:
                sz_total = sz_total + got[3]
        sy, sx, core = sy_total, sx_total, core_total
        if with_sz:
            sz = sz_total
    for d, r in digit_steps(n_gx):
        digit = (gx_me // d) % r
        at_y = split_digit(sy, 0, r, digit)
        at_z = split_digit(sz, 0, r, digit)
        at_c = split_digit(core, 1, r, digit)
        sy_total, sz_total, core_parts = at_y(0), at_z(0), [at_c(0)]
        for s in range(1, r):
            g_sy, g_sz, g_core = send_to("gx", n_gx, s * d, [at_y(s), at_z(s), at_c(s)])
            sy_total, sz_total = sy_total + g_sy, sz_total + g_sz
            core_parts.append(g_core)
        sy, sz = sy_total, sz_total
        core = jnp.concatenate(core_parts, axis=0)

    src = jnp.bitwise_xor(gx_me, jnp.arange(n_gx, dtype=jnp.int32))
    x_src = (src[:, None] * cells_x + jnp.arange(cells_x, dtype=jnp.int32)[None, :]).reshape(-1)
    phx = test_table(sketch_ids, x_src, total_x, core_stream, 5).astype(f32).reshape(S, n_gx, cells_x)
    held = core.reshape(n_gx * cells_x, E, core_rows)
    weights_x = phx.reshape(S, n_gx * cells_x)
    core_out = jnp.sum(held[:, None, :, :] * weights_x.T[:, :, None, None], axis=0).transpose(2, 1, 0)

    scale_x = 3.0**1.5 / math.sqrt(cells_y * total_z * total_q)
    scale_y = 3.0**1.5 / math.sqrt(total_x * total_z * total_q)
    scale_z = 3.0**1.5 / math.sqrt(total_x * cells_y * total_q)
    scale_core = 9.0 / math.sqrt(total_x * cells_y * total_z * total_q)
    return (
        sx * scale_x,
        sy.reshape(rows_each, K) * scale_y,
        sz.reshape(cols_each, cells_z).T * scale_z,
        core_out * scale_core,
    )


def solution(mesh):
    in_specs = (P("groups", "vert", None, "gx", None, "gz"), P("groups"), P("groups", "vert"))
    out_specs = (
        P(("groups", "gx"), None),
        P(("groups", "gx", "gz", "vert"), None),
        P(("groups", "gz"), ("gx", "vert")),
        P(("groups", "gx"), None, None),
    )
    return jax.shard_map(shards, mesh=mesh, in_specs=in_specs, out_specs=out_specs, check_vma=False)
```

```python
import math

import jax
import jax.numpy as jnp
from jax import lax
from jax.sharding import PartitionSpec as P

K = 128
S = 48
E = 2


def mix_bits(mixed):
    mixed = jnp.bitwise_xor(mixed, lax.shift_right_logical(mixed, jnp.int32(16)))
    mixed = mixed * 739982445
    mixed = jnp.bitwise_xor(mixed, lax.shift_right_logical(mixed, jnp.int32(13)))
    mixed = mixed * 695872825
    return jnp.bitwise_xor(mixed, lax.shift_right_logical(mixed, jnp.int32(16)))


def test_table(row_ids, col_ids, stride, stream, salt):
    row_term = (row_ids * stride) * -1640531535
    col_term = col_ids * -1640531535
    mixed = row_term[:, None] + col_term[None, :] + (stream * -2048144777 + salt)
    upper = lax.shift_right_logical(mix_bits(mixed), jnp.int32(9))
    return ((2 * upper + 1).astype(jnp.float32) * 2.0 ** (-24) - 1.0).astype(jnp.bfloat16)


def digit_steps(n):
    d, out = 1, []
    while d < n:
        r = 4 if n // d >= 4 else 2
        out.append((d, r))
        d *= r
    return out


def split_digit(arr, dim, r, digit):
    shape = arr.shape
    split = arr.reshape(shape[:dim] + (shape[dim] // r, r) + shape[dim + 1 :])

    def at(s):
        return lax.dynamic_index_in_dim(split, jnp.bitwise_xor(digit, s), dim + 1, keepdims=False)

    return at


def send_to(axes, n, shift, pieces):
    dense = all(p.size % 128 == 0 for p in pieces)
    if dense:
        flat = jnp.concatenate([p.reshape(-1, 128) for p in pieces], axis=0)
    else:
        flat = jnp.concatenate([p.reshape(-1) for p in pieces])
    got = lax.ppermute(flat, axes, [(i, i ^ shift) for i in range(n)])
    out, at = [], 0
    for p in pieces:
        rows = p.size // 128 if dense else p.size
        out.append(got[at : at + rows].reshape(p.shape))
        at += rows
    return out


def linear_index(axes):
    idx = 0
    for a in axes:
        idx = idx * lax.axis_size(a) + lax.axis_index(a)
    return idx


def shards(flow_field, test_streams, snapshot_ids):
    highest = lax.Precision.HIGHEST
    f32 = jnp.float32
    bf16 = jnp.bfloat16
    batches, local_snaps, variables, cells_x, cells_y, cells_z = flow_field.shape
    n_gx = lax.axis_size("gx")
    n_gz = lax.axis_size("gz")
    n_vert = lax.axis_size("vert")
    total_x = cells_x * n_gx
    total_z = cells_z * n_gz
    total_q = variables * batches * local_snaps * n_vert
    factor_stream = test_streams[0]
    core_stream = test_streams[1]
    gx_me = lax.axis_index("gx")
    rank_ids = jnp.arange(K, dtype=jnp.int32)
    sketch_ids = jnp.arange(S, dtype=jnp.int32)
    x_ids = gx_me * cells_x + jnp.arange(cells_x, dtype=jnp.int32)
    y_ids = jnp.arange(cells_y, dtype=jnp.int32)
    z_ids = lax.axis_index("gz") * cells_z + jnp.arange(cells_z, dtype=jnp.int32)
    q_ids = (
        snapshot_ids[:, :, None] * variables + jnp.arange(variables, dtype=jnp.int32)[None, None, :]
    ).reshape(-1)
    factor_stream, core_stream, q_ids = lax.optimization_barrier((factor_stream, core_stream, q_ids))
    ax = test_table(x_ids, rank_ids, K, factor_stream, 1).astype(f32)
    ay = test_table(y_ids, rank_ids, K, factor_stream, 2)
    az = test_table(z_ids, rank_ids, K, factor_stream, 3)
    aq = test_table(q_ids, rank_ids, K, factor_stream, 4).astype(f32)
    phy = test_table(sketch_ids, y_ids, cells_y, core_stream, 6).astype(f32)
    phz = test_table(sketch_ids, z_ids, total_z, core_stream, 7)
    phq = test_table(q_ids, jnp.arange(E, dtype=jnp.int32), E, core_stream, 8).astype(f32)

    n_q = batches * local_snaps * variables
    field = flow_field.reshape(n_q, cells_x, cells_y, cells_z)
    rows_z = field.reshape(-1, cells_z)

    qz = aq[:, None, :] * az.astype(f32)[None, :, :]
    qz_hi = qz.astype(bf16)
    qz_lo = (qz - qz_hi.astype(f32)).astype(bf16)
    both = jnp.einsum(
        "qxyz,qzk->xyk", field, jnp.concatenate([qz_hi, qz_lo], axis=-1), preferred_element_type=f32
    )
    by_q = both[..., :K] + both[..., K:]
    part_y = jnp.sum(by_q * ax[:, None, :], axis=0)
    part_x = jnp.sum(by_q * ay.astype(f32)[None, :, :], axis=1)
    along_y = jnp.einsum("qxyz,yk->qxzk", field, ay, preferred_element_type=f32)
    weights = aq[:, None, :] * ax[None, :, :]
    part_z = jnp.sum(along_y * weights[:, :, None, :], axis=(0, 1))
    first = jnp.dot(rows_z, phz.T, preferred_element_type=f32).reshape(n_q, cells_x, cells_y, S)
    high = lax.Precision.HIGH
    by_e = jnp.einsum("qxyn,qe->xeyn", first, phq, precision=high)
    part_core = jnp.einsum("my,xeyn->xemn", phy, by_e, precision=high)

    rows_each = cells_y // (n_gx * n_gz * n_vert)
    cols_each = K // (n_gx * n_vert)
    core_rows = S * S // n_gx
    n_gzv = n_gz * n_vert
    sy = part_y.reshape(n_gx, n_gzv, rows_each, K)
    sz = part_z.T.reshape(n_gx, n_vert, cols_each, cells_z)
    sx = part_x
    core = (
        part_core.reshape(cells_x, E, n_gx, core_rows)
        .transpose(2, 0, 1, 3)
        .reshape(1, n_gx, cells_x * E * core_rows)
    )

    v_me = lax.axis_index("vert")
    merge_sz = n_vert == 2
    for d, r in ([] if merge_sz else digit_steps(n_vert)):
        digit = (v_me // d) % r
        at = split_digit(sz, 1, r, digit)
        total = at(0)
        for s in range(1, r):
            (got,) = send_to("vert", n_vert, s * d, [at(s)])
            total = total + got
        sz = total
    gzv_me = linear_index(("gz", "vert"))
    for d, r in digit_steps(n_gzv):
        digit = (gzv_me // d) % r
        at = split_digit(sy, 1, r, digit)
        sy_total, sx_total, core_total = at(0), sx, core
        with_sz = merge_sz and d == 1
        if with_sz:
            at_z = split_digit(sz, 1, 2, v_me)
            sz_total = at_z(0)
        for s in range(1, r):
            pieces = [at(s), sx, core] + ([at_z(1)] if with_sz and s == 1 else [])
            got = send_to(("gz", "vert"), n_gzv, s * d, pieces)
            sy_total, sx_total, core_total = sy_total + got[0], sx_total + got[1], core_total + got[2]
            if with_sz and s == 1:
                sz_total = sz_total + got[3]
        sy, sx, core = sy_total, sx_total, core_total
        if with_sz:
            sz = sz_total
    for d, r in digit_steps(n_gx):
        digit = (gx_me // d) % r
        at_y = split_digit(sy, 0, r, digit)
        at_z = split_digit(sz, 0, r, digit)
        at_c = split_digit(core, 1, r, digit)
        sy_total, sz_total, core_parts = at_y(0), at_z(0), [at_c(0)]
        for s in range(1, r):
            g_sy, g_sz, g_core = send_to("gx", n_gx, s * d, [at_y(s), at_z(s), at_c(s)])
            sy_total, sz_total = sy_total + g_sy, sz_total + g_sz
            core_parts.append(g_core)
        sy, sz = sy_total, sz_total
        core = jnp.concatenate(core_parts, axis=0)

    src = jnp.bitwise_xor(gx_me, jnp.arange(n_gx, dtype=jnp.int32))
    x_src = (src[:, None] * cells_x + jnp.arange(cells_x, dtype=jnp.int32)[None, :]).reshape(-1)
    phx = test_table(sketch_ids, x_src, total_x, core_stream, 5).astype(f32).reshape(S, n_gx, cells_x)
    held = core.reshape(n_gx * cells_x, E, core_rows)
    weights_x = phx.reshape(S, n_gx * cells_x)
    core_out = jnp.sum(held[:, None, :, :] * weights_x.T[:, :, None, None], axis=0).transpose(2, 1, 0)

    scale_x = 3.0**1.5 / math.sqrt(cells_y * total_z * total_q)
    scale_y = 3.0**1.5 / math.sqrt(total_x * total_z * total_q)
    scale_z = 3.0**1.5 / math.sqrt(total_x * cells_y * total_q)
    scale_core = 9.0 / math.sqrt(total_x * cells_y * total_z * total_q)
    return (
        sx * scale_x,
        sy.reshape(rows_each, K) * scale_y,
        sz.reshape(cols_each, cells_z).T * scale_z,
        core_out * scale_core,
    )


def solution(mesh):
    in_specs = (P("groups", "vert", None, "gx", None, "gz"), P("groups"), P("groups", "vert"))
    out_specs = (
        P(("groups", "gx"), None),
        P(("groups", "gx", "gz", "vert"), None),
        P(("groups", "gz"), ("gx", "vert")),
        P(("groups", "gx"), None, None),
    )
    return jax.shard_map(shards, mesh=mesh, in_specs=in_specs, out_specs=out_specs, check_vma=False)
```

```python
import math

import jax
import jax.numpy as jnp
from jax import lax
from jax.sharding import PartitionSpec as P

K = 128
S = 48
E = 2


def mix_bits(mixed):
    mixed = jnp.bitwise_xor(mixed, lax.shift_right_logical(mixed, jnp.int32(16)))
    mixed = mixed * 739982445
    mixed = jnp.bitwise_xor(mixed, lax.shift_right_logical(mixed, jnp.int32(13)))
    mixed = mixed * 695872825
    return jnp.bitwise_xor(mixed, lax.shift_right_logical(mixed, jnp.int32(16)))


def test_table(row_ids, col_ids, stride, stream, salt):
    row_term = (row_ids * stride) * -1640531535
    col_term = col_ids * -1640531535
    mixed = row_term[:, None] + col_term[None, :] + (stream * -2048144777 + salt)
    upper = lax.shift_right_logical(mix_bits(mixed), jnp.int32(9))
    return ((2 * upper + 1).astype(jnp.float32) * 2.0 ** (-24) - 1.0).astype(jnp.bfloat16)


def digit_steps(n):
    d, out = 1, []
    while d < n:
        r = 4 if n // d >= 4 else 2
        out.append((d, r))
        d *= r
    return out


def split_digit(arr, dim, r, digit):
    shape = arr.shape
    split = arr.reshape(shape[:dim] + (shape[dim] // r, r) + shape[dim + 1 :])

    def at(s):
        return lax.dynamic_index_in_dim(split, jnp.bitwise_xor(digit, s), dim + 1, keepdims=False)

    return at


def send_to(axes, n, shift, pieces):
    dense = all(p.size % 128 == 0 for p in pieces)
    if dense:
        flat = jnp.concatenate([p.reshape(-1, 128) for p in pieces], axis=0)
    else:
        flat = jnp.concatenate([p.reshape(-1) for p in pieces])
    got = lax.ppermute(flat, axes, [(i, i ^ shift) for i in range(n)])
    out, at = [], 0
    for p in pieces:
        rows = p.size // 128 if dense else p.size
        out.append(got[at : at + rows].reshape(p.shape))
        at += rows
    return out


def linear_index(axes):
    idx = 0
    for a in axes:
        idx = idx * lax.axis_size(a) + lax.axis_index(a)
    return idx


def shards(flow_field, test_streams, snapshot_ids):
    highest = lax.Precision.HIGHEST
    f32 = jnp.float32
    bf16 = jnp.bfloat16
    batches, local_snaps, variables, cells_x, cells_y, cells_z = flow_field.shape
    n_gx = lax.axis_size("gx")
    n_gz = lax.axis_size("gz")
    n_vert = lax.axis_size("vert")
    total_x = cells_x * n_gx
    total_z = cells_z * n_gz
    total_q = variables * batches * local_snaps * n_vert
    factor_stream = test_streams[0]
    core_stream = test_streams[1]
    gx_me = lax.axis_index("gx")
    rank_ids = jnp.arange(K, dtype=jnp.int32)
    sketch_ids = jnp.arange(S, dtype=jnp.int32)
    x_ids = gx_me * cells_x + jnp.arange(cells_x, dtype=jnp.int32)
    y_ids = jnp.arange(cells_y, dtype=jnp.int32)
    z_ids = lax.axis_index("gz") * cells_z + jnp.arange(cells_z, dtype=jnp.int32)
    flat_q = jnp.arange(batches * local_snaps * variables, dtype=jnp.int32)
    slot = (
        jnp.arange(batches, dtype=jnp.int32)[:, None] * local_snaps
        + jnp.arange(local_snaps, dtype=jnp.int32)[None, :]
    )
    picks = jnp.where((flat_q // variables)[:, None, None] == slot[None], snapshot_ids[None], 0)
    q_ids = jnp.sum(picks, axis=(1, 2)) * variables + flat_q % variables
    ax = test_table(x_ids, rank_ids, K, factor_stream, 1).astype(f32)
    ay = test_table(y_ids, rank_ids, K, factor_stream, 2)
    az = test_table(z_ids, rank_ids, K, factor_stream, 3)
    aq = test_table(q_ids, rank_ids, K, factor_stream, 4).astype(f32)
    phy = test_table(sketch_ids, y_ids, cells_y, core_stream, 6).astype(f32)
    phz = test_table(sketch_ids, z_ids, total_z, core_stream, 7)
    phq = test_table(q_ids, jnp.arange(E, dtype=jnp.int32), E, core_stream, 8).astype(f32)

    n_q = batches * local_snaps * variables
    field = flow_field.reshape(n_q, cells_x, cells_y, cells_z)
    rows_z = field.reshape(-1, cells_z)

    qz = aq[:, None, :] * az.astype(f32)[None, :, :]
    qz_hi = qz.astype(bf16)
    qz_lo = (qz - qz_hi.astype(f32)).astype(bf16)
    both = jnp.einsum(
        "qxyz,qzk->xyk", field, jnp.concatenate([qz_hi, qz_lo], axis=-1), preferred_element_type=f32
    )
    by_q = both[..., :K] + both[..., K:]
    part_y = jnp.sum(by_q * ax[:, None, :], axis=0)
    part_x = jnp.sum(by_q * ay.astype(f32)[None, :, :], axis=1)
    along_y = jnp.einsum("qxyz,yk->qxzk", field, ay, preferred_element_type=f32)
    weights = aq[:, None, :] * ax[None, :, :]
    part_z = jnp.sum(along_y * weights[:, :, None, :], axis=(0, 1))
    first = jnp.dot(rows_z, phz.T, preferred_element_type=f32).reshape(n_q, cells_x, cells_y, S)
    high = lax.Precision.HIGH
    by_e = jnp.einsum("qxyn,qe->xeyn", first, phq, precision=high)
    part_core = jnp.einsum("my,xeyn->xemn", phy, by_e, precision=high)

    rows_each = cells_y // (n_gx * n_gz * n_vert)
    cols_each = K // (n_gx * n_vert)
    core_rows = S * S // n_gx
    n_gzv = n_gz * n_vert
    sy = part_y.reshape(n_gx, n_gzv, rows_each, K)
    sz = part_z.T.reshape(n_gx, n_vert, cols_each, cells_z)
    sx = part_x
    core = (
        part_core.reshape(cells_x, E, n_gx, core_rows)
        .transpose(2, 0, 1, 3)
        .reshape(1, n_gx, cells_x * E * core_rows)
    )

    v_me = lax.axis_index("vert")
    merge_sz = n_vert == 2
    for d, r in ([] if merge_sz else digit_steps(n_vert)):
        digit = (v_me // d) % r
        at = split_digit(sz, 1, r, digit)
        total = at(0)
        for s in range(1, r):
            (got,) = send_to("vert", n_vert, s * d, [at(s)])
            total = total + got
        sz = total
    gzv_me = linear_index(("gz", "vert"))
    for d, r in digit_steps(n_gzv):
        digit = (gzv_me // d) % r
        at = split_digit(sy, 1, r, digit)
        sy_total, sx_total, core_total = at(0), sx, core
        with_sz = merge_sz and d == 1
        if with_sz:
            at_z = split_digit(sz, 1, 2, v_me)
            sz_total = at_z(0)
        for s in range(1, r):
            pieces = [at(s), sx, core] + ([at_z(1)] if with_sz and s == 1 else [])
            got = send_to(("gz", "vert"), n_gzv, s * d, pieces)
            sy_total, sx_total, core_total = sy_total + got[0], sx_total + got[1], core_total + got[2]
            if with_sz and s == 1:
                sz_total = sz_total + got[3]
        sy, sx, core = sy_total, sx_total, core_total
        if with_sz:
            sz = sz_total
    for d, r in digit_steps(n_gx):
        digit = (gx_me // d) % r
        at_y = split_digit(sy, 0, r, digit)
        at_z = split_digit(sz, 0, r, digit)
        at_c = split_digit(core, 1, r, digit)
        sy_total, sz_total, core_parts = at_y(0), at_z(0), [at_c(0)]
        for s in range(1, r):
            g_sy, g_sz, g_core = send_to("gx", n_gx, s * d, [at_y(s), at_z(s), at_c(s)])
            sy_total, sz_total = sy_total + g_sy, sz_total + g_sz
            core_parts.append(g_core)
        sy, sz = sy_total, sz_total
        core = jnp.concatenate(core_parts, axis=0)

    src = jnp.bitwise_xor(gx_me, jnp.arange(n_gx, dtype=jnp.int32))
    x_src = (src[:, None] * cells_x + jnp.arange(cells_x, dtype=jnp.int32)[None, :]).reshape(-1)
    phx = test_table(sketch_ids, x_src, total_x, core_stream, 5).astype(f32).reshape(S, n_gx, cells_x)
    held = core.reshape(n_gx * cells_x, E, core_rows)
    weights_x = phx.reshape(S, n_gx * cells_x)
    core_out = jnp.sum(held[:, None, :, :] * weights_x.T[:, :, None, None], axis=0).transpose(2, 1, 0)

    scale_x = 3.0**1.5 / math.sqrt(cells_y * total_z * total_q)
    scale_y = 3.0**1.5 / math.sqrt(total_x * total_z * total_q)
    scale_z = 3.0**1.5 / math.sqrt(total_x * cells_y * total_q)
    scale_core = 9.0 / math.sqrt(total_x * cells_y * total_z * total_q)
    return (
        sx * scale_x,
        sy.reshape(rows_each, K) * scale_y,
        sz.reshape(cols_each, cells_z).T * scale_z,
        core_out * scale_core,
    )


def solution(mesh):
    in_specs = (P("groups", "vert", None, "gx", None, "gz"), P("groups"), P("groups", "vert"))
    out_specs = (
        P(("groups", "gx"), None),
        P(("groups", "gx", "gz", "vert"), None),
        P(("groups", "gz"), ("gx", "vert")),
        P(("groups", "gx"), None, None),
    )
    return jax.shard_map(shards, mesh=mesh, in_specs=in_specs, out_specs=out_specs, check_vma=False)
```

```python
import math

import jax
import jax.numpy as jnp
from jax import lax
from jax.sharding import PartitionSpec as P

K = 128
S = 48
E = 2


def mix_bits(mixed):
    mixed = jnp.bitwise_xor(mixed, lax.shift_right_logical(mixed, jnp.int32(16)))
    mixed = mixed * 739982445
    mixed = jnp.bitwise_xor(mixed, lax.shift_right_logical(mixed, jnp.int32(13)))
    mixed = mixed * 695872825
    return jnp.bitwise_xor(mixed, lax.shift_right_logical(mixed, jnp.int32(16)))


def test_table(row_ids, col_ids, stride, stream, salt):
    row_term = (row_ids * stride) * -1640531535
    col_term = col_ids * -1640531535
    mixed = row_term[:, None] + col_term[None, :] + (stream * -2048144777 + salt)
    upper = lax.shift_right_logical(mix_bits(mixed), jnp.int32(9))
    return ((2 * upper + 1).astype(jnp.float32) * 2.0 ** (-24) - 1.0).astype(jnp.bfloat16)


def digit_steps(n):
    d, out = 1, []
    while d < n:
        r = 4 if n // d >= 4 else 2
        out.append((d, r))
        d *= r
    return out


def split_digit(arr, dim, r, digit):
    shape = arr.shape
    split = arr.reshape(shape[:dim] + (shape[dim] // r, r) + shape[dim + 1 :])

    def at(s):
        return lax.dynamic_index_in_dim(split, jnp.bitwise_xor(digit, s), dim + 1, keepdims=False)

    return at


def send_to(axes, n, shift, pieces):
    dense = all(p.size % 128 == 0 for p in pieces)
    if dense:
        flat = jnp.concatenate([p.reshape(-1, 128) for p in pieces], axis=0)
    else:
        flat = jnp.concatenate([p.reshape(-1) for p in pieces])
    got = lax.ppermute(flat, axes, [(i, i ^ shift) for i in range(n)])
    out, at = [], 0
    for p in pieces:
        rows = p.size // 128 if dense else p.size
        out.append(got[at : at + rows].reshape(p.shape))
        at += rows
    return out


def linear_index(axes):
    idx = 0
    for a in axes:
        idx = idx * lax.axis_size(a) + lax.axis_index(a)
    return idx


def shards(flow_field, test_streams, snapshot_ids):
    highest = lax.Precision.HIGHEST
    f32 = jnp.float32
    bf16 = jnp.bfloat16
    batches, local_snaps, variables, cells_x, cells_y, cells_z = flow_field.shape
    n_gx = lax.axis_size("gx")
    n_gz = lax.axis_size("gz")
    n_vert = lax.axis_size("vert")
    total_x = cells_x * n_gx
    total_z = cells_z * n_gz
    total_q = variables * batches * local_snaps * n_vert
    factor_stream = test_streams[0]
    core_stream = test_streams[1]
    gx_me = lax.axis_index("gx")
    rank_ids = jnp.arange(K, dtype=jnp.int32)
    sketch_ids = jnp.arange(S, dtype=jnp.int32)
    x_ids = gx_me * cells_x + jnp.arange(cells_x, dtype=jnp.int32)
    y_ids = jnp.arange(cells_y, dtype=jnp.int32)
    z_ids = lax.axis_index("gz") * cells_z + jnp.arange(cells_z, dtype=jnp.int32)
    flat_q = jnp.arange(batches * local_snaps * variables, dtype=jnp.int32)
    slot = (
        jnp.arange(batches, dtype=jnp.int32)[:, None] * local_snaps
        + jnp.arange(local_snaps, dtype=jnp.int32)[None, :]
    )
    picks = jnp.where((flat_q // variables)[:, None, None] == slot[None], snapshot_ids[None], 0)
    q_ids = jnp.sum(picks, axis=(1, 2)) * variables + flat_q % variables
    src_gx = jnp.bitwise_xor(gx_me, jnp.arange(n_gx, dtype=jnp.int32))
    x_src = (src_gx[:, None] * cells_x + jnp.arange(cells_x, dtype=jnp.int32)[None, :]).reshape(-1)
    cols = [rank_ids, rank_ids, rank_ids, rank_ids, y_ids, z_ids, jnp.arange(E, dtype=jnp.int32), x_src]
    width = max(c.shape[0] for c in cols)
    ids = jnp.stack([jnp.pad(c, (0, width - c.shape[0])) for c in cols])
    salts = jnp.array([1, 2, 3, 4, 6, 7, 8, 5], jnp.int32)[:, None]
    streams = jnp.where(jnp.arange(8, dtype=jnp.int32)[:, None] < 4, test_streams[0], test_streams[1])
    terms = ids * -1640531535 + streams * -2048144777 + salts

    def table(row_ids, stride, r):
        row_term = (row_ids * stride) * -1640531535
        upper = lax.shift_right_logical(mix_bits(row_term[:, None] + terms[r, None, : cols[r].shape[0]]), jnp.int32(9))
        return ((2 * upper + 1).astype(f32) * 2.0 ** (-24) - 1.0).astype(bf16)

    ax = table(x_ids, K, 0).astype(f32)
    ay = table(y_ids, K, 1)
    az = table(z_ids, K, 2)
    aq = table(q_ids, K, 3).astype(f32)
    phy = table(sketch_ids, cells_y, 4).astype(f32)
    phz = table(sketch_ids, total_z, 5)
    phq = table(q_ids, E, 6).astype(f32)
    phx = table(sketch_ids, total_x, 7).astype(f32).reshape(S, n_gx, cells_x)

    n_q = batches * local_snaps * variables
    field = flow_field.reshape(n_q, cells_x, cells_y, cells_z)
    rows_z = field.reshape(-1, cells_z)

    qz = aq[:, None, :] * az.astype(f32)[None, :, :]
    qz_hi = qz.astype(bf16)
    qz_lo = (qz - qz_hi.astype(f32)).astype(bf16)
    both = jnp.einsum(
        "qxyz,qzk->xyk", field, jnp.concatenate([qz_hi, qz_lo], axis=-1), preferred_element_type=f32
    )
    by_q = both[..., :K] + both[..., K:]
    part_y = jnp.sum(by_q * ax[:, None, :], axis=0)
    part_x = jnp.sum(by_q * ay.astype(f32)[None, :, :], axis=1)
    along_y = jnp.einsum("qxyz,yk->qxzk", field, ay, preferred_element_type=f32)
    weights = aq[:, None, :] * ax[None, :, :]
    part_z = jnp.sum(along_y * weights[:, :, None, :], axis=(0, 1))
    first = jnp.dot(rows_z, phz.T, preferred_element_type=f32).reshape(n_q, cells_x, cells_y, S)
    high = lax.Precision.HIGH
    by_e = jnp.einsum("qxyn,qe->xeyn", first, phq, precision=high)
    part_core = jnp.einsum("my,xeyn->xemn", phy, by_e, precision=high)

    rows_each = cells_y // (n_gx * n_gz * n_vert)
    cols_each = K // (n_gx * n_vert)
    core_rows = S * S // n_gx
    n_gzv = n_gz * n_vert
    sy = part_y.reshape(n_gx, n_gzv, rows_each, K)
    sz = part_z.T.reshape(n_gx, n_vert, cols_each, cells_z)
    sx = part_x
    core = (
        part_core.reshape(cells_x, E, n_gx, core_rows)
        .transpose(2, 0, 1, 3)
        .reshape(1, n_gx, cells_x * E * core_rows)
    )

    v_me = lax.axis_index("vert")
    merge_sz = n_vert == 2
    for d, r in ([] if merge_sz else digit_steps(n_vert)):
        digit = (v_me // d) % r
        at = split_digit(sz, 1, r, digit)
        total = at(0)
        for s in range(1, r):
            (got,) = send_to("vert", n_vert, s * d, [at(s)])
            total = total + got
        sz = total
    gzv_me = linear_index(("gz", "vert"))
    for d, r in digit_steps(n_gzv):
        digit = (gzv_me // d) % r
        at = split_digit(sy, 1, r, digit)
        sy_total, sx_total, core_total = at(0), sx, core
        with_sz = merge_sz and d == 1
        if with_sz:
            at_z = split_digit(sz, 1, 2, v_me)
            sz_total = at_z(0)
        for s in range(1, r):
            pieces = [at(s), sx, core] + ([at_z(1)] if with_sz and s == 1 else [])
            got = send_to(("gz", "vert"), n_gzv, s * d, pieces)
            sy_total, sx_total, core_total = sy_total + got[0], sx_total + got[1], core_total + got[2]
            if with_sz and s == 1:
                sz_total = sz_total + got[3]
        sy, sx, core = sy_total, sx_total, core_total
        if with_sz:
            sz = sz_total
    for d, r in digit_steps(n_gx):
        digit = (gx_me // d) % r
        at_y = split_digit(sy, 0, r, digit)
        at_z = split_digit(sz, 0, r, digit)
        at_c = split_digit(core, 1, r, digit)
        sy_total, sz_total, core_parts = at_y(0), at_z(0), [at_c(0)]
        for s in range(1, r):
            g_sy, g_sz, g_core = send_to("gx", n_gx, s * d, [at_y(s), at_z(s), at_c(s)])
            sy_total, sz_total = sy_total + g_sy, sz_total + g_sz
            core_parts.append(g_core)
        sy, sz = sy_total, sz_total
        core = jnp.concatenate(core_parts, axis=0)

    held = core.reshape(n_gx * cells_x, E, core_rows)
    weights_x = phx.reshape(S, n_gx * cells_x)
    core_out = jnp.sum(held[:, None, :, :] * weights_x.T[:, :, None, None], axis=0).transpose(2, 1, 0)

    scale_x = 3.0**1.5 / math.sqrt(cells_y * total_z * total_q)
    scale_y = 3.0**1.5 / math.sqrt(total_x * total_z * total_q)
    scale_z = 3.0**1.5 / math.sqrt(total_x * cells_y * total_q)
    scale_core = 9.0 / math.sqrt(total_x * cells_y * total_z * total_q)
    return (
        sx * scale_x,
        sy.reshape(rows_each, K) * scale_y,
        sz.reshape(cols_each, cells_z).T * scale_z,
        core_out * scale_core,
    )


def solution(mesh):
    in_specs = (P("groups", "vert", None, "gx", None, "gz"), P("groups"), P("groups", "vert"))
    out_specs = (
        P(("groups", "gx"), None),
        P(("groups", "gx", "gz", "vert"), None),
        P(("groups", "gz"), ("gx", "vert")),
        P(("groups", "gx"), None, None),
    )
    return jax.shard_map(shards, mesh=mesh, in_specs=in_specs, out_specs=out_specs, check_vma=False)
```

```python
import math

import jax
import jax.numpy as jnp
from jax import lax
from jax.sharding import PartitionSpec as P

K = 128
S = 48
E = 2


def mix_bits(mixed):
    mixed = jnp.bitwise_xor(mixed, lax.shift_right_logical(mixed, jnp.int32(16)))
    mixed = mixed * 739982445
    mixed = jnp.bitwise_xor(mixed, lax.shift_right_logical(mixed, jnp.int32(13)))
    mixed = mixed * 695872825
    return jnp.bitwise_xor(mixed, lax.shift_right_logical(mixed, jnp.int32(16)))


def test_table(row_ids, col_ids, stride, stream, salt):
    row_term = (row_ids * stride) * -1640531535
    col_term = col_ids * -1640531535
    mixed = row_term[:, None] + col_term[None, :] + (stream * -2048144777 + salt)
    upper = lax.shift_right_logical(mix_bits(mixed), jnp.int32(9))
    return ((2 * upper + 1).astype(jnp.float32) * 2.0 ** (-24) - 1.0).astype(jnp.bfloat16)


def digit_steps(n):
    d, out = 1, []
    while d < n:
        r = 4 if n // d >= 4 else 2
        out.append((d, r))
        d *= r
    return out


def split_digit(arr, dim, r, digit):
    shape = arr.shape
    split = arr.reshape(shape[:dim] + (shape[dim] // r, r) + shape[dim + 1 :])

    def at(s):
        return lax.dynamic_index_in_dim(split, jnp.bitwise_xor(digit, s), dim + 1, keepdims=False)

    return at


def send_to(axes, n, shift, pieces):
    dense = all(p.size % 128 == 0 for p in pieces)
    if dense:
        flat = jnp.concatenate([p.reshape(-1, 128) for p in pieces], axis=0)
    else:
        flat = jnp.concatenate([p.reshape(-1) for p in pieces])
    got = lax.ppermute(flat, axes, [(i, i ^ shift) for i in range(n)])
    out, at = [], 0
    for p in pieces:
        rows = p.size // 128 if dense else p.size
        out.append(got[at : at + rows].reshape(p.shape))
        at += rows
    return out


def linear_index(axes):
    idx = 0
    for a in axes:
        idx = idx * lax.axis_size(a) + lax.axis_index(a)
    return idx


def shards(flow_field, test_streams, snapshot_ids):
    highest = lax.Precision.HIGHEST
    f32 = jnp.float32
    bf16 = jnp.bfloat16
    batches, local_snaps, variables, cells_x, cells_y, cells_z = flow_field.shape
    n_gx = lax.axis_size("gx")
    n_gz = lax.axis_size("gz")
    n_vert = lax.axis_size("vert")
    total_x = cells_x * n_gx
    total_z = cells_z * n_gz
    total_q = variables * batches * local_snaps * n_vert
    factor_stream = test_streams[0]
    core_stream = test_streams[1]
    gx_me = lax.axis_index("gx")
    rank_ids = jnp.arange(K, dtype=jnp.int32)
    sketch_ids = jnp.arange(S, dtype=jnp.int32)
    x_ids = gx_me * cells_x + jnp.arange(cells_x, dtype=jnp.int32)
    y_ids = jnp.arange(cells_y, dtype=jnp.int32)
    z_ids = lax.axis_index("gz") * cells_z + jnp.arange(cells_z, dtype=jnp.int32)
    flat_q = jnp.arange(batches * local_snaps * variables, dtype=jnp.int32)
    slot = (
        jnp.arange(batches, dtype=jnp.int32)[:, None] * local_snaps
        + jnp.arange(local_snaps, dtype=jnp.int32)[None, :]
    )
    picks = jnp.where((flat_q // variables)[:, None, None] == slot[None], snapshot_ids[None], 0)
    q_ids = jnp.sum(picks, axis=(1, 2)) * variables + flat_q % variables
    ax = test_table(x_ids, rank_ids, K, factor_stream, 1).astype(f32)
    ay = test_table(y_ids, rank_ids, K, factor_stream, 2)
    az = test_table(z_ids, rank_ids, K, factor_stream, 3)
    aq = test_table(q_ids, rank_ids, K, factor_stream, 4).astype(f32)
    phy = test_table(sketch_ids, y_ids, cells_y, core_stream, 6).astype(f32)
    phz = test_table(sketch_ids, z_ids, total_z, core_stream, 7)
    phq = test_table(q_ids, jnp.arange(E, dtype=jnp.int32), E, core_stream, 8).astype(f32)

    n_q = batches * local_snaps * variables
    field = flow_field.reshape(n_q, cells_x, cells_y, cells_z)
    rows_z = field.reshape(-1, cells_z)

    qz = aq[:, None, :] * az.astype(f32)[None, :, :]
    qz_hi = qz.astype(bf16)
    qz_lo = (qz - qz_hi.astype(f32)).astype(bf16)
    both = jnp.einsum(
        "qxyz,qzk->xyk", field, jnp.concatenate([qz_hi, qz_lo], axis=-1), preferred_element_type=f32
    )
    by_q = both[..., :K] + both[..., K:]
    part_y = jnp.sum(by_q * ax[:, None, :], axis=0)
    part_x = jnp.sum(by_q * ay.astype(f32)[None, :, :], axis=1)
    along_y = jnp.einsum("qxyz,yk->qxzk", field, ay, preferred_element_type=f32)
    weights = aq[:, None, :] * ax[None, :, :]
    part_z = jnp.sum(along_y * weights[:, :, None, :], axis=(0, 1))
    first = jnp.dot(rows_z, phz.T, preferred_element_type=f32).reshape(n_q, cells_x, cells_y, S)
    high = lax.Precision.HIGH
    by_e = jnp.einsum("qxyn,qe->xeyn", first, phq, precision=high)
    part_core = jnp.einsum("my,xeyn->xemn", phy, by_e, precision=high)

    rows_each = cells_y // (n_gx * n_gz * n_vert)
    cols_each = K // (n_gx * n_vert)
    core_rows = S * S // n_gx
    n_gzv = n_gz * n_vert
    sy = part_y.reshape(n_gx, n_gzv, rows_each, K)
    sz = part_z.T.reshape(n_gx, n_vert, cols_each, cells_z)
    sx = part_x
    core = (
        part_core.reshape(cells_x, E, n_gx, core_rows)
        .transpose(2, 0, 1, 3)
        .reshape(1, n_gx, cells_x * E * core_rows)
    )

    v_me = lax.axis_index("vert")
    merge_sz = n_vert == 2
    for d, r in ([] if merge_sz else digit_steps(n_vert)):
        digit = (v_me // d) % r
        at = split_digit(sz, 1, r, digit)
        total = at(0)
        for s in range(1, r):
            (got,) = send_to("vert", n_vert, s * d, [at(s)])
            total = total + got
        sz = total
    gzv_me = linear_index(("gz", "vert"))
    for d, r in digit_steps(n_gzv):
        digit = (gzv_me // d) % r
        at = split_digit(sy, 1, r, digit)
        sy_total, sx_total, core_total = at(0), sx, core
        with_sz = merge_sz and d == 1
        if with_sz:
            at_z = split_digit(sz, 1, 2, v_me)
            sz_total = at_z(0)
        for s in range(1, r):
            pieces = [at(s), sx, core] + ([at_z(1)] if with_sz and s == 1 else [])
            got = send_to(("gz", "vert"), n_gzv, s * d, pieces)
            sy_total, sx_total, core_total = sy_total + got[0], sx_total + got[1], core_total + got[2]
            if with_sz and s == 1:
                sz_total = sz_total + got[3]
        sy, sx, core = sy_total, sx_total, core_total
        if with_sz:
            sz = sz_total
    src = jnp.bitwise_xor(gx_me, jnp.arange(n_gx, dtype=jnp.int32))
    x_src = (src[:, None] * cells_x + jnp.arange(cells_x, dtype=jnp.int32)[None, :]).reshape(-1)
    phx = test_table(sketch_ids, x_src, total_x, core_stream, 5).astype(f32).reshape(S, n_gx, cells_x)
    core, phx = lax.optimization_barrier((core, phx))
    for d, r in digit_steps(n_gx):
        digit = (gx_me // d) % r
        at_y = split_digit(sy, 0, r, digit)
        at_z = split_digit(sz, 0, r, digit)
        at_c = split_digit(core, 1, r, digit)
        sy_total, sz_total, core_parts = at_y(0), at_z(0), [at_c(0)]
        for s in range(1, r):
            g_sy, g_sz, g_core = send_to("gx", n_gx, s * d, [at_y(s), at_z(s), at_c(s)])
            sy_total, sz_total = sy_total + g_sy, sz_total + g_sz
            core_parts.append(g_core)
        sy, sz = sy_total, sz_total
        core = jnp.concatenate(core_parts, axis=0)

    held = core.reshape(n_gx * cells_x, E, core_rows)
    weights_x = phx.reshape(S, n_gx * cells_x)
    core_out = jnp.sum(held[:, None, :, :] * weights_x.T[:, :, None, None], axis=0).transpose(2, 1, 0)

    scale_x = 3.0**1.5 / math.sqrt(cells_y * total_z * total_q)
    scale_y = 3.0**1.5 / math.sqrt(total_x * total_z * total_q)
    scale_z = 3.0**1.5 / math.sqrt(total_x * cells_y * total_q)
    scale_core = 9.0 / math.sqrt(total_x * cells_y * total_z * total_q)
    return (
        sx * scale_x,
        sy.reshape(rows_each, K) * scale_y,
        sz.reshape(cols_each, cells_z).T * scale_z,
        core_out * scale_core,
    )


def solution(mesh):
    in_specs = (P("groups", "vert", None, "gx", None, "gz"), P("groups"), P("groups", "vert"))
    out_specs = (
        P(("groups", "gx"), None),
        P(("groups", "gx", "gz", "vert"), None),
        P(("groups", "gz"), ("gx", "vert")),
        P(("groups", "gx"), None, None),
    )
    return jax.shard_map(shards, mesh=mesh, in_specs=in_specs, out_specs=out_specs, check_vma=False)
```

```python
import math

import jax
import jax.numpy as jnp
from jax import lax
from jax.sharding import PartitionSpec as P

K = 128
S = 48
E = 2


def mix_bits(mixed):
    mixed = jnp.bitwise_xor(mixed, lax.shift_right_logical(mixed, jnp.int32(16)))
    mixed = mixed * 739982445
    mixed = jnp.bitwise_xor(mixed, lax.shift_right_logical(mixed, jnp.int32(13)))
    mixed = mixed * 695872825
    return jnp.bitwise_xor(mixed, lax.shift_right_logical(mixed, jnp.int32(16)))


def test_table(row_ids, col_ids, stride, stream, salt):
    row_term = (row_ids * stride) * -1640531535
    col_term = col_ids * -1640531535
    mixed = row_term[:, None] + col_term[None, :] + (stream * -2048144777 + salt)
    upper = lax.shift_right_logical(mix_bits(mixed), jnp.int32(9))
    return ((2 * upper + 1).astype(jnp.float32) * 2.0 ** (-24) - 1.0).astype(jnp.bfloat16)


def digit_steps(n):
    d, out = 1, []
    while d < n:
        r = 4 if n // d >= 4 else 2
        out.append((d, r))
        d *= r
    return out


def split_digit(arr, dim, r, digit):
    shape = arr.shape
    split = arr.reshape(shape[:dim] + (shape[dim] // r, r) + shape[dim + 1 :])

    def at(s):
        return lax.dynamic_index_in_dim(split, jnp.bitwise_xor(digit, s), dim + 1, keepdims=False)

    return at


def send_to(axes, n, shift, pieces):
    dense = all(p.size % 128 == 0 for p in pieces)
    if dense:
        flat = jnp.concatenate([p.reshape(-1, 128) for p in pieces], axis=0)
    else:
        flat = jnp.concatenate([p.reshape(-1) for p in pieces])
    got = lax.ppermute(flat, axes, [(i, i ^ shift) for i in range(n)])
    out, at = [], 0
    for p in pieces:
        rows = p.size // 128 if dense else p.size
        out.append(got[at : at + rows].reshape(p.shape))
        at += rows
    return out


def linear_index(axes):
    idx = 0
    for a in axes:
        idx = idx * lax.axis_size(a) + lax.axis_index(a)
    return idx


def shards(flow_field, test_streams, snapshot_ids):
    highest = lax.Precision.HIGHEST
    f32 = jnp.float32
    bf16 = jnp.bfloat16
    batches, local_snaps, variables, cells_x, cells_y, cells_z = flow_field.shape
    n_gx = lax.axis_size("gx")
    n_gz = lax.axis_size("gz")
    n_vert = lax.axis_size("vert")
    total_x = cells_x * n_gx
    total_z = cells_z * n_gz
    total_q = variables * batches * local_snaps * n_vert
    factor_stream = test_streams[0]
    core_stream = test_streams[1]
    gx_me = lax.axis_index("gx")
    rank_ids = jnp.arange(K, dtype=jnp.int32)
    sketch_ids = jnp.arange(S, dtype=jnp.int32)
    x_ids = gx_me * cells_x + jnp.arange(cells_x, dtype=jnp.int32)
    y_ids = jnp.arange(cells_y, dtype=jnp.int32)
    z_ids = lax.axis_index("gz") * cells_z + jnp.arange(cells_z, dtype=jnp.int32)
    flat_q = jnp.arange(batches * local_snaps * variables, dtype=jnp.int32)
    slot = (
        jnp.arange(batches, dtype=jnp.int32)[:, None] * local_snaps
        + jnp.arange(local_snaps, dtype=jnp.int32)[None, :]
    )
    picks = jnp.where((flat_q // variables)[:, None, None] == slot[None], snapshot_ids[None], 0)
    q_ids = jnp.sum(picks, axis=(1, 2)) * variables + flat_q % variables
    ax = test_table(x_ids, rank_ids, K, factor_stream, 1).astype(f32)
    ay = test_table(y_ids, rank_ids, K, factor_stream, 2)
    az = test_table(z_ids, rank_ids, K, factor_stream, 3)
    aq = test_table(q_ids, rank_ids, K, factor_stream, 4).astype(f32)
    phy = test_table(sketch_ids, y_ids, cells_y, core_stream, 6).astype(f32)
    phz = test_table(sketch_ids, z_ids, total_z, core_stream, 7)
    phq = test_table(q_ids, jnp.arange(E, dtype=jnp.int32), E, core_stream, 8).astype(f32)
    phz, az = lax.optimization_barrier((phz, az))

    n_q = batches * local_snaps * variables
    field = flow_field.reshape(n_q, cells_x, cells_y, cells_z)
    rows_z = field.reshape(-1, cells_z)

    qz = aq[:, None, :] * az.astype(f32)[None, :, :]
    qz_hi = qz.astype(bf16)
    qz_lo = (qz - qz_hi.astype(f32)).astype(bf16)
    both = jnp.einsum(
        "qxyz,qzk->xyk", field, jnp.concatenate([qz_hi, qz_lo], axis=-1), preferred_element_type=f32
    )
    by_q = both[..., :K] + both[..., K:]
    part_y = jnp.sum(by_q * ax[:, None, :], axis=0)
    part_x = jnp.sum(by_q * ay.astype(f32)[None, :, :], axis=1)
    along_y = jnp.einsum("qxyz,yk->qxzk", field, ay, preferred_element_type=f32)
    weights = aq[:, None, :] * ax[None, :, :]
    part_z = jnp.sum(along_y * weights[:, :, None, :], axis=(0, 1))
    first = jnp.dot(rows_z, phz.T, preferred_element_type=f32).reshape(n_q, cells_x, cells_y, S)
    high = lax.Precision.HIGH
    by_e = jnp.einsum("qxyn,qe->xeyn", first, phq, precision=high)
    part_core = jnp.einsum("my,xeyn->xemn", phy, by_e, precision=high)

    rows_each = cells_y // (n_gx * n_gz * n_vert)
    cols_each = K // (n_gx * n_vert)
    core_rows = S * S // n_gx
    n_gzv = n_gz * n_vert
    sy = part_y.reshape(n_gx, n_gzv, rows_each, K)
    sz = part_z.T.reshape(n_gx, n_vert, cols_each, cells_z)
    sx = part_x
    core = (
        part_core.reshape(cells_x, E, n_gx, core_rows)
        .transpose(2, 0, 1, 3)
        .reshape(1, n_gx, cells_x * E * core_rows)
    )

    v_me = lax.axis_index("vert")
    merge_sz = n_vert == 2
    for d, r in ([] if merge_sz else digit_steps(n_vert)):
        digit = (v_me // d) % r
        at = split_digit(sz, 1, r, digit)
        total = at(0)
        for s in range(1, r):
            (got,) = send_to("vert", n_vert, s * d, [at(s)])
            total = total + got
        sz = total
    gzv_me = linear_index(("gz", "vert"))
    for d, r in digit_steps(n_gzv):
        digit = (gzv_me // d) % r
        at = split_digit(sy, 1, r, digit)
        sy_total, sx_total, core_total = at(0), sx, core
        with_sz = merge_sz and d == 1
        if with_sz:
            at_z = split_digit(sz, 1, 2, v_me)
            sz_total = at_z(0)
        for s in range(1, r):
            pieces = [at(s), sx, core] + ([at_z(1)] if with_sz and s == 1 else [])
            got = send_to(("gz", "vert"), n_gzv, s * d, pieces)
            sy_total, sx_total, core_total = sy_total + got[0], sx_total + got[1], core_total + got[2]
            if with_sz and s == 1:
                sz_total = sz_total + got[3]
        sy, sx, core = sy_total, sx_total, core_total
        if with_sz:
            sz = sz_total
    src = jnp.bitwise_xor(gx_me, jnp.arange(n_gx, dtype=jnp.int32))
    x_src = (src[:, None] * cells_x + jnp.arange(cells_x, dtype=jnp.int32)[None, :]).reshape(-1)
    phx = test_table(sketch_ids, x_src, total_x, core_stream, 5).astype(f32).reshape(S, n_gx, cells_x)
    core, phx = lax.optimization_barrier((core, phx))
    for d, r in digit_steps(n_gx):
        digit = (gx_me // d) % r
        at_y = split_digit(sy, 0, r, digit)
        at_z = split_digit(sz, 0, r, digit)
        at_c = split_digit(core, 1, r, digit)
        sy_total, sz_total, core_parts = at_y(0), at_z(0), [at_c(0)]
        for s in range(1, r):
            g_sy, g_sz, g_core = send_to("gx", n_gx, s * d, [at_y(s), at_z(s), at_c(s)])
            sy_total, sz_total = sy_total + g_sy, sz_total + g_sz
            core_parts.append(g_core)
        sy, sz = sy_total, sz_total
        core = jnp.concatenate(core_parts, axis=0)

    held = core.reshape(n_gx * cells_x, E, core_rows)
    weights_x = phx.reshape(S, n_gx * cells_x)
    core_out = jnp.sum(held[:, None, :, :] * weights_x.T[:, :, None, None], axis=0).transpose(2, 1, 0)

    scale_x = 3.0**1.5 / math.sqrt(cells_y * total_z * total_q)
    scale_y = 3.0**1.5 / math.sqrt(total_x * total_z * total_q)
    scale_z = 3.0**1.5 / math.sqrt(total_x * cells_y * total_q)
    scale_core = 9.0 / math.sqrt(total_x * cells_y * total_z * total_q)
    return (
        sx * scale_x,
        sy.reshape(rows_each, K) * scale_y,
        sz.reshape(cols_each, cells_z).T * scale_z,
        core_out * scale_core,
    )


def solution(mesh):
    in_specs = (P("groups", "vert", None, "gx", None, "gz"), P("groups"), P("groups", "vert"))
    out_specs = (
        P(("groups", "gx"), None),
        P(("groups", "gx", "gz", "vert"), None),
        P(("groups", "gz"), ("gx", "vert")),
        P(("groups", "gx"), None, None),
    )
    return jax.shard_map(shards, mesh=mesh, in_specs=in_specs, out_specs=out_specs, check_vma=False)
```

```python
import math

import jax
import jax.numpy as jnp
from jax import lax
from jax.sharding import PartitionSpec as P

K = 128
S = 48
E = 2


def mix_bits(mixed):
    mixed = jnp.bitwise_xor(mixed, lax.shift_right_logical(mixed, jnp.int32(16)))
    mixed = mixed * 739982445
    mixed = jnp.bitwise_xor(mixed, lax.shift_right_logical(mixed, jnp.int32(13)))
    mixed = mixed * 695872825
    return jnp.bitwise_xor(mixed, lax.shift_right_logical(mixed, jnp.int32(16)))


def test_table(row_ids, col_ids, stride, stream, salt):
    row_term = (row_ids * stride) * -1640531535
    col_term = col_ids * -1640531535
    mixed = row_term[:, None] + col_term[None, :] + (stream * -2048144777 + salt)
    upper = lax.shift_right_logical(mix_bits(mixed), jnp.int32(9))
    return ((2 * upper + 1).astype(jnp.float32) * 2.0 ** (-24) - 1.0).astype(jnp.bfloat16)


def digit_steps(n):
    d, out = 1, []
    while d < n:
        r = 4 if n // d >= 4 else 2
        out.append((d, r))
        d *= r
    return out


def split_digit(arr, dim, r, digit):
    shape = arr.shape
    split = arr.reshape(shape[:dim] + (shape[dim] // r, r) + shape[dim + 1 :])

    def at(s):
        return lax.dynamic_index_in_dim(split, jnp.bitwise_xor(digit, s), dim + 1, keepdims=False)

    return at


def send_to(axes, n, shift, pieces):
    dense = all(p.size % 128 == 0 for p in pieces)
    if dense:
        flat = jnp.concatenate([p.reshape(-1, 128) for p in pieces], axis=0)
    else:
        flat = jnp.concatenate([p.reshape(-1) for p in pieces])
    got = lax.ppermute(flat, axes, [(i, i ^ shift) for i in range(n)])
    out, at = [], 0
    for p in pieces:
        rows = p.size // 128 if dense else p.size
        out.append(got[at : at + rows].reshape(p.shape))
        at += rows
    return out


def linear_index(axes):
    idx = 0
    for a in axes:
        idx = idx * lax.axis_size(a) + lax.axis_index(a)
    return idx


def shards(flow_field, test_streams, snapshot_ids):
    highest = lax.Precision.HIGHEST
    f32 = jnp.float32
    bf16 = jnp.bfloat16
    batches, local_snaps, variables, cells_x, cells_y, cells_z = flow_field.shape
    n_gx = lax.axis_size("gx")
    n_gz = lax.axis_size("gz")
    n_vert = lax.axis_size("vert")
    total_x = cells_x * n_gx
    total_z = cells_z * n_gz
    total_q = variables * batches * local_snaps * n_vert
    which_stream = jnp.arange(test_streams.shape[0], dtype=jnp.int32)
    factor_stream = jnp.sum(jnp.where(which_stream == 0, test_streams, 0))
    core_stream = jnp.sum(jnp.where(which_stream == 1, test_streams, 0))
    gx_me = lax.axis_index("gx")
    rank_ids = jnp.arange(K, dtype=jnp.int32)
    sketch_ids = jnp.arange(S, dtype=jnp.int32)
    x_ids = gx_me * cells_x + jnp.arange(cells_x, dtype=jnp.int32)
    y_ids = jnp.arange(cells_y, dtype=jnp.int32)
    z_ids = lax.axis_index("gz") * cells_z + jnp.arange(cells_z, dtype=jnp.int32)
    flat_q = jnp.arange(batches * local_snaps * variables, dtype=jnp.int32)
    slot = (
        jnp.arange(batches, dtype=jnp.int32)[:, None] * local_snaps
        + jnp.arange(local_snaps, dtype=jnp.int32)[None, :]
    )
    picks = jnp.where((flat_q // variables)[:, None, None] == slot[None], snapshot_ids[None], 0)
    q_ids = jnp.sum(picks, axis=(1, 2)) * variables + flat_q % variables
    ax = test_table(x_ids, rank_ids, K, factor_stream, 1).astype(f32)
    ay = test_table(y_ids, rank_ids, K, factor_stream, 2)
    az = test_table(z_ids, rank_ids, K, factor_stream, 3)
    aq = test_table(q_ids, rank_ids, K, factor_stream, 4).astype(f32)
    phy = test_table(sketch_ids, y_ids, cells_y, core_stream, 6).astype(f32)
    phz = test_table(sketch_ids, z_ids, total_z, core_stream, 7)
    phq = test_table(q_ids, jnp.arange(E, dtype=jnp.int32), E, core_stream, 8).astype(f32)

    n_q = batches * local_snaps * variables
    field = flow_field.reshape(n_q, cells_x, cells_y, cells_z)
    rows_z = field.reshape(-1, cells_z)

    qz = aq[:, None, :] * az.astype(f32)[None, :, :]
    qz_hi = qz.astype(bf16)
    qz_lo = (qz - qz_hi.astype(f32)).astype(bf16)
    both = jnp.einsum(
        "qxyz,qzk->xyk", field, jnp.concatenate([qz_hi, qz_lo], axis=-1), preferred_element_type=f32
    )
    by_q = both[..., :K] + both[..., K:]
    part_y = jnp.sum(by_q * ax[:, None, :], axis=0)
    part_x = jnp.sum(by_q * ay.astype(f32)[None, :, :], axis=1)
    along_y = jnp.einsum("qxyz,yk->qxzk", field, ay, preferred_element_type=f32)
    weights = aq[:, None, :] * ax[None, :, :]
    part_z = jnp.sum(along_y * weights[:, :, None, :], axis=(0, 1))
    first = jnp.dot(rows_z, phz.T, preferred_element_type=f32).reshape(n_q, cells_x, cells_y, S)
    high = lax.Precision.HIGH
    by_e = jnp.einsum("qxyn,qe->xeyn", first, phq, precision=high)
    part_core = jnp.einsum("my,xeyn->xemn", phy, by_e, precision=high)

    rows_each = cells_y // (n_gx * n_gz * n_vert)
    cols_each = K // (n_gx * n_vert)
    core_rows = S * S // n_gx
    n_gzv = n_gz * n_vert
    sy = part_y.reshape(n_gx, n_gzv, rows_each, K)
    sz = part_z.T.reshape(n_gx, n_vert, cols_each, cells_z)
    sx = part_x
    core = (
        part_core.reshape(cells_x, E, n_gx, core_rows)
        .transpose(2, 0, 1, 3)
        .reshape(1, n_gx, cells_x * E * core_rows)
    )

    v_me = lax.axis_index("vert")
    merge_sz = n_vert == 2
    for d, r in ([] if merge_sz else digit_steps(n_vert)):
        digit = (v_me // d) % r
        at = split_digit(sz, 1, r, digit)
        total = at(0)
        for s in range(1, r):
            (got,) = send_to("vert", n_vert, s * d, [at(s)])
            total = total + got
        sz = total
    gzv_me = linear_index(("gz", "vert"))
    for d, r in digit_steps(n_gzv):
        digit = (gzv_me // d) % r
        at = split_digit(sy, 1, r, digit)
        sy_total, sx_total, core_total = at(0), sx, core
        with_sz = merge_sz and d == 1
        if with_sz:
            at_z = split_digit(sz, 1, 2, v_me)
            sz_total = at_z(0)
        for s in range(1, r):
            pieces = [at(s), sx, core] + ([at_z(1)] if with_sz and s == 1 else [])
            got = send_to(("gz", "vert"), n_gzv, s * d, pieces)
            sy_total, sx_total, core_total = sy_total + got[0], sx_total + got[1], core_total + got[2]
            if with_sz and s == 1:
                sz_total = sz_total + got[3]
        sy, sx, core = sy_total, sx_total, core_total
        if with_sz:
            sz = sz_total
    src = jnp.bitwise_xor(gx_me, jnp.arange(n_gx, dtype=jnp.int32))
    x_src = (src[:, None] * cells_x + jnp.arange(cells_x, dtype=jnp.int32)[None, :]).reshape(-1)
    phx = test_table(sketch_ids, x_src, total_x, core_stream, 5).astype(f32).reshape(S, n_gx, cells_x)
    core, phx = lax.optimization_barrier((core, phx))
    for d, r in digit_steps(n_gx):
        digit = (gx_me // d) % r
        at_y = split_digit(sy, 0, r, digit)
        at_z = split_digit(sz, 0, r, digit)
        at_c = split_digit(core, 1, r, digit)
        sy_total, sz_total, core_parts = at_y(0), at_z(0), [at_c(0)]
        for s in range(1, r):
            g_sy, g_sz, g_core = send_to("gx", n_gx, s * d, [at_y(s), at_z(s), at_c(s)])
            sy_total, sz_total = sy_total + g_sy, sz_total + g_sz
            core_parts.append(g_core)
        sy, sz = sy_total, sz_total
        core = jnp.concatenate(core_parts, axis=0)

    held = core.reshape(n_gx * cells_x, E, core_rows)
    weights_x = phx.reshape(S, n_gx * cells_x)
    core_out = jnp.sum(held[:, None, :, :] * weights_x.T[:, :, None, None], axis=0).transpose(2, 1, 0)

    scale_x = 3.0**1.5 / math.sqrt(cells_y * total_z * total_q)
    scale_y = 3.0**1.5 / math.sqrt(total_x * total_z * total_q)
    scale_z = 3.0**1.5 / math.sqrt(total_x * cells_y * total_q)
    scale_core = 9.0 / math.sqrt(total_x * cells_y * total_z * total_q)
    return (
        sx * scale_x,
        sy.reshape(rows_each, K) * scale_y,
        sz.reshape(cols_each, cells_z).T * scale_z,
        core_out * scale_core,
    )


def solution(mesh):
    in_specs = (P("groups", "vert", None, "gx", None, "gz"), P("groups"), P("groups", "vert"))
    out_specs = (
        P(("groups", "gx"), None),
        P(("groups", "gx", "gz", "vert"), None),
        P(("groups", "gz"), ("gx", "vert")),
        P(("groups", "gx"), None, None),
    )
    return jax.shard_map(shards, mesh=mesh, in_specs=in_specs, out_specs=out_specs, check_vma=False)
```

```python
import math

import jax
import jax.numpy as jnp
from jax import lax
from jax.sharding import PartitionSpec as P

K = 128
S = 48
E = 2


def mix_bits(mixed):
    mixed = jnp.bitwise_xor(mixed, lax.shift_right_logical(mixed, jnp.int32(16)))
    mixed = mixed * 739982445
    mixed = jnp.bitwise_xor(mixed, lax.shift_right_logical(mixed, jnp.int32(13)))
    mixed = mixed * 695872825
    return jnp.bitwise_xor(mixed, lax.shift_right_logical(mixed, jnp.int32(16)))


def test_table(row_ids, col_ids, stride, stream, salt):
    row_term = (row_ids * stride) * -1640531535
    col_term = col_ids * -1640531535
    mixed = row_term[:, None] + col_term[None, :] + (stream * -2048144777 + salt)
    upper = lax.shift_right_logical(mix_bits(mixed), jnp.int32(9))
    return ((2 * upper + 1).astype(jnp.float32) * 2.0 ** (-24) - 1.0).astype(jnp.bfloat16)


def digit_steps(n):
    d, out = 1, []
    while d < n:
        r = 4 if n // d >= 4 else 2
        out.append((d, r))
        d *= r
    return out


def split_digit(arr, dim, r, digit):
    shape = arr.shape
    split = arr.reshape(shape[:dim] + (shape[dim] // r, r) + shape[dim + 1 :])

    def at(s):
        return lax.dynamic_index_in_dim(split, jnp.bitwise_xor(digit, s), dim + 1, keepdims=False)

    return at


def send_to(axes, n, shift, pieces):
    dense = all(p.size % 128 == 0 for p in pieces)
    if dense:
        flat = jnp.concatenate([p.reshape(-1, 128) for p in pieces], axis=0)
    else:
        flat = jnp.concatenate([p.reshape(-1) for p in pieces])
    got = lax.ppermute(flat, axes, [(i, i ^ shift) for i in range(n)])
    out, at = [], 0
    for p in pieces:
        rows = p.size // 128 if dense else p.size
        out.append(got[at : at + rows].reshape(p.shape))
        at += rows
    return out


def linear_index(axes):
    idx = 0
    for a in axes:
        idx = idx * lax.axis_size(a) + lax.axis_index(a)
    return idx


def shards(flow_field, test_streams, snapshot_ids):
    highest = lax.Precision.HIGHEST
    f32 = jnp.float32
    bf16 = jnp.bfloat16
    batches, local_snaps, variables, cells_x, cells_y, cells_z = flow_field.shape
    n_gx = lax.axis_size("gx")
    n_gz = lax.axis_size("gz")
    n_vert = lax.axis_size("vert")
    total_x = cells_x * n_gx
    total_z = cells_z * n_gz
    total_q = variables * batches * local_snaps * n_vert
    factor_stream = test_streams[0]
    core_stream = test_streams[1]
    gx_me = lax.axis_index("gx")
    rank_ids = jnp.arange(K, dtype=jnp.int32)
    sketch_ids = jnp.arange(S, dtype=jnp.int32)
    x_ids = gx_me * cells_x + jnp.arange(cells_x, dtype=jnp.int32)
    y_ids = jnp.arange(cells_y, dtype=jnp.int32)
    z_ids = lax.axis_index("gz") * cells_z + jnp.arange(cells_z, dtype=jnp.int32)
    flat_q = jnp.arange(batches * local_snaps * variables, dtype=jnp.int32)
    slot = (
        jnp.arange(batches, dtype=jnp.int32)[:, None] * local_snaps
        + jnp.arange(local_snaps, dtype=jnp.int32)[None, :]
    )
    picks = jnp.where((flat_q // variables)[:, None, None] == slot[None], snapshot_ids[None], 0)
    q_ids = jnp.sum(picks, axis=(1, 2)) * variables + flat_q % variables
    ax = test_table(x_ids, rank_ids, K, factor_stream, 1).astype(f32)
    ay = test_table(y_ids, rank_ids, K, factor_stream, 2)
    az = test_table(z_ids, rank_ids, K, factor_stream, 3)
    aq = test_table(q_ids, rank_ids, K, factor_stream, 4).astype(f32)
    phy = test_table(sketch_ids, y_ids, cells_y, core_stream, 6).astype(f32)
    phz = test_table(sketch_ids, z_ids, total_z, core_stream, 7)
    phq = test_table(q_ids, jnp.arange(E, dtype=jnp.int32), E, core_stream, 8).astype(f32)

    n_q = batches * local_snaps * variables
    field = flow_field.reshape(n_q, cells_x, cells_y, cells_z)
    rows_z = field.reshape(-1, cells_z)

    qz = aq[:, None, :] * az.astype(f32)[None, :, :]
    qz_hi = qz.astype(bf16)
    qz_lo = (qz - qz_hi.astype(f32)).astype(bf16)
    both = jnp.einsum(
        "qxyz,qzk->xyk", field, jnp.concatenate([qz_hi, qz_lo], axis=-1), preferred_element_type=f32
    )
    by_q = both[..., :K] + both[..., K:]
    part_y = jnp.sum(by_q * ax[:, None, :], axis=0)
    part_x = jnp.sum(by_q * ay.astype(f32)[None, :, :], axis=1)
    along_y = jnp.einsum("qxyz,yk->qxzk", field, ay, preferred_element_type=f32)
    weights = aq[:, None, :] * ax[None, :, :]
    part_z = jnp.sum(along_y * weights[:, :, None, :], axis=(0, 1))
    first = jnp.dot(rows_z, phz.T, preferred_element_type=f32).reshape(n_q, cells_x, cells_y, S)
    high = lax.Precision.HIGH
    by_e = jnp.einsum("qxyn,qe->xeyn", first, phq, precision=high)
    part_core = jnp.einsum("my,xeyn->xemn", phy, by_e, precision=high)

    rows_each = cells_y // (n_gx * n_gz * n_vert)
    cols_each = K // (n_gx * n_vert)
    core_rows = S * S // n_gx
    n_gzv = n_gz * n_vert
    sy = part_y.reshape(n_gx, n_gzv, rows_each, K)
    sz = part_z.T.reshape(n_gx, n_vert, cols_each, cells_z)
    sx = part_x
    core = (
        part_core.reshape(cells_x, E, n_gx, core_rows)
        .transpose(2, 0, 1, 3)
        .reshape(1, n_gx, cells_x * E * core_rows)
    )

    v_me = lax.axis_index("vert")
    merge_sz = n_vert == 2
    for d, r in ([] if merge_sz else digit_steps(n_vert)):
        digit = (v_me // d) % r
        at = split_digit(sz, 1, r, digit)
        total = at(0)
        for s in range(1, r):
            (got,) = send_to("vert", n_vert, s * d, [at(s)])
            total = total + got
        sz = total
    gzv_me = linear_index(("gz", "vert"))
    for d, r in digit_steps(n_gzv):
        digit = (gzv_me // d) % r
        at = split_digit(sy, 1, r, digit)
        sy_total, sx_total, core_total = at(0), sx, core
        with_sz = merge_sz and d == 1
        if with_sz:
            at_z = split_digit(sz, 1, 2, v_me)
            sz_total = at_z(0)
        for s in range(r - 1, 0, -1):
            pieces = [at(s), sx, core] + ([at_z(1)] if with_sz and s == 1 else [])
            got = send_to(("gz", "vert"), n_gzv, s * d, pieces)
            sy_total, sx_total, core_total = sy_total + got[0], sx_total + got[1], core_total + got[2]
            if with_sz and s == 1:
                sz_total = sz_total + got[3]
        sy, sx, core = sy_total, sx_total, core_total
        if with_sz:
            sz = sz_total
    src = jnp.bitwise_xor(gx_me, jnp.arange(n_gx, dtype=jnp.int32))
    x_src = (src[:, None] * cells_x + jnp.arange(cells_x, dtype=jnp.int32)[None, :]).reshape(-1)
    phx = test_table(sketch_ids, x_src, total_x, core_stream, 5).astype(f32).reshape(S, n_gx, cells_x)
    core, phx = lax.optimization_barrier((core, phx))
    for d, r in digit_steps(n_gx):
        digit = (gx_me // d) % r
        at_y = split_digit(sy, 0, r, digit)
        at_z = split_digit(sz, 0, r, digit)
        at_c = split_digit(core, 1, r, digit)
        sy_total, sz_total, core_parts = at_y(0), at_z(0), [at_c(0)] + [None] * (r - 1)
        for s in range(r - 1, 0, -1):
            g_sy, g_sz, g_core = send_to("gx", n_gx, s * d, [at_y(s), at_z(s), at_c(s)])
            sy_total, sz_total = sy_total + g_sy, sz_total + g_sz
            core_parts[s] = g_core
        sy, sz = sy_total, sz_total
        core = jnp.concatenate(core_parts, axis=0)

    held = core.reshape(n_gx * cells_x, E, core_rows)
    weights_x = phx.reshape(S, n_gx * cells_x)
    core_out = jnp.sum(held[:, None, :, :] * weights_x.T[:, :, None, None], axis=0).transpose(2, 1, 0)

    scale_x = 3.0**1.5 / math.sqrt(cells_y * total_z * total_q)
    scale_y = 3.0**1.5 / math.sqrt(total_x * total_z * total_q)
    scale_z = 3.0**1.5 / math.sqrt(total_x * cells_y * total_q)
    scale_core = 9.0 / math.sqrt(total_x * cells_y * total_z * total_q)
    return (
        sx * scale_x,
        sy.reshape(rows_each, K) * scale_y,
        sz.reshape(cols_each, cells_z).T * scale_z,
        core_out * scale_core,
    )


def solution(mesh):
    in_specs = (P("groups", "vert", None, "gx", None, "gz"), P("groups"), P("groups", "vert"))
    out_specs = (
        P(("groups", "gx"), None),
        P(("groups", "gx", "gz", "vert"), None),
        P(("groups", "gz"), ("gx", "vert")),
        P(("groups", "gx"), None, None),
    )
    return jax.shard_map(shards, mesh=mesh, in_specs=in_specs, out_specs=out_specs, check_vma=False)
```

```python
import math

import jax
import jax.numpy as jnp
from jax import lax
from jax.sharding import PartitionSpec as P

K = 128
S = 48
E = 2


def mix_bits(mixed):
    mixed = jnp.bitwise_xor(mixed, lax.shift_right_logical(mixed, jnp.int32(16)))
    mixed = mixed * 739982445
    mixed = jnp.bitwise_xor(mixed, lax.shift_right_logical(mixed, jnp.int32(13)))
    mixed = mixed * 695872825
    return jnp.bitwise_xor(mixed, lax.shift_right_logical(mixed, jnp.int32(16)))


def test_table(row_ids, col_ids, stride, stream, salt):
    row_term = (row_ids * stride) * -1640531535
    col_term = col_ids * -1640531535
    mixed = row_term[:, None] + col_term[None, :] + (stream * -2048144777 + salt)
    upper = lax.shift_right_logical(mix_bits(mixed), jnp.int32(9))
    return ((2 * upper + 1).astype(jnp.float32) * 2.0 ** (-24) - 1.0).astype(jnp.bfloat16)


def digit_steps(n):
    d, out = 1, []
    while d < n:
        r = 4 if n // d >= 4 else 2
        out.append((d, r))
        d *= r
    return out


def split_digit(arr, dim, r, digit):
    shape = arr.shape
    split = arr.reshape(shape[:dim] + (shape[dim] // r, r) + shape[dim + 1 :])

    def at(s):
        return lax.dynamic_index_in_dim(split, jnp.bitwise_xor(digit, s), dim + 1, keepdims=False)

    return at


def send_to(axes, n, shift, pieces):
    dense = all(p.size % 128 == 0 for p in pieces)
    if dense:
        flat = jnp.concatenate([p.reshape(-1, 128) for p in pieces], axis=0)
    else:
        flat = jnp.concatenate([p.reshape(-1) for p in pieces])
    got = lax.ppermute(flat, axes, [(i, i ^ shift) for i in range(n)])
    out, at = [], 0
    for p in pieces:
        rows = p.size // 128 if dense else p.size
        out.append(got[at : at + rows].reshape(p.shape))
        at += rows
    return out


def linear_index(axes):
    idx = 0
    for a in axes:
        idx = idx * lax.axis_size(a) + lax.axis_index(a)
    return idx


def shards(flow_field, test_streams, snapshot_ids):
    highest = lax.Precision.HIGHEST
    f32 = jnp.float32
    bf16 = jnp.bfloat16
    batches, local_snaps, variables, cells_x, cells_y, cells_z = flow_field.shape
    n_gx = lax.axis_size("gx")
    n_gz = lax.axis_size("gz")
    n_vert = lax.axis_size("vert")
    total_x = cells_x * n_gx
    total_z = cells_z * n_gz
    total_q = variables * batches * local_snaps * n_vert
    factor_stream = test_streams[0]
    core_stream = test_streams[1]
    gx_me = lax.axis_index("gx")
    rank_ids = jnp.arange(K, dtype=jnp.int32)
    sketch_ids = jnp.arange(S, dtype=jnp.int32)
    x_ids = gx_me * cells_x + jnp.arange(cells_x, dtype=jnp.int32)
    y_ids = jnp.arange(cells_y, dtype=jnp.int32)
    z_ids = lax.axis_index("gz") * cells_z + jnp.arange(cells_z, dtype=jnp.int32)
    flat_q = jnp.arange(batches * local_snaps * variables, dtype=jnp.int32)
    slot = (
        jnp.arange(batches, dtype=jnp.int32)[:, None] * local_snaps
        + jnp.arange(local_snaps, dtype=jnp.int32)[None, :]
    )
    picks = jnp.where((flat_q // variables)[:, None, None] == slot[None], snapshot_ids[None], 0)
    q_ids = jnp.sum(picks, axis=(1, 2)) * variables + flat_q % variables
    ax = test_table(x_ids, rank_ids, K, factor_stream, 1).astype(f32)
    ay = test_table(y_ids, rank_ids, K, factor_stream, 2)
    az = test_table(z_ids, rank_ids, K, factor_stream, 3)
    aq = test_table(q_ids, rank_ids, K, factor_stream, 4).astype(f32)
    phy = test_table(sketch_ids, y_ids, cells_y, core_stream, 6).astype(f32)
    phz = test_table(sketch_ids, z_ids, total_z, core_stream, 7)
    phq = test_table(q_ids, jnp.arange(E, dtype=jnp.int32), E, core_stream, 8).astype(f32)

    n_q = batches * local_snaps * variables
    field = flow_field.reshape(n_q, cells_x, cells_y, cells_z)
    rows_z = field.reshape(-1, cells_z)

    qz = aq[:, None, :] * az.astype(f32)[None, :, :]
    qz_hi = qz.astype(bf16)
    qz_lo = (qz - qz_hi.astype(f32)).astype(bf16)
    both = jnp.einsum(
        "qxyz,qzk->xyk", field, jnp.concatenate([qz_hi, qz_lo], axis=-1), preferred_element_type=f32
    )
    by_q = both[..., :K] + both[..., K:]
    part_y = jnp.sum(by_q * ax[:, None, :], axis=0)
    part_x = jnp.sum(by_q * ay.astype(f32)[None, :, :], axis=1)
    along_y = jnp.einsum("qxyz,yk->qxzk", field, ay, preferred_element_type=f32)
    weights = aq[:, None, :] * ax[None, :, :]
    part_z = jnp.sum(along_y * weights[:, :, None, :], axis=(0, 1))
    first = jnp.dot(rows_z, phz.T, preferred_element_type=f32).reshape(n_q, cells_x, cells_y, S)
    high = lax.Precision.HIGH
    by_e = jnp.einsum("qxyn,qe->xeyn", first, phq, precision=high)
    part_core = jnp.einsum("my,xeyn->xemn", phy, by_e, precision=high)

    rows_each = cells_y // (n_gx * n_gz * n_vert)
    cols_each = K // (n_gx * n_vert)
    core_rows = S * S // n_gx
    n_gzv = n_gz * n_vert
    sy = part_y.reshape(n_gx, n_gzv, rows_each, K)
    sz = part_z.T.reshape(n_gx, n_vert, cols_each, cells_z)
    sx = part_x
    core = (
        part_core.reshape(cells_x, E, n_gx, core_rows)
        .transpose(2, 0, 1, 3)
        .reshape(1, n_gx, cells_x * E * core_rows)
    )

    v_me = lax.axis_index("vert")
    merge_sz = n_vert == 2
    for d, r in ([] if merge_sz else digit_steps(n_vert)):
        digit = (v_me // d) % r
        at = split_digit(sz, 1, r, digit)
        total = at(0)
        for s in range(1, r):
            (got,) = send_to("vert", n_vert, s * d, [at(s)])
            total = total + got
        sz = total
    gzv_me = linear_index(("gz", "vert"))
    for d, r in digit_steps(n_gzv):
        digit = (gzv_me // d) % r
        at = split_digit(sy, 1, r, digit)
        sy_total, sx_total, core_total = at(0), sx, core
        with_sz = merge_sz and d == 1
        if with_sz:
            at_z = split_digit(sz, 1, 2, v_me)
            sz_total = at_z(0)
        for s in range(1, r):
            pieces = [at(s), sx, core] + ([at_z(1)] if with_sz and s == 1 else [])
            got = send_to(("gz", "vert"), n_gzv, s * d, pieces)
            sy_total, sx_total, core_total = sy_total + got[0], sx_total + got[1], core_total + got[2]
            if with_sz and s == 1:
                sz_total = sz_total + got[3]
        sy, sx, core = sy_total, sx_total, core_total
        if with_sz:
            sz = sz_total
    src = jnp.bitwise_xor(gx_me, jnp.arange(n_gx, dtype=jnp.int32))
    x_src = (src[:, None] * cells_x + jnp.arange(cells_x, dtype=jnp.int32)[None, :]).reshape(-1)
    phx = test_table(sketch_ids, x_src, total_x, core_stream, 5).astype(f32).reshape(S, n_gx, cells_x)
    core, phx = lax.optimization_barrier((core, phx))
    for d, r in digit_steps(n_gx):
        digit = (gx_me // d) % r
        at_y = split_digit(sy, 0, r, digit)
        at_z = split_digit(sz, 0, r, digit)
        at_c = split_digit(core, 1, r, digit)
        sy_total, sz_total, core_parts = at_y(0), at_z(0), [at_c(0)] + [None] * (r - 1)
        for s in ([1, 3, 2] if r == 4 else list(range(1, r))):
            g_sy, g_sz, g_core = send_to("gx", n_gx, s * d, [at_y(s), at_z(s), at_c(s)])
            sy_total, sz_total = sy_total + g_sy, sz_total + g_sz
            core_parts[s] = g_core
        sy, sz = sy_total, sz_total
        core = jnp.concatenate(core_parts, axis=0)

    held = core.reshape(n_gx * cells_x, E, core_rows)
    weights_x = phx.reshape(S, n_gx * cells_x)
    core_out = jnp.sum(held[:, None, :, :] * weights_x.T[:, :, None, None], axis=0).transpose(2, 1, 0)

    scale_x = 3.0**1.5 / math.sqrt(cells_y * total_z * total_q)
    scale_y = 3.0**1.5 / math.sqrt(total_x * total_z * total_q)
    scale_z = 3.0**1.5 / math.sqrt(total_x * cells_y * total_q)
    scale_core = 9.0 / math.sqrt(total_x * cells_y * total_z * total_q)
    return (
        sx * scale_x,
        sy.reshape(rows_each, K) * scale_y,
        sz.reshape(cols_each, cells_z).T * scale_z,
        core_out * scale_core,
    )


def solution(mesh):
    in_specs = (P("groups", "vert", None, "gx", None, "gz"), P("groups"), P("groups", "vert"))
    out_specs = (
        P(("groups", "gx"), None),
        P(("groups", "gx", "gz", "vert"), None),
        P(("groups", "gz"), ("gx", "vert")),
        P(("groups", "gx"), None, None),
    )
    return jax.shard_map(shards, mesh=mesh, in_specs=in_specs, out_specs=out_specs, check_vma=False)
```

```python
import math

import jax
import jax.numpy as jnp
from jax import lax
from jax.sharding import PartitionSpec as P

K = 128
S = 48
E = 2


def mix_bits(mixed):
    mixed = jnp.bitwise_xor(mixed, lax.shift_right_logical(mixed, jnp.int32(16)))
    mixed = mixed * 739982445
    mixed = jnp.bitwise_xor(mixed, lax.shift_right_logical(mixed, jnp.int32(13)))
    mixed = mixed * 695872825
    return jnp.bitwise_xor(mixed, lax.shift_right_logical(mixed, jnp.int32(16)))


def test_table(row_ids, col_ids, stride, stream, salt):
    row_term = (row_ids * stride) * -1640531535
    col_term = col_ids * -1640531535
    mixed = row_term[:, None] + col_term[None, :] + (stream * -2048144777 + salt)
    upper = lax.shift_right_logical(mix_bits(mixed), jnp.int32(9))
    return ((2 * upper + 1).astype(jnp.float32) * 2.0 ** (-24) - 1.0).astype(jnp.bfloat16)


def digit_steps(n):
    d, out = 1, []
    while d < n:
        r = 4 if n // d >= 4 else 2
        out.append((d, r))
        d *= r
    return out


def split_digit(arr, dim, r, digit):
    shape = arr.shape
    split = arr.reshape(shape[:dim] + (shape[dim] // r, r) + shape[dim + 1 :])

    def at(s):
        return lax.dynamic_index_in_dim(split, jnp.bitwise_xor(digit, s), dim + 1, keepdims=False)

    return at


def send_to(axes, n, shift, pieces):
    dense = all(p.size % 128 == 0 for p in pieces)
    if dense:
        flat = jnp.concatenate([p.reshape(-1, 128) for p in pieces], axis=0)
    else:
        flat = jnp.concatenate([p.reshape(-1) for p in pieces])
    got = lax.ppermute(flat, axes, [(i, i ^ shift) for i in range(n)])
    out, at = [], 0
    for p in pieces:
        rows = p.size // 128 if dense else p.size
        out.append(got[at : at + rows].reshape(p.shape))
        at += rows
    return out


def linear_index(axes):
    idx = 0
    for a in axes:
        idx = idx * lax.axis_size(a) + lax.axis_index(a)
    return idx


def shards(flow_field, test_streams, snapshot_ids):
    highest = lax.Precision.HIGHEST
    f32 = jnp.float32
    bf16 = jnp.bfloat16
    batches, local_snaps, variables, cells_x, cells_y, cells_z = flow_field.shape
    n_gx = lax.axis_size("gx")
    n_gz = lax.axis_size("gz")
    n_vert = lax.axis_size("vert")
    total_x = cells_x * n_gx
    total_z = cells_z * n_gz
    total_q = variables * batches * local_snaps * n_vert
    factor_stream = test_streams[0]
    core_stream = test_streams[1]
    gx_me = lax.axis_index("gx")
    rank_ids = jnp.arange(K, dtype=jnp.int32)
    sketch_ids = jnp.arange(S, dtype=jnp.int32)
    x_ids = gx_me * cells_x + jnp.arange(cells_x, dtype=jnp.int32)
    y_ids = jnp.arange(cells_y, dtype=jnp.int32)
    z_ids = lax.axis_index("gz") * cells_z + jnp.arange(cells_z, dtype=jnp.int32)
    flat_q = jnp.arange(batches * local_snaps * variables, dtype=jnp.int32)
    slot = (
        jnp.arange(batches, dtype=jnp.int32)[:, None] * local_snaps
        + jnp.arange(local_snaps, dtype=jnp.int32)[None, :]
    )
    picks = jnp.where((flat_q // variables)[:, None, None] == slot[None], snapshot_ids[None], 0)
    q_ids = jnp.sum(picks, axis=(1, 2)) * variables + flat_q % variables
    ax = test_table(x_ids, rank_ids, K, factor_stream, 1).astype(f32)
    ay = test_table(y_ids, rank_ids, K, factor_stream, 2)
    az = test_table(z_ids, rank_ids, K, factor_stream, 3)
    aq = test_table(q_ids, rank_ids, K, factor_stream, 4).astype(f32)
    phy = test_table(sketch_ids, y_ids, cells_y, core_stream, 6).astype(f32)
    phz = test_table(sketch_ids, z_ids, total_z, core_stream, 7)
    phq = test_table(q_ids, jnp.arange(E, dtype=jnp.int32), E, core_stream, 8).astype(f32)

    n_q = batches * local_snaps * variables
    field = flow_field.reshape(n_q, cells_x, cells_y, cells_z)
    rows_z = field.reshape(-1, cells_z)

    qz = aq[:, None, :] * az.astype(f32)[None, :, :]
    qz_hi = qz.astype(bf16)
    qz_lo = (qz - qz_hi.astype(f32)).astype(bf16)
    both = jnp.einsum(
        "qxyz,qzk->xyk", field, jnp.concatenate([qz_hi, qz_lo], axis=-1), preferred_element_type=f32
    )
    by_q = both[..., :K] + both[..., K:]
    part_y = jnp.sum(by_q * ax[:, None, :], axis=0)
    part_x = jnp.sum(by_q * ay.astype(f32)[None, :, :], axis=1)
    along_y = jnp.einsum("qxyz,yk->qxzk", field, ay, preferred_element_type=f32)
    weights = aq[:, None, :] * ax[None, :, :]
    part_z = jnp.sum(along_y * weights[:, :, None, :], axis=(0, 1))
    first = jnp.dot(rows_z, phz.T, preferred_element_type=f32).reshape(n_q, cells_x, cells_y, S)
    high = lax.Precision.HIGH
    by_e = jnp.einsum("qxyn,qe->xeyn", first, phq, precision=high)
    part_core = jnp.einsum("my,xeyn->xemn", phy, by_e, precision=high)

    rows_each = cells_y // (n_gx * n_gz * n_vert)
    cols_each = K // (n_gx * n_vert)
    core_rows = S * S // n_gx
    n_gzv = n_gz * n_vert
    sy = part_y.reshape(n_gx, n_gzv, rows_each, K)
    sz = part_z.T.reshape(n_gx, n_vert, cols_each, cells_z)
    sx = part_x
    core = (
        part_core.reshape(cells_x, E, n_gx, core_rows)
        .transpose(2, 0, 1, 3)
        .reshape(1, n_gx, cells_x * E * core_rows)
    )

    v_me = lax.axis_index("vert")
    merge_sz = n_vert == 2
    for d, r in ([] if merge_sz else digit_steps(n_vert)):
        digit = (v_me // d) % r
        at = split_digit(sz, 1, r, digit)
        total = at(0)
        for s in range(1, r):
            (got,) = send_to("vert", n_vert, s * d, [at(s)])
            total = total + got
        sz = total
    gzv_me = linear_index(("gz", "vert"))
    for d, r in digit_steps(n_gzv):
        digit = (gzv_me // d) % r
        at = split_digit(sy, 1, r, digit)
        sy_total, sx_total, core_total = at(0), sx, core
        with_sz = merge_sz and d == 1
        if with_sz:
            at_z = split_digit(sz, 1, 2, v_me)
            sz_total = at_z(0)
        for s in ([1, 3, 2] if r == 4 else list(range(1, r))):
            pieces = [at(s), sx, core] + ([at_z(1)] if with_sz and s == 1 else [])
            got = send_to(("gz", "vert"), n_gzv, s * d, pieces)
            sy_total, sx_total, core_total = sy_total + got[0], sx_total + got[1], core_total + got[2]
            if with_sz and s == 1:
                sz_total = sz_total + got[3]
        sy, sx, core = sy_total, sx_total, core_total
        if with_sz:
            sz = sz_total
    src = jnp.bitwise_xor(gx_me, jnp.arange(n_gx, dtype=jnp.int32))
    x_src = (src[:, None] * cells_x + jnp.arange(cells_x, dtype=jnp.int32)[None, :]).reshape(-1)
    phx = test_table(sketch_ids, x_src, total_x, core_stream, 5).astype(f32).reshape(S, n_gx, cells_x)
    core, phx = lax.optimization_barrier((core, phx))
    for d, r in digit_steps(n_gx):
        digit = (gx_me // d) % r
        at_y = split_digit(sy, 0, r, digit)
        at_z = split_digit(sz, 0, r, digit)
        at_c = split_digit(core, 1, r, digit)
        sy_total, sz_total, core_parts = at_y(0), at_z(0), [at_c(0)]
        for s in range(1, r):
            g_sy, g_sz, g_core = send_to("gx", n_gx, s * d, [at_y(s), at_z(s), at_c(s)])
            sy_total, sz_total = sy_total + g_sy, sz_total + g_sz
            core_parts.append(g_core)
        sy, sz = sy_total, sz_total
        core = jnp.concatenate(core_parts, axis=0)

    held = core.reshape(n_gx * cells_x, E, core_rows)
    weights_x = phx.reshape(S, n_gx * cells_x)
    core_out = jnp.sum(held[:, None, :, :] * weights_x.T[:, :, None, None], axis=0).transpose(2, 1, 0)

    scale_x = 3.0**1.5 / math.sqrt(cells_y * total_z * total_q)
    scale_y = 3.0**1.5 / math.sqrt(total_x * total_z * total_q)
    scale_z = 3.0**1.5 / math.sqrt(total_x * cells_y * total_q)
    scale_core = 9.0 / math.sqrt(total_x * cells_y * total_z * total_q)
    return (
        sx * scale_x,
        sy.reshape(rows_each, K) * scale_y,
        sz.reshape(cols_each, cells_z).T * scale_z,
        core_out * scale_core,
    )


def solution(mesh):
    in_specs = (P("groups", "vert", None, "gx", None, "gz"), P("groups"), P("groups", "vert"))
    out_specs = (
        P(("groups", "gx"), None),
        P(("groups", "gx", "gz", "vert"), None),
        P(("groups", "gz"), ("gx", "vert")),
        P(("groups", "gx"), None, None),
    )
    return jax.shard_map(shards, mesh=mesh, in_specs=in_specs, out_specs=out_specs, check_vma=False)
```

```python
import math

import jax
import jax.numpy as jnp
from jax import lax
from jax.sharding import PartitionSpec as P

K = 128
S = 48
E = 2


def mix_bits(mixed):
    mixed = jnp.bitwise_xor(mixed, lax.shift_right_logical(mixed, jnp.int32(16)))
    mixed = mixed * 739982445
    mixed = jnp.bitwise_xor(mixed, lax.shift_right_logical(mixed, jnp.int32(13)))
    mixed = mixed * 695872825
    return jnp.bitwise_xor(mixed, lax.shift_right_logical(mixed, jnp.int32(16)))


def test_table(row_ids, col_ids, stride, stream, salt):
    row_term = (row_ids * stride) * -1640531535
    col_term = col_ids * -1640531535
    mixed = row_term[:, None] + col_term[None, :] + (stream * -2048144777 + salt)
    upper = lax.shift_right_logical(mix_bits(mixed), jnp.int32(9))
    return ((2 * upper + 1).astype(jnp.float32) * 2.0 ** (-24) - 1.0).astype(jnp.bfloat16)


def digit_steps(n):
    d, out = 1, []
    while d < n:
        r = 4 if n // d >= 4 else 2
        out.append((d, r))
        d *= r
    return out


def split_digit(arr, dim, r, digit):
    shape = arr.shape
    split = arr.reshape(shape[:dim] + (shape[dim] // r, r) + shape[dim + 1 :])

    def at(s):
        return lax.dynamic_index_in_dim(split, jnp.bitwise_xor(digit, s), dim + 1, keepdims=False)

    return at


def send_to(axes, n, shift, pieces):
    dense = all(p.size % 128 == 0 for p in pieces)
    if dense:
        flat = jnp.concatenate([p.reshape(-1, 128) for p in pieces], axis=0)
    else:
        flat = jnp.concatenate([p.reshape(-1) for p in pieces])
    got = lax.ppermute(flat, axes, [(i, i ^ shift) for i in range(n)])
    out, at = [], 0
    for p in pieces:
        rows = p.size // 128 if dense else p.size
        out.append(got[at : at + rows].reshape(p.shape))
        at += rows
    return out


def linear_index(axes):
    idx = 0
    for a in axes:
        idx = idx * lax.axis_size(a) + lax.axis_index(a)
    return idx


def shards(flow_field, test_streams, snapshot_ids):
    highest = lax.Precision.HIGHEST
    f32 = jnp.float32
    bf16 = jnp.bfloat16
    batches, local_snaps, variables, cells_x, cells_y, cells_z = flow_field.shape
    n_gx = lax.axis_size("gx")
    n_gz = lax.axis_size("gz")
    n_vert = lax.axis_size("vert")
    total_x = cells_x * n_gx
    total_z = cells_z * n_gz
    total_q = variables * batches * local_snaps * n_vert
    factor_stream = test_streams[0]
    core_stream = test_streams[1]
    gx_me = lax.axis_index("gx")
    rank_ids = jnp.arange(K, dtype=jnp.int32)
    sketch_ids = jnp.arange(S, dtype=jnp.int32)
    x_ids = gx_me * cells_x + jnp.arange(cells_x, dtype=jnp.int32)
    y_ids = jnp.arange(cells_y, dtype=jnp.int32)
    z_ids = lax.axis_index("gz") * cells_z + jnp.arange(cells_z, dtype=jnp.int32)
    flat_q = jnp.arange(batches * local_snaps * variables, dtype=jnp.int32)
    slot = (
        jnp.arange(batches, dtype=jnp.int32)[:, None] * local_snaps
        + jnp.arange(local_snaps, dtype=jnp.int32)[None, :]
    )
    picks = jnp.where((flat_q // variables)[:, None, None] == slot[None], snapshot_ids[None], 0)
    q_ids = jnp.sum(picks, axis=(1, 2)) * variables + flat_q % variables
    ax = test_table(x_ids, rank_ids, K, factor_stream, 1).astype(f32)
    ay = test_table(y_ids, rank_ids, K, factor_stream, 2)
    az = test_table(z_ids, rank_ids, K, factor_stream, 3)
    aq = test_table(q_ids, rank_ids, K, factor_stream, 4).astype(f32)
    phy = test_table(sketch_ids, y_ids, cells_y, core_stream, 6).astype(f32)
    phz = test_table(sketch_ids, z_ids, total_z, core_stream, 7)
    phq = test_table(q_ids, jnp.arange(E, dtype=jnp.int32), E, core_stream, 8).astype(f32)

    n_q = batches * local_snaps * variables
    field = flow_field.reshape(n_q, cells_x, cells_y, cells_z)
    rows_z = field.reshape(-1, cells_z)

    qz = aq[:, None, :] * az.astype(f32)[None, :, :]
    qz_hi = qz.astype(bf16)
    qz_lo = (qz - qz_hi.astype(f32)).astype(bf16)
    both = jnp.einsum(
        "qxyz,qzk->xyk", field, jnp.concatenate([qz_hi, qz_lo], axis=-1), preferred_element_type=f32
    )
    by_q = both[..., :K] + both[..., K:]
    part_y = jnp.sum(by_q * ax[:, None, :], axis=0)
    part_x = jnp.sum(by_q * ay.astype(f32)[None, :, :], axis=1)
    along_y = jnp.einsum("qxyz,yk->qxzk", field, ay, preferred_element_type=f32)
    weights = aq[:, None, :] * ax[None, :, :]
    part_z = jnp.sum(along_y * weights[:, :, None, :], axis=(0, 1))
    first = jnp.dot(rows_z, phz.T, preferred_element_type=f32).reshape(n_q, cells_x, cells_y, S)
    high = lax.Precision.HIGH
    by_e = jnp.einsum("qxyn,qe->xeyn", first, phq, precision=high)
    part_core = jnp.einsum("my,xeyn->xemn", phy, by_e, precision=high)

    rows_each = cells_y // (n_gx * n_gz * n_vert)
    cols_each = K // (n_gx * n_vert)
    core_rows = S * S // n_gx
    n_gzv = n_gz * n_vert
    sy = part_y.reshape(n_gx, n_gzv, rows_each, K)
    sz = part_z.T.reshape(n_gx, n_vert, cols_each, cells_z)
    sx = part_x
    core = (
        part_core.reshape(cells_x, E, n_gx, core_rows)
        .transpose(2, 0, 1, 3)
        .reshape(1, n_gx, cells_x * E * core_rows)
    )

    v_me = lax.axis_index("vert")
    merge_sz = n_vert == 2
    for d, r in ([] if merge_sz else digit_steps(n_vert)):
        digit = (v_me // d) % r
        at = split_digit(sz, 1, r, digit)
        total = at(0)
        for s in range(1, r):
            (got,) = send_to("vert", n_vert, s * d, [at(s)])
            total = total + got
        sz = total
    gzv_me = linear_index(("gz", "vert"))
    for d, r in digit_steps(n_gzv):
        digit = (gzv_me // d) % r
        at = split_digit(sy, 1, r, digit)
        sy_total, sx_total, core_total = at(0), sx, core
        with_sz = merge_sz and d == 1
        if with_sz:
            at_z = split_digit(sz, 1, 2, v_me)
            sz_total = at_z(0)
        for s in range(1, r):
            pieces = [at(s), sx, core] + ([at_z(1)] if with_sz and s == 1 else [])
            got = send_to(("gz", "vert"), n_gzv, s * d, pieces)
            sy_total, sx_total, core_total = sy_total + got[0], sx_total + got[1], core_total + got[2]
            if with_sz and s == 1:
                sz_total = sz_total + got[3]
        sy, sx, core = sy_total, sx_total, core_total
        if with_sz:
            sz = sz_total
    src = jnp.bitwise_xor(gx_me, jnp.arange(n_gx, dtype=jnp.int32))
    x_src = (src[:, None] * cells_x + jnp.arange(cells_x, dtype=jnp.int32)[None, :]).reshape(-1)
    phx = test_table(sketch_ids, x_src, total_x, core_stream, 5).astype(f32).reshape(S, n_gx, cells_x)
    scale_core = 9.0 / math.sqrt(total_x * cells_y * total_z * total_q)
    core, phx = lax.optimization_barrier((core, phx * scale_core))
    for d, r in digit_steps(n_gx):
        digit = (gx_me // d) % r
        at_y = split_digit(sy, 0, r, digit)
        at_z = split_digit(sz, 0, r, digit)
        at_c = split_digit(core, 1, r, digit)
        sy_total, sz_total, core_parts = at_y(0), at_z(0), [at_c(0)]
        for s in range(1, r):
            g_sy, g_sz, g_core = send_to("gx", n_gx, s * d, [at_y(s), at_z(s), at_c(s)])
            sy_total, sz_total = sy_total + g_sy, sz_total + g_sz
            core_parts.append(g_core)
        sy, sz = sy_total, sz_total
        core = jnp.concatenate(core_parts, axis=0)

    held = core.reshape(n_gx * cells_x, E, core_rows)
    weights_x = phx.reshape(S, n_gx * cells_x)
    core_out = jnp.sum(held[:, None, :, :] * weights_x.T[:, :, None, None], axis=0).transpose(2, 1, 0)

    scale_x = 3.0**1.5 / math.sqrt(cells_y * total_z * total_q)
    scale_y = 3.0**1.5 / math.sqrt(total_x * total_z * total_q)
    scale_z = 3.0**1.5 / math.sqrt(total_x * cells_y * total_q)
    return (
        sx * scale_x,
        sy.reshape(rows_each, K) * scale_y,
        sz.reshape(cols_each, cells_z).T * scale_z,
        core_out,
    )


def solution(mesh):
    in_specs = (P("groups", "vert", None, "gx", None, "gz"), P("groups"), P("groups", "vert"))
    out_specs = (
        P(("groups", "gx"), None),
        P(("groups", "gx", "gz", "vert"), None),
        P(("groups", "gz"), ("gx", "vert")),
        P(("groups", "gx"), None, None),
    )
    return jax.shard_map(shards, mesh=mesh, in_specs=in_specs, out_specs=out_specs, check_vma=False)
```

```python
import math

import jax
import jax.numpy as jnp
from jax import lax
from jax.sharding import PartitionSpec as P

K = 128
S = 48
E = 2


def mix_bits(mixed):
    mixed = jnp.bitwise_xor(mixed, lax.shift_right_logical(mixed, jnp.int32(16)))
    mixed = mixed * 739982445
    mixed = jnp.bitwise_xor(mixed, lax.shift_right_logical(mixed, jnp.int32(13)))
    mixed = mixed * 695872825
    return jnp.bitwise_xor(mixed, lax.shift_right_logical(mixed, jnp.int32(16)))


def test_table(row_ids, col_ids, stride, stream, salt):
    row_term = (row_ids * stride) * -1640531535
    col_term = col_ids * -1640531535
    mixed = row_term[:, None] + col_term[None, :] + (stream * -2048144777 + salt)
    upper = lax.shift_right_logical(mix_bits(mixed), jnp.int32(9))
    return ((2 * upper + 1).astype(jnp.float32) * 2.0 ** (-24) - 1.0).astype(jnp.bfloat16)


def digit_steps(n):
    d, out = 1, []
    while d < n:
        r = 4 if n // d >= 4 else 2
        out.append((d, r))
        d *= r
    return out


def split_digit(arr, dim, r, digit):
    shape = arr.shape
    split = arr.reshape(shape[:dim] + (shape[dim] // r, r) + shape[dim + 1 :])

    def at(s):
        return lax.dynamic_index_in_dim(split, jnp.bitwise_xor(digit, s), dim + 1, keepdims=False)

    return at


def send_to(axes, n, shift, pieces):
    dense = all(p.size % 128 == 0 for p in pieces)
    if dense:
        flat = jnp.concatenate([p.reshape(-1, 128) for p in pieces], axis=0)
    else:
        flat = jnp.concatenate([p.reshape(-1) for p in pieces])
    got = lax.ppermute(flat, axes, [(i, i ^ shift) for i in range(n)])
    out, at = [], 0
    for p in pieces:
        rows = p.size // 128 if dense else p.size
        out.append(got[at : at + rows].reshape(p.shape))
        at += rows
    return out


def linear_index(axes):
    idx = 0
    for a in axes:
        idx = idx * lax.axis_size(a) + lax.axis_index(a)
    return idx


def shards(flow_field, test_streams, snapshot_ids):
    highest = lax.Precision.HIGHEST
    f32 = jnp.float32
    bf16 = jnp.bfloat16
    batches, local_snaps, variables, cells_x, cells_y, cells_z = flow_field.shape
    n_gx = lax.axis_size("gx")
    n_gz = lax.axis_size("gz")
    n_vert = lax.axis_size("vert")
    total_x = cells_x * n_gx
    total_z = cells_z * n_gz
    total_q = variables * batches * local_snaps * n_vert
    factor_stream = test_streams[0]
    core_stream = test_streams[1]
    gx_me = lax.axis_index("gx")
    rank_ids = jnp.arange(K, dtype=jnp.int32)
    sketch_ids = jnp.arange(S, dtype=jnp.int32)
    x_ids = gx_me * cells_x + jnp.arange(cells_x, dtype=jnp.int32)
    y_ids = jnp.arange(cells_y, dtype=jnp.int32)
    z_ids = lax.axis_index("gz") * cells_z + jnp.arange(cells_z, dtype=jnp.int32)
    flat_q = jnp.arange(batches * local_snaps * variables, dtype=jnp.int32)
    slot = (
        jnp.arange(batches, dtype=jnp.int32)[:, None] * local_snaps
        + jnp.arange(local_snaps, dtype=jnp.int32)[None, :]
    )
    picks = jnp.where((flat_q // variables)[:, None, None] == slot[None], snapshot_ids[None], 0)
    q_ids = jnp.sum(picks, axis=(1, 2)) * variables + flat_q % variables
    ax = test_table(x_ids, rank_ids, K, factor_stream, 1).astype(f32)
    ay = test_table(y_ids, rank_ids, K, factor_stream, 2)
    az = test_table(z_ids, rank_ids, K, factor_stream, 3)
    aq = test_table(q_ids, rank_ids, K, factor_stream, 4).astype(f32)
    phy = test_table(sketch_ids, y_ids, cells_y, core_stream, 6).astype(f32)
    phz = test_table(sketch_ids, z_ids, total_z, core_stream, 7)
    phq = test_table(q_ids, jnp.arange(E, dtype=jnp.int32), E, core_stream, 8).astype(f32)

    n_q = batches * local_snaps * variables
    field = flow_field.reshape(n_q, cells_x, cells_y, cells_z)
    rows_z = field.reshape(-1, cells_z)

    qz = aq[:, None, :] * az.astype(f32)[None, :, :]
    by_q = jnp.einsum(
        "qxyz,qzk->xyk", field.astype(f32), qz, precision=lax.Precision.HIGH, preferred_element_type=f32
    )
    part_y = jnp.sum(by_q * ax[:, None, :], axis=0)
    part_x = jnp.sum(by_q * ay.astype(f32)[None, :, :], axis=1)
    along_y = jnp.einsum("qxyz,yk->qxzk", field, ay, preferred_element_type=f32)
    weights = aq[:, None, :] * ax[None, :, :]
    part_z = jnp.sum(along_y * weights[:, :, None, :], axis=(0, 1))
    first = jnp.dot(rows_z, phz.T, preferred_element_type=f32).reshape(n_q, cells_x, cells_y, S)
    high = lax.Precision.HIGH
    by_e = jnp.einsum("qxyn,qe->xeyn", first, phq, precision=high)
    part_core = jnp.einsum("my,xeyn->xemn", phy, by_e, precision=high)

    rows_each = cells_y // (n_gx * n_gz * n_vert)
    cols_each = K // (n_gx * n_vert)
    core_rows = S * S // n_gx
    n_gzv = n_gz * n_vert
    sy = part_y.reshape(n_gx, n_gzv, rows_each, K)
    sz = part_z.T.reshape(n_gx, n_vert, cols_each, cells_z)
    sx = part_x
    core = (
        part_core.reshape(cells_x, E, n_gx, core_rows)
        .transpose(2, 0, 1, 3)
        .reshape(1, n_gx, cells_x * E * core_rows)
    )

    v_me = lax.axis_index("vert")
    merge_sz = n_vert == 2
    for d, r in ([] if merge_sz else digit_steps(n_vert)):
        digit = (v_me // d) % r
        at = split_digit(sz, 1, r, digit)
        total = at(0)
        for s in range(1, r):
            (got,) = send_to("vert", n_vert, s * d, [at(s)])
            total = total + got
        sz = total
    gzv_me = linear_index(("gz", "vert"))
    for d, r in digit_steps(n_gzv):
        digit = (gzv_me // d) % r
        at = split_digit(sy, 1, r, digit)
        sy_total, sx_total, core_total = at(0), sx, core
        with_sz = merge_sz and d == 1
        if with_sz:
            at_z = split_digit(sz, 1, 2, v_me)
            sz_total = at_z(0)
        for s in range(1, r):
            pieces = [at(s), sx, core] + ([at_z(1)] if with_sz and s == 1 else [])
            got = send_to(("gz", "vert"), n_gzv, s * d, pieces)
            sy_total, sx_total, core_total = sy_total + got[0], sx_total + got[1], core_total + got[2]
            if with_sz and s == 1:
                sz_total = sz_total + got[3]
        sy, sx, core = sy_total, sx_total, core_total
        if with_sz:
            sz = sz_total
    src = jnp.bitwise_xor(gx_me, jnp.arange(n_gx, dtype=jnp.int32))
    x_src = (src[:, None] * cells_x + jnp.arange(cells_x, dtype=jnp.int32)[None, :]).reshape(-1)
    phx = test_table(sketch_ids, x_src, total_x, core_stream, 5).astype(f32).reshape(S, n_gx, cells_x)
    core, phx = lax.optimization_barrier((core, phx))
    for d, r in digit_steps(n_gx):
        digit = (gx_me // d) % r
        at_y = split_digit(sy, 0, r, digit)
        at_z = split_digit(sz, 0, r, digit)
        at_c = split_digit(core, 1, r, digit)
        sy_total, sz_total, core_parts = at_y(0), at_z(0), [at_c(0)]
        for s in range(1, r):
            g_sy, g_sz, g_core = send_to("gx", n_gx, s * d, [at_y(s), at_z(s), at_c(s)])
            sy_total, sz_total = sy_total + g_sy, sz_total + g_sz
            core_parts.append(g_core)
        sy, sz = sy_total, sz_total
        core = jnp.concatenate(core_parts, axis=0)

    held = core.reshape(n_gx * cells_x, E, core_rows)
    weights_x = phx.reshape(S, n_gx * cells_x)
    core_out = jnp.sum(held[:, None, :, :] * weights_x.T[:, :, None, None], axis=0).transpose(2, 1, 0)

    scale_x = 3.0**1.5 / math.sqrt(cells_y * total_z * total_q)
    scale_y = 3.0**1.5 / math.sqrt(total_x * total_z * total_q)
    scale_z = 3.0**1.5 / math.sqrt(total_x * cells_y * total_q)
    scale_core = 9.0 / math.sqrt(total_x * cells_y * total_z * total_q)
    return (
        sx * scale_x,
        sy.reshape(rows_each, K) * scale_y,
        sz.reshape(cols_each, cells_z).T * scale_z,
        core_out * scale_core,
    )


def solution(mesh):
    in_specs = (P("groups", "vert", None, "gx", None, "gz"), P("groups"), P("groups", "vert"))
    out_specs = (
        P(("groups", "gx"), None),
        P(("groups", "gx", "gz", "vert"), None),
        P(("groups", "gz"), ("gx", "vert")),
        P(("groups", "gx"), None, None),
    )
    return jax.shard_map(shards, mesh=mesh, in_specs=in_specs, out_specs=out_specs, check_vma=False)
```

```python
import math

import jax
import jax.numpy as jnp
from jax import lax
from jax.sharding import PartitionSpec as P

K = 128
S = 48
E = 2


def mix_bits(mixed):
    mixed = jnp.bitwise_xor(mixed, lax.shift_right_logical(mixed, jnp.int32(16)))
    mixed = mixed * 739982445
    mixed = jnp.bitwise_xor(mixed, lax.shift_right_logical(mixed, jnp.int32(13)))
    mixed = mixed * 695872825
    return jnp.bitwise_xor(mixed, lax.shift_right_logical(mixed, jnp.int32(16)))


def test_table(row_ids, col_ids, stride, stream, salt):
    row_term = (row_ids * stride) * -1640531535
    col_term = col_ids * -1640531535
    mixed = row_term[:, None] + col_term[None, :] + (stream * -2048144777 + salt)
    upper = lax.shift_right_logical(mix_bits(mixed), jnp.int32(9))
    return ((2 * upper + 1).astype(jnp.float32) * 2.0 ** (-24) - 1.0).astype(jnp.bfloat16)


def digit_steps(n):
    d, out = 1, []
    while d < n:
        r = 4 if n // d >= 4 else 2
        out.append((d, r))
        d *= r
    return out


def split_digit(arr, dim, r, digit):
    shape = arr.shape
    split = arr.reshape(shape[:dim] + (shape[dim] // r, r) + shape[dim + 1 :])

    def at(s):
        return lax.dynamic_index_in_dim(split, jnp.bitwise_xor(digit, s), dim + 1, keepdims=False)

    return at


def send_to(axes, n, shift, pieces):
    dense = all(p.size % 128 == 0 for p in pieces)
    if dense:
        flat = jnp.concatenate([p.reshape(-1, 128) for p in pieces], axis=0)
    else:
        flat = jnp.concatenate([p.reshape(-1) for p in pieces])
    got = lax.ppermute(flat, axes, [(i, i ^ shift) for i in range(n)])
    out, at = [], 0
    for p in pieces:
        rows = p.size // 128 if dense else p.size
        out.append(got[at : at + rows].reshape(p.shape))
        at += rows
    return out


def linear_index(axes):
    idx = 0
    for a in axes:
        idx = idx * lax.axis_size(a) + lax.axis_index(a)
    return idx


def shards(flow_field, test_streams, snapshot_ids):
    highest = lax.Precision.HIGHEST
    f32 = jnp.float32
    bf16 = jnp.bfloat16
    batches, local_snaps, variables, cells_x, cells_y, cells_z = flow_field.shape
    n_gx = lax.axis_size("gx")
    n_gz = lax.axis_size("gz")
    n_vert = lax.axis_size("vert")
    total_x = cells_x * n_gx
    total_z = cells_z * n_gz
    total_q = variables * batches * local_snaps * n_vert
    factor_stream = test_streams[0]
    core_stream = test_streams[1]
    gx_me = lax.axis_index("gx")
    rank_ids = jnp.arange(K, dtype=jnp.int32)
    sketch_ids = jnp.arange(S, dtype=jnp.int32)
    x_ids = gx_me * cells_x + jnp.arange(cells_x, dtype=jnp.int32)
    y_ids = jnp.arange(cells_y, dtype=jnp.int32)
    z_ids = lax.axis_index("gz") * cells_z + jnp.arange(cells_z, dtype=jnp.int32)
    flat_q = jnp.arange(batches * local_snaps * variables, dtype=jnp.int32)
    slot = (
        jnp.arange(batches, dtype=jnp.int32)[:, None] * local_snaps
        + jnp.arange(local_snaps, dtype=jnp.int32)[None, :]
    )
    picks = jnp.where((flat_q // variables)[:, None, None] == slot[None], snapshot_ids[None], 0)
    q_ids = jnp.sum(picks, axis=(1, 2)) * variables + flat_q % variables
    ax = test_table(x_ids, rank_ids, K, factor_stream, 1).astype(f32)
    ay = test_table(y_ids, rank_ids, K, factor_stream, 2)
    az = test_table(z_ids, rank_ids, K, factor_stream, 3)
    aq = test_table(q_ids, rank_ids, K, factor_stream, 4).astype(f32)
    phy = test_table(sketch_ids, y_ids, cells_y, core_stream, 6).astype(f32)
    phz = test_table(sketch_ids, z_ids, total_z, core_stream, 7)
    phq = test_table(q_ids, jnp.arange(E, dtype=jnp.int32), E, core_stream, 8).astype(f32)

    n_q = batches * local_snaps * variables
    field = flow_field.reshape(n_q, cells_x, cells_y, cells_z)
    rows_z = field.reshape(-1, cells_z)

    qz = aq[:, None, :] * az.astype(f32)[None, :, :]
    qz_hi = qz.astype(bf16)
    qz_lo = (qz - qz_hi.astype(f32)).astype(bf16)
    both = jnp.einsum(
        "qxyz,qzk->xyk", field, jnp.concatenate([qz_hi, qz_lo], axis=-1), preferred_element_type=f32
    )
    by_q = both[..., :K] + both[..., K:]
    part_y = jnp.sum(by_q * ax[:, None, :], axis=0)
    part_x = jnp.sum(by_q * ay.astype(f32)[None, :, :], axis=1)
    along_y = jnp.einsum("qxyz,yk->qxkz", field, ay, preferred_element_type=f32)
    weights = aq[:, None, :] * ax[None, :, :]
    part_z_t = jnp.sum(along_y * weights[:, :, :, None], axis=(0, 1))
    first = jnp.dot(rows_z, phz.T, preferred_element_type=f32).reshape(n_q, cells_x, cells_y, S)
    high = lax.Precision.HIGH
    by_e = jnp.einsum("qxyn,qe->xeyn", first, phq, precision=high)
    part_core = jnp.einsum("my,xeyn->xemn", phy, by_e, precision=high)

    rows_each = cells_y // (n_gx * n_gz * n_vert)
    cols_each = K // (n_gx * n_vert)
    core_rows = S * S // n_gx
    n_gzv = n_gz * n_vert
    sy = part_y.reshape(n_gx, n_gzv, rows_each, K)
    sz = part_z_t.reshape(n_gx, n_vert, cols_each, cells_z)
    sx = part_x
    core = (
        part_core.reshape(cells_x, E, n_gx, core_rows)
        .transpose(2, 0, 1, 3)
        .reshape(1, n_gx, cells_x * E * core_rows)
    )

    v_me = lax.axis_index("vert")
    merge_sz = n_vert == 2
    for d, r in ([] if merge_sz else digit_steps(n_vert)):
        digit = (v_me // d) % r
        at = split_digit(sz, 1, r, digit)
        total = at(0)
        for s in range(1, r):
            (got,) = send_to("vert", n_vert, s * d, [at(s)])
            total = total + got
        sz = total
    gzv_me = linear_index(("gz", "vert"))
    for d, r in digit_steps(n_gzv):
        digit = (gzv_me // d) % r
        at = split_digit(sy, 1, r, digit)
        sy_total, sx_total, core_total = at(0), sx, core
        with_sz = merge_sz and d == 1
        if with_sz:
            at_z = split_digit(sz, 1, 2, v_me)
            sz_total = at_z(0)
        for s in range(1, r):
            pieces = [at(s), sx, core] + ([at_z(1)] if with_sz and s == 1 else [])
            got = send_to(("gz", "vert"), n_gzv, s * d, pieces)
            sy_total, sx_total, core_total = sy_total + got[0], sx_total + got[1], core_total + got[2]
            if with_sz and s == 1:
                sz_total = sz_total + got[3]
        sy, sx, core = sy_total, sx_total, core_total
        if with_sz:
            sz = sz_total
    src = jnp.bitwise_xor(gx_me, jnp.arange(n_gx, dtype=jnp.int32))
    x_src = (src[:, None] * cells_x + jnp.arange(cells_x, dtype=jnp.int32)[None, :]).reshape(-1)
    phx = test_table(sketch_ids, x_src, total_x, core_stream, 5).astype(f32).reshape(S, n_gx, cells_x)
    core, phx = lax.optimization_barrier((core, phx))
    for d, r in digit_steps(n_gx):
        digit = (gx_me // d) % r
        at_y = split_digit(sy, 0, r, digit)
        at_z = split_digit(sz, 0, r, digit)
        at_c = split_digit(core, 1, r, digit)
        sy_total, sz_total, core_parts = at_y(0), at_z(0), [at_c(0)]
        for s in range(1, r):
            g_sy, g_sz, g_core = send_to("gx", n_gx, s * d, [at_y(s), at_z(s), at_c(s)])
            sy_total, sz_total = sy_total + g_sy, sz_total + g_sz
            core_parts.append(g_core)
        sy, sz = sy_total, sz_total
        core = jnp.concatenate(core_parts, axis=0)

    held = core.reshape(n_gx * cells_x, E, core_rows)
    weights_x = phx.reshape(S, n_gx * cells_x)
    core_out = jnp.sum(held[:, None, :, :] * weights_x.T[:, :, None, None], axis=0).transpose(2, 1, 0)

    scale_x = 3.0**1.5 / math.sqrt(cells_y * total_z * total_q)
    scale_y = 3.0**1.5 / math.sqrt(total_x * total_z * total_q)
    scale_z = 3.0**1.5 / math.sqrt(total_x * cells_y * total_q)
    scale_core = 9.0 / math.sqrt(total_x * cells_y * total_z * total_q)
    return (
        sx * scale_x,
        sy.reshape(rows_each, K) * scale_y,
        sz.reshape(cols_each, cells_z).T * scale_z,
        core_out * scale_core,
    )


def solution(mesh):
    in_specs = (P("groups", "vert", None, "gx", None, "gz"), P("groups"), P("groups", "vert"))
    out_specs = (
        P(("groups", "gx"), None),
        P(("groups", "gx", "gz", "vert"), None),
        P(("groups", "gz"), ("gx", "vert")),
        P(("groups", "gx"), None, None),
    )
    return jax.shard_map(shards, mesh=mesh, in_specs=in_specs, out_specs=out_specs, check_vma=False)
```
